32 devices in a mesh: dp: 16 (over z, y, core), head: 2 (over x).
Axes of the slice: x: 2, y: 2, z: 4, core: 2. Of those that a mesh axis runs over, the one named last changes fastest.
Arguments:
- layer_input: bfloat16 [16, 256, 768], P('dp', 'head'), may hold values from -6 to 6
- pair_input: bfloat16 [16, 256, 256, 256], P('dp', 'head'), may hold values from -6 to 6
- time_cond: float32 [16, 256], P('dp'), may hold values from -6 to 6
- chain_lengths: int32 [16], P('dp'), may hold values from 128 to 256, as said below
- residue_mask: int32 [16, 256], P('dp'), may hold values from 0 to 1, as said below
- mod_weight: bfloat16 [256, 4608], replicated, may hold values from -0.375 to 0.375
- mod_bias: float32 [4608], replicated, may hold values from -3 to 3
- qkv_weight: bfloat16 [768, 3, 768], P(None, None, 'head'), may hold values from -0.21875 to 0.21875
- pair_gain: float32 [256], replicated, may hold values from 0.25 to 1.75
- pair_weight: bfloat16 [256, 12], replicated, may hold values from -0.375 to 0.375
- out_weight: bfloat16 [768, 768], P('head'), may hold values from -0.625 to 0.625
- out_bias: float32 [768], replicated, may hold values from -3 to 3
- gate_up_weight: bfloat16 [768, 2, 3072], P(None, None, 'head'), may hold values from -0.21875 to 0.21875
- down_weight: bfloat16 [3072, 768], P('head'), may hold values from -0.21875 to 0.21875
- output_grad: bfloat16 [16, 256, 768], P('dp', 'head'), may hold values from -6 to 6
Outputs:
- layer_output: bfloat16 [16, 256, 768], P('dp', 'head')
- input_grad: float32 [16, 256, 768], P('dp', 'head')
- pair_grad: bfloat16 [16, 256, 256, 256], P('dp', 'head')
- cond_grad: float32 [16, 256], P('dp')
- mod_weight_grad: float32 [256, 4608], replicated
- mod_bias_grad: float32 [4608], replicated
- qkv_weight_grad: float32 [768, 3, 768], P('dp', None, 'head')
- pair_gain_grad: float32 [256], replicated
- pair_weight_grad: float32 [256, 12], replicated
- out_weight_grad: float32 [768, 768], P('head', 'dp')
- out_bias_grad: float32 [768], replicated
- gate_up_grad: float32 [768, 2, 3072], P('dp', None, 'head')
- down_grad: float32 [3072, 768], P('head', 'dp')
The draws below stay inside these ranges and needn't reach their ends.
Inputs may be any that keep to these rules, and one draw needn't show every extreme that they name: `chain_lengths`: each chain has 128 to 256 residues in use; the first chain has all 256. `residue_mask`: the first residue of every chain is resolved.
All inputs are finite; a program needn't handle non-finite values.
Results may differ from the reference program's by a relative error of at most 0.014.
The reference program's roundings to bfloat16 on the way count: a program that leaves them out, or rounds other values in their place, can miss the bound.
Values may be sent and summed in bfloat16 or wider, within the bound.
No kernel may reach another device: no remote copies, remote signals or barrier semaphores. Data moves between devices by JAX's collectives and lax.ppermute only.
A program may use at most 256 MiB of HBM per device.

```python
import jax
import jax.numpy as jnp
from jax import lax

D = 768
H = 12
DH = 64
PD = 256
FF = 3072
DC = 256
L = 256
CHAINS = 16


def draw_chain_lengths(key, part):
    counts = jax.random.randint(key, (CHAINS,), L // 2, L + 1).astype(jnp.int32)
    return counts.at[0].set(L)


def draw_residue_mask(key, part):
    levels = jax.random.randint(key, (CHAINS, L), 0, 8)
    resolved = jnp.where(levels > 0, 1, 0).astype(jnp.int32)
    return resolved.at[:, 0].set(1)


def level_of(rng, shape, cuts, low, top_value):
    gain = 1.0
    for axis_at, blocks in cuts:
        heights = jax.random.uniform(jax.random.fold_in(jax.random.fold_in(rng, 6), axis_at), (blocks,), jnp.float32, low / len(cuts), top_value / len(cuts))
        gain = gain * jnp.repeat(jnp.exp(heights), shape[axis_at] // blocks).reshape((-1,) + (1,) * (len(shape) - 1 - axis_at))
    return gain


def scatter_about(key, extent, width, reach, cuts=(), kind=jnp.bfloat16):
    values = jax.random.normal(key, extent, jnp.float32) * width
    if len(cuts) > 0:
        values = level_of(key, extent, cuts, -0.22, 0.18) * values
    return jnp.clip(values, min=-reach, max=reach).astype(kind)


def setup_inputs(seed: int = 0) -> dict:
    splits = jax.random.split(jax.random.key(seed), 16)
    return {
        "layer_input": scatter_about(splits[0], (CHAINS, L, D), 1.0, 6.0, ((0, 16), (1, 2))),
        "pair_input": scatter_about(splits[1], (CHAINS, L, L, PD), 1.0, 6.0, ((0, 16), (1, 2))),
        "time_cond": scatter_about(splits[2], (CHAINS, DC), 1.0, 6.0, ((0, 16),), jnp.float32),
        "chain_lengths": draw_chain_lengths(jax.random.fold_in(splits[15], 71), 0),
        "residue_mask": draw_residue_mask(jax.random.fold_in(splits[15], 71), 0),
        "mod_weight": scatter_about(splits[5], (DC, 6 * D), DC ** -0.5, 0.375),
        "mod_bias": scatter_about(splits[6], (6 * D,), 0.5, 3.0, (), jnp.float32),
        "qkv_weight": scatter_about(splits[7], (D, 3, H * DH), D ** -0.5, 0.21875, ((2, 2),)),
        "pair_gain": jnp.clip(1.0 + 0.15 * jax.random.normal(splits[8], (PD,), jnp.float32), 0.25, 1.75),
        "pair_weight": scatter_about(splits[9], (PD, H), PD ** -0.5, 0.375),
        "out_weight": scatter_about(splits[10], (H * DH, D), (H * DH // 8) ** -0.5, 0.625, ((0, 2),)),
        "out_bias": scatter_about(splits[11], (D,), 0.5, 3.0, (), jnp.float32),
        "gate_up_weight": scatter_about(splits[12], (D, 2, FF), D ** -0.5, 0.21875, ((2, 2),)),
        "down_weight": scatter_about(splits[13], (FF, D), (FF // 4) ** -0.5, 0.21875, ((0, 2),)),
        "output_grad": scatter_about(splits[14], (CHAINS, L, D), 1.0, 6.0, ((0, 16), (1, 2))),
    }


@jax.custom_vjp
def low(v):
    return lax.optimization_barrier(v.astype(jnp.bfloat16)).astype(jnp.float32)

@jax.custom_vjp
def low_back(v):
    return v

def low_keep(v):
    return (low(v), None)

def low_pass(kept, grad):
    return (grad,)

def back_keep(v):
    return (v, None)

def back_low(kept, grad):
    return (low(grad),)
low.defvjp(low_keep, low_pass)
low_back.defvjp(back_keep, back_low)
epsilon = 1e-05
precise = lax.Precision.HIGHEST

def layer_norm(values):
    centred = values - lax.optimization_barrier(jnp.mean(values, axis=-1, keepdims=True))
    return centred * lax.rsqrt(lax.optimization_barrier(jnp.mean(centred * centred, axis=-1, keepdims=True)) + epsilon)

def chain_layer(params, residues, pair_feats, cond_vec, valid):
    mod_weight, mod_bias, qkv_weight, pair_gain, pair_weight, out_weight, out_bias, gate_up_weight, down_weight = params
    cond_act = low(jax.nn.silu(cond_vec))
    modulation = jnp.dot(cond_act, mod_weight, precision=precise) + mod_bias
    scale_a, shift_a, gate_a, scale_t, shift_t, gate_t = jnp.split(modulation, 6)
    normed_a = low(layer_norm(residues) * (1.0 + scale_a) + shift_a)
    projected = low(low_back(jnp.einsum('ld,dtf->tlf', normed_a, qkv_weight, precision=precise)))
    queries = projected[0].reshape(L, H, DH)
    keys = projected[1].reshape(L, H, DH)
    values = projected[2].reshape(L, H, DH)
    pair_normed = low(layer_norm(pair_feats) * pair_gain)
    biases = low(jnp.einsum('qkp,ph->hqk', pair_normed, pair_weight, precision=precise))
    scores = jnp.einsum('qhe,khe->hqk', queries, keys, precision=precise) * DH ** (-0.5) + biases
    scores = jnp.where(valid[None, None, :], low_back(scores), -1000000000.0)
    row_max = lax.optimization_barrier(jnp.max(scores, axis=-1, keepdims=True))
    exp_scores = jnp.exp(scores - row_max)
    probs = low(exp_scores / lax.optimization_barrier(jnp.sum(exp_scores, axis=-1, keepdims=True)))
    mixed = jnp.einsum('hqk,khe->qhe', probs, values, precision=precise).reshape(L, H * DH)
    mixed = low(low_back(mixed))
    attn_branch = low_back(jnp.dot(mixed, out_weight, precision=precise)) + out_bias
    middle = residues + jax.nn.sigmoid(gate_a) * attn_branch
    normed_t = low(layer_norm(middle) * (1.0 + scale_t) + shift_t)
    gate_up = low_back(jnp.einsum('ld,dtf->tlf', normed_t, gate_up_weight, precision=precise))
    hidden = low(jax.nn.silu(gate_up[0]) * gate_up[1])
    ffn_branch = low_back(jnp.dot(hidden, down_weight, precision=precise))
    return middle + jax.nn.sigmoid(gate_t) * ffn_branch

def reference(layer_input, pair_input, time_cond, chain_lengths, residue_mask, mod_weight, mod_bias, qkv_weight, pair_gain, pair_weight, out_weight, out_bias, gate_up_weight, down_weight, output_grad):
    params = tuple((matrix.astype(jnp.float32) for matrix in (mod_weight, mod_bias, qkv_weight, pair_gain, pair_weight, out_weight, out_bias, gate_up_weight, down_weight)))
    positions = jnp.arange(L, dtype=jnp.int32)
    valid = (positions[None, :] < chain_lengths[:, None]) & ((residue_mask == 1) | (positions[None, :] == 0))

    def one_chain(totals, inputs):
        residues, pair_feats, cond_vec, chain_valid, grad_out = inputs

        def forward(params_in, res_in, pair_in, cond_in):
            return chain_layer(params_in, res_in, pair_in, cond_in, chain_valid)
        result, pullback = jax.vjp(forward, params, residues.astype(jnp.float32), pair_feats.astype(jnp.float32), cond_vec.astype(jnp.float32))
        param_grads, res_grad, pair_grad, cond_grad = pullback(grad_out.astype(jnp.float32))
        totals = jax.tree.map(lambda running, addend: running + addend, totals, param_grads)
        return (totals, (result.astype(jnp.bfloat16), res_grad, pair_grad.astype(jnp.bfloat16), cond_grad))
    zero_grads = jax.tree.map(jnp.zeros_like, params)
    totals, chain_outs = lax.scan(one_chain, zero_grads, (layer_input, pair_input, time_cond, valid, output_grad))
    layer_output, input_grad, pair_grad, cond_grad = chain_outs
    g_mod_w, g_mod_b, g_qkv, g_pair_gain, g_pair_w, g_out_w, g_out_b, g_gate_up, g_down = totals
    return (layer_output, input_grad, pair_grad, cond_grad, g_mod_w, g_mod_b, g_qkv, g_pair_gain, g_pair_w, g_out_w, g_out_b, g_gate_up, g_down)
```

```python
import jax
import jax.numpy as jnp
from jax import lax
from jax.sharding import PartitionSpec as P

DH = 64


epsilon = 1e-05
masked_score = -1000000000.0
precise = lax.Precision.HIGHEST
LANES = 128


def layer_norm(values):
    centred = values - jnp.mean(values, axis=-1, keepdims=True)
    inv_std = lax.rsqrt(jnp.mean(centred * centred, axis=-1, keepdims=True) + epsilon)
    return (centred * inv_std, inv_std)


def norm_back(normed, inv_std, grad):
    mean_grad = jnp.mean(grad, axis=-1, keepdims=True)
    mean_proj = jnp.mean(grad * normed, axis=-1, keepdims=True)
    return inv_std * (grad - mean_grad - normed * mean_proj)


def silu_slope(values):
    sigma = jax.nn.sigmoid(values)
    return sigma * (1.0 + values * (1.0 - sigma))


def head_split(values):
    return values.reshape(values.shape[:-1] + (values.shape[-1] // DH, DH))


def swap_heads(values):
    return lax.ppermute(values, "head", [(0, 1), (1, 0)])


def whole_rows(own, first):
    other = swap_heads(own)
    return jnp.where(
        first,
        jnp.concatenate([own, other], axis=1),
        jnp.concatenate([other, own], axis=1),
    )


def own_rows(values, head, rows):
    return lax.dynamic_slice_in_dim(values, head * rows, rows, 1)


def head_sum(part):
    return part + swap_heads(part)


def attn_scores(queries, keys, biases, valid):
    scores = jnp.einsum("cqhe,ckhe->chqk", queries, keys, preferred_element_type=jnp.float32)
    scores = scores * DH ** (-0.5) + biases.astype(jnp.float32)
    return jnp.where(valid[:, None, None, :], scores, masked_score)


def to_chunks(values, parts):
    return values.reshape(parts, -1, LANES)


def shards(
    layer_input,
    pair_input,
    time_cond,
    chain_lengths,
    residue_mask,
    mod_weight,
    mod_bias,
    qkv_weight,
    pair_gain,
    pair_weight,
    out_weight,
    out_bias,
    gate_up_weight,
    down_weight,
    output_grad,
):
    chains = layer_input.shape[0]
    rows = layer_input.shape[1]
    width = layer_input.shape[2]
    length = residue_mask.shape[1]
    head = lax.axis_index("head")
    first = head == 0
    data_count = lax.axis_size("dp")

    x_rows = whole_rows(layer_input, first)
    g_rows = whole_rows(output_grad, first)

    positions = jnp.arange(length, dtype=jnp.int32)
    valid = (positions[None, :] < chain_lengths[:, None]) & (
        (residue_mask == 1) | (positions[None, :] == 0)
    )
    silu_cond = jax.nn.silu(time_cond).astype(jnp.bfloat16)
    modulation = jnp.dot(silu_cond, mod_weight, preferred_element_type=jnp.float32) + mod_bias
    scale_a, shift_a, gate_a, scale_t, shift_t, gate_t = [
        modulation[:, None, section * width : (section + 1) * width] for section in range(6)
    ]

    pair_norm, pair_inv = layer_norm(pair_input.astype(jnp.float32))
    pair_normed = (pair_norm * pair_gain).astype(jnp.bfloat16)
    bias_rows = jnp.einsum(
        "cqkp,ph->chqk", pair_normed, pair_weight, preferred_element_type=jnp.float32
    ).astype(jnp.bfloat16)
    biases = lax.all_to_all(bias_rows, "head", split_axis=1, concat_axis=2, tiled=True)

    residues = x_rows.astype(jnp.float32)
    norm_in, inv_in = layer_norm(residues)
    normed_a = (norm_in * (1.0 + scale_a) + shift_a).astype(jnp.bfloat16)
    projected = jnp.einsum(
        "cld,dtf->tclf", normed_a, qkv_weight, preferred_element_type=jnp.float32
    ).astype(jnp.bfloat16)
    queries = head_split(projected[0])
    keys = head_split(projected[1])
    values = head_split(projected[2])
    scores = attn_scores(queries, keys, biases, valid)
    row_max = jnp.max(scores, axis=-1, keepdims=True)
    exp_scores = jnp.exp(scores - row_max)
    row_total = jnp.sum(exp_scores, axis=-1, keepdims=True)
    attn_probs = exp_scores / row_total
    probs_low = attn_probs.astype(jnp.bfloat16)
    mixed = jnp.einsum("chqk,ckhe->cqhe", probs_low, values, preferred_element_type=jnp.float32)
    mixed = mixed.reshape(mixed.shape[:2] + (-1,)).astype(jnp.bfloat16)
    attn_part = jnp.einsum("clf,fd->cld", mixed, out_weight, preferred_element_type=jnp.float32)
    attn_branch = head_sum(attn_part) + out_bias
    sig_a = jax.nn.sigmoid(gate_a)
    middle = residues + sig_a * attn_branch

    norm_mid, inv_mid = layer_norm(middle)
    normed_t = (norm_mid * (1.0 + scale_t) + shift_t).astype(jnp.bfloat16)
    gate_up = jnp.einsum(
        "cld,dtf->tclf", normed_t, gate_up_weight, preferred_element_type=jnp.float32
    )
    hidden = (jax.nn.silu(gate_up[0]) * gate_up[1]).astype(jnp.bfloat16)
    ffn_part = jnp.einsum(
        "clf,fd->cld", hidden, down_weight, preferred_element_type=jnp.float32
    ).astype(jnp.bfloat16)
    ffn_branch = ffn_part.astype(jnp.float32) + swap_heads(ffn_part).astype(jnp.float32)
    sig_t = jax.nn.sigmoid(gate_t)
    layer_output = own_rows((middle + sig_t * ffn_branch).astype(jnp.bfloat16), head, rows)

    grad_out = g_rows.astype(jnp.float32)
    d_ffn = (grad_out * sig_t).astype(jnp.bfloat16)
    d_gate_t = jnp.sum(grad_out * ffn_branch * sig_t * (1.0 - sig_t), axis=1)
    down_grad_t = jnp.einsum("cld,clf->df", d_ffn, hidden, preferred_element_type=jnp.float32)
    d_hidden = jnp.einsum("cld,fd->clf", d_ffn, down_weight, preferred_element_type=jnp.float32)
    d_gate = d_hidden * gate_up[1] * silu_slope(gate_up[0])
    d_up = d_hidden * jax.nn.silu(gate_up[0])
    d_gate_up = jnp.stack([d_gate, d_up]).astype(jnp.bfloat16)
    gate_up_grad = jnp.einsum(
        "cld,tclf->dtf", normed_t, d_gate_up, preferred_element_type=jnp.float32
    )
    ffn_in_part = jnp.einsum(
        "tclf,dtf->cld", d_gate_up, gate_up_weight, preferred_element_type=jnp.float32
    )
    d_normed_t = head_sum(ffn_in_part)
    d_middle = grad_out + norm_back(norm_mid, inv_mid, d_normed_t * (1.0 + scale_t))
    d_scale_t = jnp.sum(d_normed_t * norm_mid, axis=1)
    d_shift_t = jnp.sum(d_normed_t, axis=1)
    d_attn = d_middle * sig_a
    d_gate_a = jnp.sum(d_middle * attn_branch * sig_a * (1.0 - sig_a), axis=1)
    d_out_bias = jnp.sum(d_attn, axis=(0, 1))
    d_attn_low = d_attn.astype(jnp.bfloat16)

    out_weight_grad_t = jnp.einsum(
        "cld,clf->df", d_attn_low, mixed, preferred_element_type=jnp.float32
    )
    d_mixed = head_split(
        jnp.einsum(
            "cld,fd->clf", d_attn_low, out_weight, preferred_element_type=jnp.float32
        ).astype(jnp.bfloat16)
    )
    d_values = jnp.einsum("chqk,cqhe->ckhe", probs_low, d_mixed, preferred_element_type=jnp.float32)
    d_probs = jnp.einsum("cqhe,ckhe->chqk", d_mixed, values, preferred_element_type=jnp.float32)
    d_scores = (
        attn_probs * (d_probs - jnp.sum(d_probs * attn_probs, axis=-1, keepdims=True))
    ).astype(jnp.bfloat16)
    d_queries = jnp.einsum(
        "chqk,ckhe->cqhe", d_scores, keys, preferred_element_type=jnp.float32
    ) * DH ** (-0.5)
    d_keys = jnp.einsum(
        "chqk,cqhe->ckhe", d_scores, queries, preferred_element_type=jnp.float32
    ) * DH ** (-0.5)
    d_qkv = (
        jnp.stack([d_queries, d_keys, d_values]).reshape(3, chains, length, -1).astype(jnp.bfloat16)
    )
    qkv_grad = jnp.einsum("cld,tclf->dtf", normed_a, d_qkv, preferred_element_type=jnp.float32)

    packed = jnp.concatenate(
        [
            to_chunks(qkv_grad, data_count),
            to_chunks(out_weight_grad_t, data_count),
            to_chunks(gate_up_grad, data_count),
            to_chunks(down_grad_t, data_count),
        ],
        axis=1,
    ).astype(jnp.bfloat16)
    reduced = lax.psum_scatter(packed, "dp", scatter_dimension=0, tiled=True)[0].astype(
        jnp.float32
    )

    attn_in_part = jnp.einsum(
        "tclf,dtf->cld", d_qkv, qkv_weight, preferred_element_type=jnp.float32
    ).astype(jnp.bfloat16)
    d_normed_a = attn_in_part.astype(jnp.float32) + swap_heads(attn_in_part).astype(jnp.float32)
    input_grad = own_rows(
        d_middle + norm_back(norm_in, inv_in, d_normed_a * (1.0 + scale_a)), head, rows
    )
    d_scale_a = jnp.sum(d_normed_a * norm_in, axis=1)
    d_shift_a = jnp.sum(d_normed_a, axis=1)
    d_modulation = jnp.concatenate(
        [d_scale_a, d_shift_a, d_gate_a, d_scale_t, d_shift_t, d_gate_t], axis=-1
    )

    d_bias_rows = lax.all_to_all(d_scores, "head", split_axis=2, concat_axis=1, tiled=True)
    pair_weight_grad = jnp.einsum(
        "cqkp,chqk->ph", pair_normed, d_bias_rows, preferred_element_type=jnp.float32
    )
    d_pair_normed = jnp.einsum(
        "chqk,ph->cqkp", d_bias_rows, pair_weight, preferred_element_type=jnp.float32
    )
    pair_gain_grad = jnp.sum(d_pair_normed * pair_norm, axis=(0, 1, 2))
    pair_grad = norm_back(pair_norm, pair_inv, d_pair_normed * pair_gain).astype(jnp.bfloat16)

    pair_small = head_sum(
        jnp.concatenate([pair_weight_grad.reshape(-1), pair_gain_grad])[None]
    )
    small = jnp.concatenate(
        [d_modulation, time_cond, pair_small, d_out_bias[None]],
        axis=-1,
    )
    small_rows = lax.all_gather(small, "dp", axis=0, tiled=True)
    mod_size = d_modulation.shape[-1]
    cond_size = time_cond.shape[-1]
    pw_size = pair_weight.size
    pg_size = pair_gain.size
    mod_chain = small_rows[:, :mod_size]
    cond_chain = small_rows[:, mod_size : mod_size + cond_size]
    rest = jnp.sum(small_rows[:, mod_size + cond_size :], axis=0)
    pair_weight_grad = rest[:pw_size].reshape(pair_weight.shape)
    pair_gain_grad = rest[pw_size : pw_size + pg_size]
    out_bias_grad = rest[pw_size + pg_size :]
    cond_act = lax.optimization_barrier(jax.nn.silu(cond_chain).astype(jnp.bfloat16)).astype(
        jnp.float32
    )
    mod_weight_grad = jnp.dot(cond_act.T, mod_chain, precision=precise)
    mod_bias_grad = jnp.sum(mod_chain, axis=0)
    cond_grad = jnp.dot(
        d_modulation, mod_weight.astype(jnp.float32).T, precision=precise
    ) * silu_slope(time_cond)

    sizes = [
        qkv_grad.size // data_count,
        out_weight_grad_t.size // data_count,
        gate_up_grad.size // data_count,
        down_grad_t.size // data_count,
    ]
    flat = reduced.reshape(-1)
    offsets = [0]
    for size in sizes:
        offsets.append(offsets[-1] + size)
    pieces = [flat[offsets[i] : offsets[i + 1]] for i in range(4)]
    qkv_grad = pieces[0].reshape((-1,) + qkv_grad.shape[1:])
    out_weight_grad = pieces[1].reshape(-1, out_weight_grad_t.shape[1]).T
    gate_up_grad = pieces[2].reshape((-1,) + gate_up_grad.shape[1:])
    down_grad = pieces[3].reshape(-1, down_grad_t.shape[1]).T
    return (
        layer_output,
        input_grad,
        pair_grad,
        cond_grad,
        mod_weight_grad,
        mod_bias_grad,
        qkv_grad,
        pair_gain_grad,
        pair_weight_grad,
        out_weight_grad,
        out_bias_grad,
        gate_up_grad,
        down_grad,
    )


def solution(mesh):
    placed = (
        P("dp", "head", None),
        P("dp", "head", None, None),
        P("dp", None),
        P("dp"),
        P("dp", None),
        P(),
        P(),
        P(None, None, "head"),
        P(),
        P(),
        P("head", None),
        P(),
        P(None, None, "head"),
        P("head", None),
        P("dp", "head", None),
    )
    return jax.shard_map(
        shards,
        mesh=mesh,
        in_specs=placed,
        out_specs=(
            P("dp", "head", None),
            P("dp", "head", None),
            P("dp", "head", None, None),
            P("dp", None),
            P(),
            P(),
            P("dp", None, "head"),
            P(),
            P(),
            P("head", "dp"),
            P(),
            P("dp", None, "head"),
            P("head", "dp"),
        ),
        check_vma=False,
    )
```

```python
import jax
import jax.numpy as jnp
from jax import lax
from jax.experimental import pallas as pl
from jax.experimental.pallas import tpu as pltpu
from jax.sharding import PartitionSpec as P

DH = 64


epsilon = 1e-05
masked_score = -1000000000.0
precise = lax.Precision.HIGHEST
LANES = 128
PAIR_TILE = 2048
HEAD_PAD = 16


def pair_stats(x):
    centred = x - jnp.mean(x, axis=-1, keepdims=True)
    inv_std = lax.rsqrt(jnp.mean(centred * centred, axis=-1, keepdims=True) + epsilon)
    return centred * inv_std, inv_std


def pair_forward_kernel(x_ref, gain_ref, wt_ref, bias_ref):
    normed, _ = pair_stats(x_ref[...].astype(jnp.float32))
    scaled = (normed * gain_ref[...]).astype(jnp.bfloat16)
    bias = lax.dot_general(
        wt_ref[...], scaled, (((1,), (1,)), ((), ())), preferred_element_type=jnp.float32
    )
    bias_ref[...] = bias[: bias_ref.shape[0]].astype(bias_ref.dtype)


def pair_forward(flat, gain, wt, heads):
    m, width = flat.shape
    tile = min(PAIR_TILE, m)
    return pl.pallas_call(
        pair_forward_kernel,
        grid=(m // tile,),
        in_specs=[
            pl.BlockSpec((tile, width), lambda i: (i, 0)),
            pl.BlockSpec((1, width), lambda i: (0, 0)),
            pl.BlockSpec(wt.shape, lambda i: (0, 0)),
        ],
        out_specs=pl.BlockSpec((heads, tile), lambda i: (0, i)),
        out_shape=jax.ShapeDtypeStruct((heads, m), jnp.bfloat16),
        cost_estimate=pl.CostEstimate(
            flops=m * width * (2 * HEAD_PAD + 10),
            transcendentals=m,
            bytes_accessed=m * width * 2 + heads * m * 2,
        ),
    )(flat, gain, wt)


def pair_backward_kernel(x_ref, ds_ref, gain_ref, wt_ref, grad_ref, wg_ref, gg_ref):
    step = pl.program_id(0)
    normed, inv_std = pair_stats(x_ref[...].astype(jnp.float32))
    gain = gain_ref[...]
    scaled = (normed * gain).astype(jnp.bfloat16)
    ds = ds_ref[...]
    d_scaled = lax.dot_general(
        ds, wt_ref[...], (((0,), (0,)), ((), ())), preferred_element_type=jnp.float32
    )
    wg = lax.dot_general(ds, scaled, (((1,), (0,)), ((), ())), preferred_element_type=jnp.float32)
    gg = jnp.sum(d_scaled * normed, axis=0, keepdims=True)
    d_normed = d_scaled * gain
    mean_grad = jnp.mean(d_normed, axis=-1, keepdims=True)
    mean_proj = jnp.mean(d_normed * normed, axis=-1, keepdims=True)
    grad_ref[...] = (inv_std * (d_normed - mean_grad - normed * mean_proj)).astype(grad_ref.dtype)

    @pl.when(step == 0)
    def _():
        wg_ref[...] = jnp.zeros_like(wg_ref)
        gg_ref[...] = jnp.zeros_like(gg_ref)

    wg_ref[...] += wg
    gg_ref[...] += gg


def pair_backward(flat, ds, gain, wt):
    m, width = flat.shape
    tile = min(PAIR_TILE, m)
    pad = ds.shape[0]
    return pl.pallas_call(
        pair_backward_kernel,
        grid=(m // tile,),
        in_specs=[
            pl.BlockSpec((tile, width), lambda i: (i, 0)),
            pl.BlockSpec((pad, tile), lambda i: (0, i)),
            pl.BlockSpec((1, width), lambda i: (0, 0)),
            pl.BlockSpec(wt.shape, lambda i: (0, 0)),
        ],
        out_specs=[
            pl.BlockSpec((tile, width), lambda i: (i, 0)),
            pl.BlockSpec((pad, width), lambda i: (0, 0)),
            pl.BlockSpec((1, width), lambda i: (0, 0)),
        ],
        out_shape=[
            jax.ShapeDtypeStruct((m, width), jnp.bfloat16),
            jax.ShapeDtypeStruct((pad, width), jnp.float32),
            jax.ShapeDtypeStruct((1, width), jnp.float32),
        ],
        compiler_params=pltpu.CompilerParams(dimension_semantics=("arbitrary",)),
        cost_estimate=pl.CostEstimate(
            flops=m * width * (4 * HEAD_PAD + 20),
            transcendentals=m,
            bytes_accessed=2 * m * width * 2 + pad * m * 2,
        ),
    )(flat, ds, gain, wt)


def layer_norm(values):
    centred = values - jnp.mean(values, axis=-1, keepdims=True)
    inv_std = lax.rsqrt(jnp.mean(centred * centred, axis=-1, keepdims=True) + epsilon)
    return (centred * inv_std, inv_std)


def norm_back(normed, inv_std, grad):
    mean_grad = jnp.mean(grad, axis=-1, keepdims=True)
    mean_proj = jnp.mean(grad * normed, axis=-1, keepdims=True)
    return inv_std * (grad - mean_grad - normed * mean_proj)


def silu_slope(values):
    sigma = jax.nn.sigmoid(values)
    return sigma * (1.0 + values * (1.0 - sigma))


def head_split(values):
    return values.reshape(values.shape[:-1] + (values.shape[-1] // DH, DH))


def swap_heads(values):
    return lax.ppermute(values, "head", [(0, 1), (1, 0)])


def whole_rows(own, first):
    other = swap_heads(own)
    return jnp.where(
        first,
        jnp.concatenate([own, other], axis=1),
        jnp.concatenate([other, own], axis=1),
    )


def own_rows(values, head, rows):
    return lax.dynamic_slice_in_dim(values, head * rows, rows, 1)


def head_sum(part):
    return part + swap_heads(part)


def attn_scores(queries, keys, biases, valid):
    scores = jnp.einsum("cqhe,ckhe->chqk", queries, keys, preferred_element_type=jnp.float32)
    scores = scores * DH ** (-0.5) + biases.astype(jnp.float32)
    return jnp.where(valid[:, None, None, :], scores, masked_score)


def to_chunks(values, parts):
    return values.reshape(parts, -1, LANES)


def shards(
    layer_input,
    pair_input,
    time_cond,
    chain_lengths,
    residue_mask,
    mod_weight,
    mod_bias,
    qkv_weight,
    pair_gain,
    pair_weight,
    out_weight,
    out_bias,
    gate_up_weight,
    down_weight,
    output_grad,
):
    chains = layer_input.shape[0]
    rows = layer_input.shape[1]
    width = layer_input.shape[2]
    length = residue_mask.shape[1]
    head = lax.axis_index("head")
    first = head == 0
    data_count = lax.axis_size("dp")

    x_rows = whole_rows(layer_input, first)
    g_rows = whole_rows(output_grad, first)

    positions = jnp.arange(length, dtype=jnp.int32)
    valid = (positions[None, :] < chain_lengths[:, None]) & (
        (residue_mask == 1) | (positions[None, :] == 0)
    )
    silu_cond = jax.nn.silu(time_cond).astype(jnp.bfloat16)
    modulation = jnp.dot(silu_cond, mod_weight, preferred_element_type=jnp.float32) + mod_bias
    scale_a, shift_a, gate_a, scale_t, shift_t, gate_t = [
        modulation[:, None, section * width : (section + 1) * width] for section in range(6)
    ]

    heads_all = pair_weight.shape[1]
    pair_width = pair_input.shape[-1]
    pair_flat = pair_input.reshape(-1, pair_width)
    pair_wt = jnp.zeros((HEAD_PAD, pair_width), jnp.bfloat16).at[:heads_all].set(pair_weight.T)
    pair_gain_row = pair_gain.reshape(1, pair_width)
    bias_flat = pair_forward(pair_flat, pair_gain_row, pair_wt, heads_all)
    bias_rows = jnp.moveaxis(
        bias_flat.reshape((heads_all,) + pair_input.shape[:3]), 0, 1
    )
    biases = lax.all_to_all(bias_rows, "head", split_axis=1, concat_axis=2, tiled=True)

    residues = x_rows.astype(jnp.float32)
    norm_in, inv_in = layer_norm(residues)
    normed_a = (norm_in * (1.0 + scale_a) + shift_a).astype(jnp.bfloat16)
    projected = jnp.einsum(
        "cld,dtf->tclf", normed_a, qkv_weight, preferred_element_type=jnp.float32
    ).astype(jnp.bfloat16)
    queries = head_split(projected[0])
    keys = head_split(projected[1])
    values = head_split(projected[2])
    scores = attn_scores(queries, keys, biases, valid)
    row_max = jnp.max(scores, axis=-1, keepdims=True)
    exp_scores = jnp.exp(scores - row_max)
    row_total = jnp.sum(exp_scores, axis=-1, keepdims=True)
    attn_probs = exp_scores / row_total
    probs_low = attn_probs.astype(jnp.bfloat16)
    mixed = jnp.einsum("chqk,ckhe->cqhe", probs_low, values, preferred_element_type=jnp.float32)
    mixed = mixed.reshape(mixed.shape[:2] + (-1,)).astype(jnp.bfloat16)
    attn_part = jnp.einsum("clf,fd->cld", mixed, out_weight, preferred_element_type=jnp.float32)
    attn_branch = head_sum(attn_part) + out_bias
    sig_a = jax.nn.sigmoid(gate_a)
    middle = residues + sig_a * attn_branch

    norm_mid, inv_mid = layer_norm(middle)
    normed_t = (norm_mid * (1.0 + scale_t) + shift_t).astype(jnp.bfloat16)
    gate_up = jnp.einsum(
        "cld,dtf->tclf", normed_t, gate_up_weight, preferred_element_type=jnp.float32
    )
    hidden = (jax.nn.silu(gate_up[0]) * gate_up[1]).astype(jnp.bfloat16)
    ffn_part = jnp.einsum(
        "clf,fd->cld", hidden, down_weight, preferred_element_type=jnp.float32
    ).astype(jnp.bfloat16)
    ffn_branch = ffn_part.astype(jnp.float32) + swap_heads(ffn_part).astype(jnp.float32)
    sig_t = jax.nn.sigmoid(gate_t)
    layer_output = own_rows((middle + sig_t * ffn_branch).astype(jnp.bfloat16), head, rows)

    grad_out = g_rows.astype(jnp.float32)
    d_ffn = (grad_out * sig_t).astype(jnp.bfloat16)
    d_gate_t = jnp.sum(grad_out * ffn_branch * sig_t * (1.0 - sig_t), axis=1)
    down_grad_t = jnp.einsum("cld,clf->df", d_ffn, hidden, preferred_element_type=jnp.float32)
    d_hidden = jnp.einsum("cld,fd->clf", d_ffn, down_weight, preferred_element_type=jnp.float32)
    d_gate = d_hidden * gate_up[1] * silu_slope(gate_up[0])
    d_up = d_hidden * jax.nn.silu(gate_up[0])
    d_gate_up = jnp.stack([d_gate, d_up]).astype(jnp.bfloat16)
    gate_up_grad = jnp.einsum(
        "cld,tclf->dtf", normed_t, d_gate_up, preferred_element_type=jnp.float32
    )
    ffn_in_part = jnp.einsum(
        "tclf,dtf->cld", d_gate_up, gate_up_weight, preferred_element_type=jnp.float32
    )
    d_normed_t = head_sum(ffn_in_part)
    d_middle = grad_out + norm_back(norm_mid, inv_mid, d_normed_t * (1.0 + scale_t))
    d_scale_t = jnp.sum(d_normed_t * norm_mid, axis=1)
    d_shift_t = jnp.sum(d_normed_t, axis=1)
    d_attn = d_middle * sig_a
    d_gate_a = jnp.sum(d_middle * attn_branch * sig_a * (1.0 - sig_a), axis=1)
    d_out_bias = jnp.sum(d_attn, axis=(0, 1))
    d_attn_low = d_attn.astype(jnp.bfloat16)

    out_weight_grad_t = jnp.einsum(
        "cld,clf->df", d_attn_low, mixed, preferred_element_type=jnp.float32
    )
    d_mixed = head_split(
        jnp.einsum(
            "cld,fd->clf", d_attn_low, out_weight, preferred_element_type=jnp.float32
        ).astype(jnp.bfloat16)
    )
    d_values = jnp.einsum("chqk,cqhe->ckhe", probs_low, d_mixed, preferred_element_type=jnp.float32)
    d_probs = jnp.einsum("cqhe,ckhe->chqk", d_mixed, values, preferred_element_type=jnp.float32)
    d_scores = (
        attn_probs * (d_probs - jnp.sum(d_probs * attn_probs, axis=-1, keepdims=True))
    ).astype(jnp.bfloat16)
    d_queries = jnp.einsum(
        "chqk,ckhe->cqhe", d_scores, keys, preferred_element_type=jnp.float32
    ) * DH ** (-0.5)
    d_keys = jnp.einsum(
        "chqk,cqhe->ckhe", d_scores, queries, preferred_element_type=jnp.float32
    ) * DH ** (-0.5)
    d_qkv = (
        jnp.stack([d_queries, d_keys, d_values]).reshape(3, chains, length, -1).astype(jnp.bfloat16)
    )
    qkv_grad = jnp.einsum("cld,tclf->dtf", normed_a, d_qkv, preferred_element_type=jnp.float32)

    packed = jnp.concatenate(
        [
            to_chunks(qkv_grad, data_count),
            to_chunks(out_weight_grad_t, data_count),
            to_chunks(gate_up_grad, data_count),
            to_chunks(down_grad_t, data_count),
        ],
        axis=1,
    ).astype(jnp.bfloat16)
    reduced = lax.psum_scatter(packed, "dp", scatter_dimension=0, tiled=True)[0].astype(
        jnp.float32
    )

    attn_in_part = jnp.einsum(
        "tclf,dtf->cld", d_qkv, qkv_weight, preferred_element_type=jnp.float32
    ).astype(jnp.bfloat16)
    d_normed_a = attn_in_part.astype(jnp.float32) + swap_heads(attn_in_part).astype(jnp.float32)
    input_grad = own_rows(
        d_middle + norm_back(norm_in, inv_in, d_normed_a * (1.0 + scale_a)), head, rows
    )
    d_scale_a = jnp.sum(d_normed_a * norm_in, axis=1)
    d_shift_a = jnp.sum(d_normed_a, axis=1)
    d_modulation = jnp.concatenate(
        [d_scale_a, d_shift_a, d_gate_a, d_scale_t, d_shift_t, d_gate_t], axis=-1
    )

    d_bias_rows = lax.all_to_all(d_scores, "head", split_axis=2, concat_axis=1, tiled=True)
    d_bias_flat = jnp.moveaxis(d_bias_rows, 1, 0).reshape(heads_all, -1)
    d_bias_flat = jnp.pad(d_bias_flat, ((0, HEAD_PAD - heads_all), (0, 0)))
    pair_grad, pair_wg, pair_gg = pair_backward(pair_flat, d_bias_flat, pair_gain_row, pair_wt)
    pair_grad = pair_grad.reshape(pair_input.shape)
    pair_weight_grad = pair_wg[:heads_all].T
    pair_gain_grad = pair_gg[0]

    pair_small = head_sum(
        jnp.concatenate([pair_weight_grad.reshape(-1), pair_gain_grad])[None]
    )
    small = jnp.concatenate(
        [d_modulation, time_cond, pair_small, d_out_bias[None]],
        axis=-1,
    )
    small_rows = lax.all_gather(small, "dp", axis=0, tiled=True)
    mod_size = d_modulation.shape[-1]
    cond_size = time_cond.shape[-1]
    pw_size = pair_weight.size
    pg_size = pair_gain.size
    mod_chain = small_rows[:, :mod_size]
    cond_chain = small_rows[:, mod_size : mod_size + cond_size]
    rest = jnp.sum(small_rows[:, mod_size + cond_size :], axis=0)
    pair_weight_grad = rest[:pw_size].reshape(pair_weight.shape)
    pair_gain_grad = rest[pw_size : pw_size + pg_size]
    out_bias_grad = rest[pw_size + pg_size :]
    cond_act = lax.optimization_barrier(jax.nn.silu(cond_chain).astype(jnp.bfloat16)).astype(
        jnp.float32
    )
    mod_weight_grad = jnp.dot(cond_act.T, mod_chain, precision=precise)
    mod_bias_grad = jnp.sum(mod_chain, axis=0)
    cond_grad = jnp.dot(
        d_modulation, mod_weight.astype(jnp.float32).T, precision=precise
    ) * silu_slope(time_cond)

    sizes = [
        qkv_grad.size // data_count,
        out_weight_grad_t.size // data_count,
        gate_up_grad.size // data_count,
        down_grad_t.size // data_count,
    ]
    flat = reduced.reshape(-1)
    offsets = [0]
    for size in sizes:
        offsets.append(offsets[-1] + size)
    pieces = [flat[offsets[i] : offsets[i + 1]] for i in range(4)]
    qkv_grad = pieces[0].reshape((-1,) + qkv_grad.shape[1:])
    out_weight_grad = pieces[1].reshape(-1, out_weight_grad_t.shape[1]).T
    gate_up_grad = pieces[2].reshape((-1,) + gate_up_grad.shape[1:])
    down_grad = pieces[3].reshape(-1, down_grad_t.shape[1]).T
    return (
        layer_output,
        input_grad,
        pair_grad,
        cond_grad,
        mod_weight_grad,
        mod_bias_grad,
        qkv_grad,
        pair_gain_grad,
        pair_weight_grad,
        out_weight_grad,
        out_bias_grad,
        gate_up_grad,
        down_grad,
    )


def solution(mesh):
    placed = (
        P("dp", "head", None),
        P("dp", "head", None, None),
        P("dp", None),
        P("dp"),
        P("dp", None),
        P(),
        P(),
        P(None, None, "head"),
        P(),
        P(),
        P("head", None),
        P(),
        P(None, None, "head"),
        P("head", None),
        P("dp", "head", None),
    )
    return jax.shard_map(
        shards,
        mesh=mesh,
        in_specs=placed,
        out_specs=(
            P("dp", "head", None),
            P("dp", "head", None),
            P("dp", "head", None, None),
            P("dp", None),
            P(),
            P(),
            P("dp", None, "head"),
            P(),
            P(),
            P("head", "dp"),
            P(),
            P("dp", None, "head"),
            P("head", "dp"),
        ),
        check_vma=False,
    )
```

```python
import jax
import jax.numpy as jnp
from jax import lax
from jax.experimental import pallas as pl
from jax.experimental.pallas import tpu as pltpu
from jax.sharding import PartitionSpec as P

DH = 64


epsilon = 1e-05
masked_score = -1000000000.0
precise = lax.Precision.HIGHEST
LANES = 128
PAIR_TILE = 2048
HEAD_PAD = 16


def pair_stats(x):
    centred = x - jnp.mean(x, axis=-1, keepdims=True)
    inv_std = lax.rsqrt(jnp.mean(centred * centred, axis=-1, keepdims=True) + epsilon)
    return centred * inv_std, inv_std


def pair_forward_kernel(x_ref, gain_ref, wt_ref, bias_ref):
    normed, _ = pair_stats(x_ref[...].astype(jnp.float32))
    scaled = (normed * gain_ref[...]).astype(jnp.bfloat16)
    bias = lax.dot_general(
        wt_ref[...], scaled, (((1,), (1,)), ((), ())), preferred_element_type=jnp.float32
    )
    bias_ref[...] = bias[: bias_ref.shape[0]].astype(bias_ref.dtype)


def pair_forward(flat, gain, wt, heads):
    m, width = flat.shape
    tile = min(PAIR_TILE, m)
    return pl.pallas_call(
        pair_forward_kernel,
        grid=(m // tile,),
        in_specs=[
            pl.BlockSpec((tile, width), lambda i: (i, 0)),
            pl.BlockSpec((1, width), lambda i: (0, 0)),
            pl.BlockSpec(wt.shape, lambda i: (0, 0)),
        ],
        out_specs=pl.BlockSpec((heads, tile), lambda i: (0, i)),
        out_shape=jax.ShapeDtypeStruct((heads, m), jnp.bfloat16),
        cost_estimate=pl.CostEstimate(
            flops=m * width * (2 * HEAD_PAD + 10),
            transcendentals=m,
            bytes_accessed=m * width * 2 + heads * m * 2,
        ),
    )(flat, gain, wt)


def pair_backward_kernel(x_ref, ds_ref, gain_ref, wt_ref, grad_ref, wg_ref, gg_ref):
    step = pl.program_id(0)
    normed, inv_std = pair_stats(x_ref[...].astype(jnp.float32))
    gain = gain_ref[...]
    scaled = (normed * gain).astype(jnp.bfloat16)
    ds = ds_ref[...]
    d_scaled = lax.dot_general(
        ds, wt_ref[...], (((0,), (0,)), ((), ())), preferred_element_type=jnp.float32
    )
    wg = lax.dot_general(ds, scaled, (((1,), (0,)), ((), ())), preferred_element_type=jnp.float32)
    gg = jnp.sum(d_scaled * normed, axis=0, keepdims=True)
    d_normed = d_scaled * gain
    mean_grad = jnp.mean(d_normed, axis=-1, keepdims=True)
    mean_proj = jnp.mean(d_normed * normed, axis=-1, keepdims=True)
    grad_ref[...] = (inv_std * (d_normed - mean_grad - normed * mean_proj)).astype(grad_ref.dtype)

    @pl.when(step == 0)
    def _():
        wg_ref[...] = jnp.zeros_like(wg_ref)
        gg_ref[...] = jnp.zeros_like(gg_ref)

    wg_ref[...] += wg
    gg_ref[...] += gg


def pair_backward(flat, ds, gain, wt):
    m, width = flat.shape
    tile = min(PAIR_TILE, m)
    pad = ds.shape[0]
    return pl.pallas_call(
        pair_backward_kernel,
        grid=(m // tile,),
        in_specs=[
            pl.BlockSpec((tile, width), lambda i: (i, 0)),
            pl.BlockSpec((pad, tile), lambda i: (0, i)),
            pl.BlockSpec((1, width), lambda i: (0, 0)),
            pl.BlockSpec(wt.shape, lambda i: (0, 0)),
        ],
        out_specs=[
            pl.BlockSpec((tile, width), lambda i: (i, 0)),
            pl.BlockSpec((pad, width), lambda i: (0, 0)),
            pl.BlockSpec((1, width), lambda i: (0, 0)),
        ],
        out_shape=[
            jax.ShapeDtypeStruct((m, width), jnp.bfloat16),
            jax.ShapeDtypeStruct((pad, width), jnp.float32),
            jax.ShapeDtypeStruct((1, width), jnp.float32),
        ],
        compiler_params=pltpu.CompilerParams(dimension_semantics=("arbitrary",)),
        cost_estimate=pl.CostEstimate(
            flops=m * width * (4 * HEAD_PAD + 20),
            transcendentals=m,
            bytes_accessed=2 * m * width * 2 + pad * m * 2,
        ),
    )(flat, ds, gain, wt)


def layer_norm(values):
    centred = values - jnp.mean(values, axis=-1, keepdims=True)
    inv_std = lax.rsqrt(jnp.mean(centred * centred, axis=-1, keepdims=True) + epsilon)
    return (centred * inv_std, inv_std)


def norm_back(normed, inv_std, grad):
    mean_grad = jnp.mean(grad, axis=-1, keepdims=True)
    mean_proj = jnp.mean(grad * normed, axis=-1, keepdims=True)
    return inv_std * (grad - mean_grad - normed * mean_proj)


def silu_slope(values):
    sigma = jax.nn.sigmoid(values)
    return sigma * (1.0 + values * (1.0 - sigma))


def head_split(values):
    return values.reshape(values.shape[:-1] + (values.shape[-1] // DH, DH))


def swap_heads(values):
    return lax.ppermute(values, "head", [(0, 1), (1, 0)])


def whole_rows(own, first):
    other = swap_heads(own)
    return jnp.where(
        first,
        jnp.concatenate([own, other], axis=0),
        jnp.concatenate([other, own], axis=0),
    )


def own_rows(values, head, rows):
    return lax.dynamic_slice_in_dim(values, head * rows, rows, 1)


def head_sum(part):
    return part + swap_heads(part)


def attn_scores(queries, keys, biases, valid):
    scores = jnp.einsum("cqhe,ckhe->chqk", queries, keys, preferred_element_type=jnp.float32)
    scores = scores * DH ** (-0.5) + biases.astype(jnp.float32)
    return jnp.where(valid[:, None, None, :], scores, masked_score)


def to_chunks(values, parts):
    return values.reshape(parts, -1, LANES)


def shards(
    layer_input,
    pair_input,
    time_cond,
    chain_lengths,
    residue_mask,
    mod_weight,
    mod_bias,
    qkv_weight,
    pair_gain,
    pair_weight,
    out_weight,
    out_bias,
    gate_up_weight,
    down_weight,
    output_grad,
):
    assert layer_input.shape[0] == 1
    rows = layer_input.shape[1]
    width = layer_input.shape[2]
    length = residue_mask.shape[1]
    head = lax.axis_index("head")
    first = head == 0
    data_count = lax.axis_size("dp")
    proj = qkv_weight.shape[2]
    ffn = gate_up_weight.shape[2]
    qkv_w = qkv_weight.reshape(width, 3 * proj)
    gate_up_w = gate_up_weight.reshape(width, 2 * ffn)

    x_rows = whole_rows(layer_input[0], first)
    g_rows = whole_rows(output_grad[0], first)

    positions = jnp.arange(length, dtype=jnp.int32)
    valid = (positions < chain_lengths[0]) & ((residue_mask[0] == 1) | (positions == 0))
    silu_cond = jax.nn.silu(time_cond).astype(jnp.bfloat16)
    modulation = jnp.dot(silu_cond, mod_weight, preferred_element_type=jnp.float32) + mod_bias
    scale_a, shift_a, gate_a, scale_t, shift_t, gate_t = [
        modulation[:, section * width : (section + 1) * width] for section in range(6)
    ]

    heads_all = pair_weight.shape[1]
    pair_width = pair_input.shape[-1]
    pair_flat = pair_input.reshape(-1, pair_width)
    pair_wt = jnp.zeros((HEAD_PAD, pair_width), jnp.bfloat16).at[:heads_all].set(pair_weight.T)
    pair_gain_row = pair_gain.reshape(1, pair_width)
    bias_flat = pair_forward(pair_flat, pair_gain_row, pair_wt, heads_all)
    bias_rows = bias_flat.reshape(heads_all, rows, length)
    biases = lax.all_to_all(bias_rows, "head", split_axis=0, concat_axis=1, tiled=True)

    residues = x_rows.astype(jnp.float32)
    norm_in, inv_in = layer_norm(residues)
    normed_a = (norm_in * (1.0 + scale_a) + shift_a).astype(jnp.bfloat16)
    projected = jnp.dot(normed_a, qkv_w, preferred_element_type=jnp.float32).astype(jnp.bfloat16)
    queries = head_split(projected[:, :proj])
    keys = head_split(projected[:, proj : 2 * proj])
    values = head_split(projected[:, 2 * proj :])
    scores = jnp.einsum("qhe,khe->hqk", queries, keys, preferred_element_type=jnp.float32)
    scores = scores * DH ** (-0.5) + biases.astype(jnp.float32)
    scores = jnp.where(valid[None, None, :], scores, masked_score)
    row_max = jnp.max(scores, axis=-1, keepdims=True)
    exp_scores = jnp.exp(scores - row_max)
    row_total = jnp.sum(exp_scores, axis=-1, keepdims=True)
    attn_probs = exp_scores / row_total
    probs_low = attn_probs.astype(jnp.bfloat16)
    mixed = jnp.einsum("hqk,khe->qhe", probs_low, values, preferred_element_type=jnp.float32)
    mixed = mixed.reshape(length, proj).astype(jnp.bfloat16)
    attn_part = jnp.dot(mixed, out_weight, preferred_element_type=jnp.float32)
    attn_branch = head_sum(attn_part) + out_bias
    sig_a = jax.nn.sigmoid(gate_a)
    middle = residues + sig_a * attn_branch

    norm_mid, inv_mid = layer_norm(middle)
    normed_t = (norm_mid * (1.0 + scale_t) + shift_t).astype(jnp.bfloat16)
    gate_up = jnp.dot(normed_t, gate_up_w, preferred_element_type=jnp.float32)
    gate_pre = gate_up[:, :ffn]
    up_pre = gate_up[:, ffn:]
    hidden = (jax.nn.silu(gate_pre) * up_pre).astype(jnp.bfloat16)
    ffn_part = jnp.dot(hidden, down_weight, preferred_element_type=jnp.float32).astype(jnp.bfloat16)
    ffn_branch = ffn_part.astype(jnp.float32) + swap_heads(ffn_part).astype(jnp.float32)
    sig_t = jax.nn.sigmoid(gate_t)
    layer_output = own_rows((middle + sig_t * ffn_branch).astype(jnp.bfloat16)[None], head, rows)

    grad_out = g_rows.astype(jnp.float32)
    d_ffn = (grad_out * sig_t).astype(jnp.bfloat16)
    d_gate_t = jnp.sum(grad_out * ffn_branch * sig_t * (1.0 - sig_t), axis=0, keepdims=True)
    down_grad_t = lax.dot_general(
        d_ffn, hidden, (((0,), (0,)), ((), ())), preferred_element_type=jnp.float32
    )
    d_hidden = lax.dot_general(
        d_ffn, down_weight, (((1,), (1,)), ((), ())), preferred_element_type=jnp.float32
    )
    d_gate = d_hidden * up_pre * silu_slope(gate_pre)
    d_up = d_hidden * jax.nn.silu(gate_pre)
    d_gate_up = jnp.concatenate([d_gate, d_up], axis=1).astype(jnp.bfloat16)
    gate_up_grad = lax.dot_general(
        normed_t, d_gate_up, (((0,), (0,)), ((), ())), preferred_element_type=jnp.float32
    )
    ffn_in_part = lax.dot_general(
        d_gate_up, gate_up_w, (((1,), (1,)), ((), ())), preferred_element_type=jnp.float32
    )
    d_normed_t = head_sum(ffn_in_part)
    d_middle = grad_out + norm_back(norm_mid, inv_mid, d_normed_t * (1.0 + scale_t))
    d_scale_t = jnp.sum(d_normed_t * norm_mid, axis=0, keepdims=True)
    d_shift_t = jnp.sum(d_normed_t, axis=0, keepdims=True)
    d_attn = d_middle * sig_a
    d_gate_a = jnp.sum(d_middle * attn_branch * sig_a * (1.0 - sig_a), axis=0, keepdims=True)
    d_out_bias = jnp.sum(d_attn, axis=0, keepdims=True)
    d_attn_low = d_attn.astype(jnp.bfloat16)

    out_weight_grad_t = lax.dot_general(
        d_attn_low, mixed, (((0,), (0,)), ((), ())), preferred_element_type=jnp.float32
    )
    d_mixed = head_split(
        lax.dot_general(
            d_attn_low, out_weight, (((1,), (1,)), ((), ())), preferred_element_type=jnp.float32
        ).astype(jnp.bfloat16)
    )
    d_values = jnp.einsum("hqk,qhe->khe", probs_low, d_mixed, preferred_element_type=jnp.float32)
    d_probs = jnp.einsum("qhe,khe->hqk", d_mixed, values, preferred_element_type=jnp.float32)
    d_scores = (
        attn_probs * (d_probs - jnp.sum(d_probs * attn_probs, axis=-1, keepdims=True))
    ).astype(jnp.bfloat16)
    d_queries = jnp.einsum(
        "hqk,khe->qhe", d_scores, keys, preferred_element_type=jnp.float32
    ) * DH ** (-0.5)
    d_keys = jnp.einsum(
        "hqk,qhe->khe", d_scores, queries, preferred_element_type=jnp.float32
    ) * DH ** (-0.5)
    d_qkv = jnp.concatenate(
        [d_queries.reshape(length, proj), d_keys.reshape(length, proj), d_values.reshape(length, proj)],
        axis=1,
    ).astype(jnp.bfloat16)
    qkv_grad = lax.dot_general(
        normed_a, d_qkv, (((0,), (0,)), ((), ())), preferred_element_type=jnp.float32
    )

    packed = jnp.concatenate(
        [
            qkv_grad.astype(jnp.bfloat16),
            out_weight_grad_t.astype(jnp.bfloat16),
            gate_up_grad.astype(jnp.bfloat16),
            down_grad_t.astype(jnp.bfloat16),
        ],
        axis=1,
    )
    reduced = lax.psum_scatter(packed, "dp", scatter_dimension=0, tiled=True).astype(jnp.float32)

    attn_in_part = lax.dot_general(
        d_qkv, qkv_w, (((1,), (1,)), ((), ())), preferred_element_type=jnp.float32
    ).astype(jnp.bfloat16)
    d_normed_a = attn_in_part.astype(jnp.float32) + swap_heads(attn_in_part).astype(jnp.float32)
    input_grad = own_rows(
        (d_middle + norm_back(norm_in, inv_in, d_normed_a * (1.0 + scale_a)))[None], head, rows
    )
    d_scale_a = jnp.sum(d_normed_a * norm_in, axis=0, keepdims=True)
    d_shift_a = jnp.sum(d_normed_a, axis=0, keepdims=True)
    d_modulation = jnp.concatenate(
        [d_scale_a, d_shift_a, d_gate_a, d_scale_t, d_shift_t, d_gate_t], axis=-1
    )

    d_bias_rows = lax.all_to_all(d_scores, "head", split_axis=1, concat_axis=0, tiled=True)
    d_bias_flat = jnp.pad(d_bias_rows.reshape(heads_all, -1), ((0, HEAD_PAD - heads_all), (0, 0)))
    pair_grad, pair_wg, pair_gg = pair_backward(pair_flat, d_bias_flat, pair_gain_row, pair_wt)
    pair_grad = pair_grad.reshape(pair_input.shape)
    pair_weight_grad = pair_wg[:heads_all].T
    pair_gain_grad = pair_gg[0]

    pair_small = head_sum(
        jnp.concatenate([pair_weight_grad.reshape(-1), pair_gain_grad])[None]
    )
    small = jnp.concatenate([d_modulation, time_cond, pair_small, d_out_bias], axis=-1)
    small_rows = lax.all_gather(small, "dp", axis=0, tiled=True)
    mod_size = d_modulation.shape[-1]
    cond_size = time_cond.shape[-1]
    pw_size = pair_weight.size
    pg_size = pair_gain.size
    mod_chain = small_rows[:, :mod_size]
    cond_chain = small_rows[:, mod_size : mod_size + cond_size]
    rest = jnp.sum(small_rows[:, mod_size + cond_size :], axis=0)
    pair_weight_grad = rest[:pw_size].reshape(pair_weight.shape)
    pair_gain_grad = rest[pw_size : pw_size + pg_size]
    out_bias_grad = rest[pw_size + pg_size :]
    cond_act = lax.optimization_barrier(jax.nn.silu(cond_chain).astype(jnp.bfloat16)).astype(
        jnp.float32
    )
    mod_weight_grad = jnp.dot(cond_act.T, mod_chain, precision=precise)
    mod_bias_grad = jnp.sum(mod_chain, axis=0)
    cond_grad = jnp.dot(
        d_modulation, mod_weight.astype(jnp.float32).T, precision=precise
    ) * silu_slope(time_cond)

    cuts = [0, 3 * proj, 4 * proj, 4 * proj + 2 * ffn, 4 * proj + 3 * ffn]
    pieces = [reduced[:, cuts[i] : cuts[i + 1]] for i in range(4)]
    qkv_grad = pieces[0].reshape(-1, 3, proj)
    out_weight_grad = pieces[1].T
    gate_up_grad = pieces[2].reshape(-1, 2, ffn)
    down_grad = pieces[3].T
    return (
        layer_output,
        input_grad,
        pair_grad,
        cond_grad,
        mod_weight_grad,
        mod_bias_grad,
        qkv_grad,
        pair_gain_grad,
        pair_weight_grad,
        out_weight_grad,
        out_bias_grad,
        gate_up_grad,
        down_grad,
    )


def solution(mesh):
    placed = (
        P("dp", "head", None),
        P("dp", "head", None, None),
        P("dp", None),
        P("dp"),
        P("dp", None),
        P(),
        P(),
        P(None, None, "head"),
        P(),
        P(),
        P("head", None),
        P(),
        P(None, None, "head"),
        P("head", None),
        P("dp", "head", None),
    )
    return jax.shard_map(
        shards,
        mesh=mesh,
        in_specs=placed,
        out_specs=(
            P("dp", "head", None),
            P("dp", "head", None),
            P("dp", "head", None, None),
            P("dp", None),
            P(),
            P(),
            P("dp", None, "head"),
            P(),
            P(),
            P("head", "dp"),
            P(),
            P("dp", None, "head"),
            P("head", "dp"),
        ),
        check_vma=False,
    )
```

```python
import jax
import jax.numpy as jnp
from jax import lax
from jax.experimental import pallas as pl
from jax.experimental.pallas import tpu as pltpu
from jax.sharding import PartitionSpec as P

DH = 64


epsilon = 1e-05
masked_score = -1000000000.0
precise = lax.Precision.HIGHEST
LANES = 128
PAIR_TILE = 4096
PAIR_BACK_TILE = 2048
HEAD_PAD = 16


def pair_stats(x):
    centred = x - jnp.mean(x, axis=-1, keepdims=True)
    inv_std = lax.rsqrt(jnp.mean(centred * centred, axis=-1, keepdims=True) + epsilon)
    return centred * inv_std, inv_std


def pair_forward_kernel(x_ref, gain_ref, wt_ref, bias_ref):
    normed, _ = pair_stats(x_ref[...].astype(jnp.float32))
    scaled = (normed * gain_ref[...]).astype(jnp.bfloat16)
    bias = lax.dot_general(
        wt_ref[...], scaled, (((1,), (1,)), ((), ())), preferred_element_type=jnp.float32
    )
    bias_ref[...] = bias[: bias_ref.shape[0]].astype(bias_ref.dtype)


def pair_forward(flat, gain, wt, heads):
    m, width = flat.shape
    tile = min(PAIR_TILE, m)
    return pl.pallas_call(
        pair_forward_kernel,
        grid=(m // tile,),
        in_specs=[
            pl.BlockSpec((tile, width), lambda i: (i, 0)),
            pl.BlockSpec((1, width), lambda i: (0, 0)),
            pl.BlockSpec(wt.shape, lambda i: (0, 0)),
        ],
        out_specs=pl.BlockSpec((heads, tile), lambda i: (0, i)),
        out_shape=jax.ShapeDtypeStruct((heads, m), jnp.bfloat16),
        cost_estimate=pl.CostEstimate(
            flops=m * width * (2 * HEAD_PAD + 10),
            transcendentals=m,
            bytes_accessed=m * width * 2 + heads * m * 2,
        ),
    )(flat, gain, wt)


def pair_backward_kernel(x_ref, ds_ref, gain_ref, wt_ref, grad_ref, wg_ref, gg_ref):
    step = pl.program_id(0)
    normed, inv_std = pair_stats(x_ref[...].astype(jnp.float32))
    gain = gain_ref[...]
    scaled = (normed * gain).astype(jnp.bfloat16)
    ds = ds_ref[...]
    d_scaled = lax.dot_general(
        ds, wt_ref[...], (((0,), (0,)), ((), ())), preferred_element_type=jnp.float32
    )
    wg = lax.dot_general(ds, scaled, (((1,), (0,)), ((), ())), preferred_element_type=jnp.float32)
    gg = jnp.sum(d_scaled * normed, axis=0, keepdims=True)
    d_normed = d_scaled * gain
    mean_grad = jnp.mean(d_normed, axis=-1, keepdims=True)
    mean_proj = jnp.mean(d_normed * normed, axis=-1, keepdims=True)
    grad_ref[...] = (inv_std * (d_normed - mean_grad - normed * mean_proj)).astype(grad_ref.dtype)

    @pl.when(step == 0)
    def _():
        wg_ref[...] = jnp.zeros_like(wg_ref)
        gg_ref[...] = jnp.zeros_like(gg_ref)

    wg_ref[...] += wg
    gg_ref[...] += gg


def pair_backward(flat, ds, gain, wt):
    m, width = flat.shape
    tile = min(PAIR_BACK_TILE, m)
    pad = ds.shape[0]
    return pl.pallas_call(
        pair_backward_kernel,
        grid=(m // tile,),
        in_specs=[
            pl.BlockSpec((tile, width), lambda i: (i, 0)),
            pl.BlockSpec((pad, tile), lambda i: (0, i)),
            pl.BlockSpec((1, width), lambda i: (0, 0)),
            pl.BlockSpec(wt.shape, lambda i: (0, 0)),
        ],
        out_specs=[
            pl.BlockSpec((tile, width), lambda i: (i, 0)),
            pl.BlockSpec((pad, width), lambda i: (0, 0)),
            pl.BlockSpec((1, width), lambda i: (0, 0)),
        ],
        out_shape=[
            jax.ShapeDtypeStruct((m, width), jnp.bfloat16),
            jax.ShapeDtypeStruct((pad, width), jnp.float32),
            jax.ShapeDtypeStruct((1, width), jnp.float32),
        ],
        compiler_params=pltpu.CompilerParams(dimension_semantics=("arbitrary",)),
        cost_estimate=pl.CostEstimate(
            flops=m * width * (4 * HEAD_PAD + 20),
            transcendentals=m,
            bytes_accessed=2 * m * width * 2 + pad * m * 2,
        ),
    )(flat, ds, gain, wt)


def layer_norm(values):
    centred = values - jnp.mean(values, axis=-1, keepdims=True)
    inv_std = lax.rsqrt(jnp.mean(centred * centred, axis=-1, keepdims=True) + epsilon)
    return (centred * inv_std, inv_std)


def norm_back(normed, inv_std, grad):
    mean_grad = jnp.mean(grad, axis=-1, keepdims=True)
    mean_proj = jnp.mean(grad * normed, axis=-1, keepdims=True)
    return inv_std * (grad - mean_grad - normed * mean_proj)


def silu_slope(values):
    sigma = jax.nn.sigmoid(values)
    return sigma * (1.0 + values * (1.0 - sigma))


def head_split(values):
    return values.reshape(values.shape[:-1] + (values.shape[-1] // DH, DH))


def swap_heads(values):
    return lax.ppermute(values, "head", [(0, 1), (1, 0)])


def whole_rows(own, first):
    other = swap_heads(own)
    return jnp.where(
        first,
        jnp.concatenate([own, other], axis=0),
        jnp.concatenate([other, own], axis=0),
    )


def own_rows(values, head, rows):
    return lax.dynamic_slice_in_dim(values, head * rows, rows, 1)


def head_sum(part):
    return part + swap_heads(part)


def trade_blocks(values, head, size, axis, mine_axis):
    mine = lax.dynamic_slice_in_dim(values, head * size, size, axis)
    theirs = swap_heads(lax.dynamic_slice_in_dim(values, (1 - head) * size, size, axis))
    return jnp.where(
        head == 0,
        jnp.concatenate([mine, theirs], axis=mine_axis),
        jnp.concatenate([theirs, mine], axis=mine_axis),
    )


def attn_scores(queries, keys, biases, valid):
    scores = jnp.einsum("cqhe,ckhe->chqk", queries, keys, preferred_element_type=jnp.float32)
    scores = scores * DH ** (-0.5) + biases.astype(jnp.float32)
    return jnp.where(valid[:, None, None, :], scores, masked_score)


def to_chunks(values, parts):
    return values.reshape(parts, -1, LANES)


def shards(
    layer_input,
    pair_input,
    time_cond,
    chain_lengths,
    residue_mask,
    mod_weight,
    mod_bias,
    qkv_weight,
    pair_gain,
    pair_weight,
    out_weight,
    out_bias,
    gate_up_weight,
    down_weight,
    output_grad,
):
    assert layer_input.shape[0] == 1
    rows = layer_input.shape[1]
    width = layer_input.shape[2]
    length = residue_mask.shape[1]
    head = lax.axis_index("head")
    first = head == 0
    data_count = lax.axis_size("dp")
    proj = qkv_weight.shape[2]
    ffn = gate_up_weight.shape[2]
    qkv_w = qkv_weight.reshape(width, 3 * proj)
    gate_up_w = gate_up_weight.reshape(width, 2 * ffn)

    x_rows = whole_rows(layer_input[0], first)
    g_rows = whole_rows(output_grad[0], first)

    positions = jnp.arange(length, dtype=jnp.int32)
    valid = (positions < chain_lengths[0]) & ((residue_mask[0] == 1) | (positions == 0))
    silu_cond = jax.nn.silu(time_cond).astype(jnp.bfloat16)
    modulation = jnp.dot(silu_cond, mod_weight, preferred_element_type=jnp.float32) + mod_bias
    scale_a, shift_a, gate_a, scale_t, shift_t, gate_t = [
        modulation[:, section * width : (section + 1) * width] for section in range(6)
    ]

    heads_all = pair_weight.shape[1]
    pair_width = pair_input.shape[-1]
    pair_flat = pair_input.reshape(-1, pair_width)
    pair_wt = jnp.pad(pair_weight.T, ((0, HEAD_PAD - heads_all), (0, 0)))
    pair_gain_row = pair_gain.reshape(1, pair_width)
    bias_flat = pair_forward(pair_flat, pair_gain_row, pair_wt, heads_all)
    bias_rows = bias_flat.reshape(heads_all, rows, length)
    heads_own = proj // DH
    biases = trade_blocks(bias_rows, head, heads_own, 0, 1)

    residues = x_rows.astype(jnp.float32)
    norm_in, inv_in = layer_norm(residues)
    normed_a = (norm_in * (1.0 + scale_a) + shift_a).astype(jnp.bfloat16)
    projected = jnp.dot(normed_a, qkv_w, preferred_element_type=jnp.float32).astype(jnp.bfloat16)
    queries = head_split(projected[:, :proj])
    keys = head_split(projected[:, proj : 2 * proj])
    values = head_split(projected[:, 2 * proj :])
    scores = jnp.einsum("qhe,khe->hqk", queries, keys, preferred_element_type=jnp.float32)
    scores = scores * DH ** (-0.5) + biases.astype(jnp.float32)
    scores = jnp.where(valid[None, None, :], scores, masked_score)
    row_max = jnp.max(scores, axis=-1, keepdims=True)
    exp_scores = jnp.exp(scores - row_max)
    row_total = jnp.sum(exp_scores, axis=-1, keepdims=True)
    attn_probs = exp_scores / row_total
    probs_low = attn_probs.astype(jnp.bfloat16)
    mixed = jnp.einsum("hqk,khe->qhe", probs_low, values, preferred_element_type=jnp.float32)
    mixed = mixed.reshape(length, proj).astype(jnp.bfloat16)
    attn_part = jnp.dot(mixed, out_weight, preferred_element_type=jnp.float32)
    attn_branch = head_sum(attn_part) + out_bias
    sig_a = jax.nn.sigmoid(gate_a)
    middle = residues + sig_a * attn_branch

    norm_mid, inv_mid = layer_norm(middle)
    normed_t = (norm_mid * (1.0 + scale_t) + shift_t).astype(jnp.bfloat16)
    gate_up = jnp.dot(normed_t, gate_up_w, preferred_element_type=jnp.float32)
    gate_pre = gate_up[:, :ffn]
    up_pre = gate_up[:, ffn:]
    hidden = (jax.nn.silu(gate_pre) * up_pre).astype(jnp.bfloat16)
    ffn_part = jnp.dot(hidden, down_weight, preferred_element_type=jnp.float32).astype(jnp.bfloat16)
    ffn_branch = ffn_part.astype(jnp.float32) + swap_heads(ffn_part).astype(jnp.float32)
    sig_t = jax.nn.sigmoid(gate_t)
    layer_output = own_rows((middle + sig_t * ffn_branch).astype(jnp.bfloat16)[None], head, rows)

    grad_out = g_rows.astype(jnp.float32)
    d_ffn = (grad_out * sig_t).astype(jnp.bfloat16)
    d_gate_t = jnp.sum(grad_out * ffn_branch * sig_t * (1.0 - sig_t), axis=0, keepdims=True)
    down_grad_t = lax.dot_general(
        d_ffn, hidden, (((0,), (0,)), ((), ())), preferred_element_type=jnp.float32
    )
    d_hidden = lax.dot_general(
        d_ffn, down_weight, (((1,), (1,)), ((), ())), preferred_element_type=jnp.float32
    )
    d_gate = d_hidden * up_pre * silu_slope(gate_pre)
    d_up = d_hidden * jax.nn.silu(gate_pre)
    d_gate_up = jnp.concatenate([d_gate, d_up], axis=1).astype(jnp.bfloat16)
    gate_up_grad = lax.dot_general(
        normed_t, d_gate_up, (((0,), (0,)), ((), ())), preferred_element_type=jnp.float32
    )
    ffn_in_part = lax.dot_general(
        d_gate_up, gate_up_w, (((1,), (1,)), ((), ())), preferred_element_type=jnp.float32
    )
    d_normed_t = head_sum(ffn_in_part)
    d_middle = grad_out + norm_back(norm_mid, inv_mid, d_normed_t * (1.0 + scale_t))
    d_scale_t = jnp.sum(d_normed_t * norm_mid, axis=0, keepdims=True)
    d_shift_t = jnp.sum(d_normed_t, axis=0, keepdims=True)
    d_attn = d_middle * sig_a
    d_gate_a = jnp.sum(d_middle * attn_branch * sig_a * (1.0 - sig_a), axis=0, keepdims=True)
    d_out_bias = jnp.sum(d_attn, axis=0, keepdims=True)
    d_attn_low = d_attn.astype(jnp.bfloat16)

    out_weight_grad_t = lax.dot_general(
        d_attn_low, mixed, (((0,), (0,)), ((), ())), preferred_element_type=jnp.float32
    )
    d_mixed = head_split(
        lax.dot_general(
            d_attn_low, out_weight, (((1,), (1,)), ((), ())), preferred_element_type=jnp.float32
        ).astype(jnp.bfloat16)
    )
    d_values = jnp.einsum("hqk,qhe->khe", probs_low, d_mixed, preferred_element_type=jnp.float32)
    d_probs = jnp.einsum("qhe,khe->hqk", d_mixed, values, preferred_element_type=jnp.float32)
    d_scores = (
        attn_probs * (d_probs - jnp.sum(d_probs * attn_probs, axis=-1, keepdims=True))
    ).astype(jnp.bfloat16)
    d_queries = jnp.einsum(
        "hqk,khe->qhe", d_scores, keys, preferred_element_type=jnp.float32
    ) * DH ** (-0.5)
    d_keys = jnp.einsum(
        "hqk,qhe->khe", d_scores, queries, preferred_element_type=jnp.float32
    ) * DH ** (-0.5)
    d_qkv = jnp.concatenate(
        [d_queries.reshape(length, proj), d_keys.reshape(length, proj), d_values.reshape(length, proj)],
        axis=1,
    ).astype(jnp.bfloat16)
    qkv_grad = lax.dot_general(
        normed_a, d_qkv, (((0,), (0,)), ((), ())), preferred_element_type=jnp.float32
    )

    packed = jnp.concatenate(
        [
            qkv_grad.astype(jnp.bfloat16),
            out_weight_grad_t.astype(jnp.bfloat16),
            gate_up_grad.astype(jnp.bfloat16),
            down_grad_t.astype(jnp.bfloat16),
        ],
        axis=1,
    )
    reduced = lax.psum_scatter(packed, "dp", scatter_dimension=0, tiled=True).astype(jnp.float32)

    attn_in_part = lax.dot_general(
        d_qkv, qkv_w, (((1,), (1,)), ((), ())), preferred_element_type=jnp.float32
    ).astype(jnp.bfloat16)
    d_normed_a = attn_in_part.astype(jnp.float32) + swap_heads(attn_in_part).astype(jnp.float32)
    input_grad = own_rows(
        (d_middle + norm_back(norm_in, inv_in, d_normed_a * (1.0 + scale_a)))[None], head, rows
    )
    d_scale_a = jnp.sum(d_normed_a * norm_in, axis=0, keepdims=True)
    d_shift_a = jnp.sum(d_normed_a, axis=0, keepdims=True)
    d_modulation = jnp.concatenate(
        [d_scale_a, d_shift_a, d_gate_a, d_scale_t, d_shift_t, d_gate_t], axis=-1
    )

    d_bias_rows = trade_blocks(d_scores, head, rows, 1, 0)
    d_bias_flat = jnp.pad(d_bias_rows.reshape(heads_all, -1), ((0, HEAD_PAD - heads_all), (0, 0)))
    pair_grad, pair_wg, pair_gg = pair_backward(pair_flat, d_bias_flat, pair_gain_row, pair_wt)
    pair_grad = pair_grad.reshape(pair_input.shape)
    pair_weight_grad = pair_wg[:heads_all].T
    pair_gain_grad = pair_gg[0]

    pair_small = head_sum(
        jnp.concatenate([pair_weight_grad.reshape(-1), pair_gain_grad])[None]
    )
    small = jnp.concatenate([d_modulation, time_cond, pair_small, d_out_bias], axis=-1)
    small_rows = lax.all_gather(small, "dp", axis=0, tiled=True)
    mod_size = d_modulation.shape[-1]
    cond_size = time_cond.shape[-1]
    pw_size = pair_weight.size
    pg_size = pair_gain.size
    mod_chain = small_rows[:, :mod_size]
    cond_chain = small_rows[:, mod_size : mod_size + cond_size]
    rest = jnp.sum(small_rows[:, mod_size + cond_size :], axis=0)
    pair_weight_grad = rest[:pw_size].reshape(pair_weight.shape)
    pair_gain_grad = rest[pw_size : pw_size + pg_size]
    out_bias_grad = rest[pw_size + pg_size :]
    cond_act = lax.optimization_barrier(jax.nn.silu(cond_chain).astype(jnp.bfloat16)).astype(
        jnp.float32
    )
    mod_weight_grad = jnp.dot(cond_act.T, mod_chain, precision=precise)
    mod_bias_grad = jnp.sum(mod_chain, axis=0)
    cond_grad = jnp.dot(
        d_modulation, mod_weight.astype(jnp.float32).T, precision=precise
    ) * silu_slope(time_cond)

    cuts = [0, 3 * proj, 4 * proj, 4 * proj + 2 * ffn, 4 * proj + 3 * ffn]
    pieces = [reduced[:, cuts[i] : cuts[i + 1]] for i in range(4)]
    qkv_grad = pieces[0].reshape(-1, 3, proj)
    out_weight_grad = pieces[1].T
    gate_up_grad = pieces[2].reshape(-1, 2, ffn)
    down_grad = pieces[3].T
    return (
        layer_output,
        input_grad,
        pair_grad,
        cond_grad,
        mod_weight_grad,
        mod_bias_grad,
        qkv_grad,
        pair_gain_grad,
        pair_weight_grad,
        out_weight_grad,
        out_bias_grad,
        gate_up_grad,
        down_grad,
    )


def solution(mesh):
    placed = (
        P("dp", "head", None),
        P("dp", "head", None, None),
        P("dp", None),
        P("dp"),
        P("dp", None),
        P(),
        P(),
        P(None, None, "head"),
        P(),
        P(),
        P("head", None),
        P(),
        P(None, None, "head"),
        P("head", None),
        P("dp", "head", None),
    )
    return jax.shard_map(
        shards,
        mesh=mesh,
        in_specs=placed,
        out_specs=(
            P("dp", "head", None),
            P("dp", "head", None),
            P("dp", "head", None, None),
            P("dp", None),
            P(),
            P(),
            P("dp", None, "head"),
            P(),
            P(),
            P("head", "dp"),
            P(),
            P("dp", None, "head"),
            P("head", "dp"),
        ),
        check_vma=False,
    )
```

```python
import jax
import jax.numpy as jnp
from jax import lax
from jax.experimental import pallas as pl
from jax.experimental.pallas import tpu as pltpu
from jax.sharding import PartitionSpec as P

DH = 64


epsilon = 1e-05
masked_score = -1000000000.0
precise = lax.Precision.HIGHEST
LANES = 128
PAIR_TILE = 4096
PAIR_BACK_TILE = 2048
HEAD_PAD = 16


def pair_stats(x):
    centred = x - jnp.mean(x, axis=-1, keepdims=True)
    inv_std = lax.rsqrt(jnp.mean(centred * centred, axis=-1, keepdims=True) + epsilon)
    return centred * inv_std, inv_std


def pair_forward_kernel(x_ref, gain_ref, wt_ref, bias_ref):
    normed, _ = pair_stats(x_ref[...].astype(jnp.float32))
    scaled = (normed * gain_ref[...]).astype(jnp.bfloat16)
    bias = lax.dot_general(
        wt_ref[...], scaled, (((1,), (1,)), ((), ())), preferred_element_type=jnp.float32
    )
    bias_ref[...] = bias[: bias_ref.shape[0]].astype(bias_ref.dtype)


def pair_forward(flat, gain, wt, heads):
    m, width = flat.shape
    tile = min(PAIR_TILE, m)
    return pl.pallas_call(
        pair_forward_kernel,
        grid=(m // tile,),
        in_specs=[
            pl.BlockSpec((tile, width), lambda i: (i, 0)),
            pl.BlockSpec((1, width), lambda i: (0, 0)),
            pl.BlockSpec(wt.shape, lambda i: (0, 0)),
        ],
        out_specs=pl.BlockSpec((heads, tile), lambda i: (0, i)),
        out_shape=jax.ShapeDtypeStruct((heads, m), jnp.bfloat16),
        cost_estimate=pl.CostEstimate(
            flops=m * width * (2 * HEAD_PAD + 10),
            transcendentals=m,
            bytes_accessed=m * width * 2 + heads * m * 2,
        ),
    )(flat, gain, wt)


def pair_backward_kernel(x_ref, ds_ref, gain_ref, wt_ref, grad_ref, wg_ref, gg_ref):
    step = pl.program_id(0)
    normed, inv_std = pair_stats(x_ref[...].astype(jnp.float32))
    gain = gain_ref[...]
    scaled = (normed * gain).astype(jnp.bfloat16)
    ds = ds_ref[...]
    d_scaled = lax.dot_general(
        ds, wt_ref[...], (((0,), (0,)), ((), ())), preferred_element_type=jnp.float32
    )
    wg = lax.dot_general(ds, scaled, (((1,), (0,)), ((), ())), preferred_element_type=jnp.float32)
    gg = jnp.sum(d_scaled * normed, axis=0, keepdims=True)
    d_normed = d_scaled * gain
    mean_grad = jnp.mean(d_normed, axis=-1, keepdims=True)
    mean_proj = jnp.mean(d_normed * normed, axis=-1, keepdims=True)
    grad_ref[...] = (inv_std * (d_normed - mean_grad - normed * mean_proj)).astype(grad_ref.dtype)

    @pl.when(step == 0)
    def _():
        wg_ref[...] = jnp.zeros_like(wg_ref)
        gg_ref[...] = jnp.zeros_like(gg_ref)

    wg_ref[...] += wg
    gg_ref[...] += gg


def pair_backward(flat, ds, gain, wt):
    m, width = flat.shape
    tile = min(PAIR_BACK_TILE, m)
    pad = ds.shape[0]
    return pl.pallas_call(
        pair_backward_kernel,
        grid=(m // tile,),
        in_specs=[
            pl.BlockSpec((tile, width), lambda i: (i, 0)),
            pl.BlockSpec((pad, tile), lambda i: (0, i)),
            pl.BlockSpec((1, width), lambda i: (0, 0)),
            pl.BlockSpec(wt.shape, lambda i: (0, 0)),
        ],
        out_specs=[
            pl.BlockSpec((tile, width), lambda i: (i, 0)),
            pl.BlockSpec((pad, width), lambda i: (0, 0)),
            pl.BlockSpec((1, width), lambda i: (0, 0)),
        ],
        out_shape=[
            jax.ShapeDtypeStruct((m, width), jnp.bfloat16),
            jax.ShapeDtypeStruct((pad, width), jnp.float32),
            jax.ShapeDtypeStruct((1, width), jnp.float32),
        ],
        compiler_params=pltpu.CompilerParams(dimension_semantics=("arbitrary",)),
        cost_estimate=pl.CostEstimate(
            flops=m * width * (4 * HEAD_PAD + 20),
            transcendentals=m,
            bytes_accessed=2 * m * width * 2 + pad * m * 2,
        ),
    )(flat, ds, gain, wt)


def layer_norm(values):
    centred = values - jnp.mean(values, axis=-1, keepdims=True)
    inv_std = lax.rsqrt(jnp.mean(centred * centred, axis=-1, keepdims=True) + epsilon)
    return (centred * inv_std, inv_std)


def norm_back(normed, inv_std, grad):
    mean_grad = jnp.mean(grad, axis=-1, keepdims=True)
    mean_proj = jnp.mean(grad * normed, axis=-1, keepdims=True)
    return inv_std * (grad - mean_grad - normed * mean_proj)


def silu_slope(values):
    sigma = jax.nn.sigmoid(values)
    return sigma * (1.0 + values * (1.0 - sigma))


def head_split(values):
    return values.reshape(values.shape[:-1] + (values.shape[-1] // DH, DH))


def swap_heads(values):
    return lax.ppermute(values, "head", [(0, 1), (1, 0)])


def whole_rows(own, first):
    other = swap_heads(own)
    return jnp.where(
        first,
        jnp.concatenate([own, other], axis=0),
        jnp.concatenate([other, own], axis=0),
    )


def dp_gather(values):
    count = lax.axis_size("dp")
    index = lax.axis_index("dp")
    block = values
    step = 1
    while step < count:
        other = lax.ppermute(block, "dp", [(i, i ^ step) for i in range(count)])
        block = jnp.where(
            (index & step) == 0,
            jnp.concatenate([block, other], axis=0),
            jnp.concatenate([other, block], axis=0),
        )
        step *= 2
    return block


def dp_sum(values):
    count = lax.axis_size("dp")
    index = lax.axis_index("dp")
    step = 1
    while step < count:
        other = lax.ppermute(values, "dp", [(i, i ^ step) for i in range(count)])
        values = jnp.where((index & step) == 0, values + other, other + values)
        step *= 2
    return values


def own_rows(values, head, rows):
    return lax.dynamic_slice_in_dim(values, head * rows, rows, 1)


def head_sum(part):
    return part + swap_heads(part)


def trade_blocks(values, head, size, axis, mine_axis):
    mine = lax.dynamic_slice_in_dim(values, head * size, size, axis)
    theirs = swap_heads(lax.dynamic_slice_in_dim(values, (1 - head) * size, size, axis))
    return jnp.where(
        head == 0,
        jnp.concatenate([mine, theirs], axis=mine_axis),
        jnp.concatenate([theirs, mine], axis=mine_axis),
    )


def attn_scores(queries, keys, biases, valid):
    scores = jnp.einsum("cqhe,ckhe->chqk", queries, keys, preferred_element_type=jnp.float32)
    scores = scores * DH ** (-0.5) + biases.astype(jnp.float32)
    return jnp.where(valid[:, None, None, :], scores, masked_score)


def to_chunks(values, parts):
    return values.reshape(parts, -1, LANES)


def shards(
    layer_input,
    pair_input,
    time_cond,
    chain_lengths,
    residue_mask,
    mod_weight,
    mod_bias,
    qkv_weight,
    pair_gain,
    pair_weight,
    out_weight,
    out_bias,
    gate_up_weight,
    down_weight,
    output_grad,
):
    assert layer_input.shape[0] == 1
    rows = layer_input.shape[1]
    width = layer_input.shape[2]
    length = residue_mask.shape[1]
    head = lax.axis_index("head")
    first = head == 0
    data_count = lax.axis_size("dp")
    proj = qkv_weight.shape[2]
    ffn = gate_up_weight.shape[2]
    qkv_w = qkv_weight.reshape(width, 3 * proj)
    gate_up_w = gate_up_weight.reshape(width, 2 * ffn)

    x_rows = whole_rows(layer_input[0], first)
    g_rows = whole_rows(output_grad[0], first)

    positions = jnp.arange(length, dtype=jnp.int32)
    valid = (positions < chain_lengths[0]) & ((residue_mask[0] == 1) | (positions == 0))
    silu_cond = jax.nn.silu(time_cond).astype(jnp.bfloat16)
    modulation = jnp.dot(silu_cond, mod_weight, preferred_element_type=jnp.float32) + mod_bias
    scale_a, shift_a, gate_a, scale_t, shift_t, gate_t = [
        modulation[:, section * width : (section + 1) * width] for section in range(6)
    ]

    heads_all = pair_weight.shape[1]
    pair_width = pair_input.shape[-1]
    pair_flat = pair_input.reshape(-1, pair_width)
    pair_wt = jnp.pad(pair_weight.T, ((0, HEAD_PAD - heads_all), (0, 0)))
    pair_gain_row = pair_gain.reshape(1, pair_width)
    bias_flat = pair_forward(pair_flat, pair_gain_row, pair_wt, heads_all)
    bias_rows = bias_flat.reshape(heads_all, rows, length)
    heads_own = proj // DH
    biases = trade_blocks(bias_rows, head, heads_own, 0, 1)

    residues = x_rows.astype(jnp.float32)
    norm_in, inv_in = layer_norm(residues)
    normed_a = (norm_in * (1.0 + scale_a) + shift_a).astype(jnp.bfloat16)
    projected = jnp.dot(normed_a, qkv_w, preferred_element_type=jnp.float32).astype(jnp.bfloat16)
    queries = head_split(projected[:, :proj])
    keys = head_split(projected[:, proj : 2 * proj])
    values = head_split(projected[:, 2 * proj :])
    scores = jnp.einsum("qhe,khe->hqk", queries, keys, preferred_element_type=jnp.float32)
    scores = scores * DH ** (-0.5) + biases.astype(jnp.float32)
    scores = jnp.where(valid[None, None, :], scores, masked_score)
    row_max = jnp.max(scores, axis=-1, keepdims=True)
    exp_scores = jnp.exp(scores - row_max)
    row_total = jnp.sum(exp_scores, axis=-1, keepdims=True)
    attn_probs = exp_scores / row_total
    probs_low = attn_probs.astype(jnp.bfloat16)
    mixed = jnp.einsum("hqk,khe->qhe", probs_low, values, preferred_element_type=jnp.float32)
    mixed = mixed.reshape(length, proj).astype(jnp.bfloat16)
    attn_part = jnp.dot(mixed, out_weight, preferred_element_type=jnp.float32)
    attn_branch = head_sum(attn_part) + out_bias
    sig_a = jax.nn.sigmoid(gate_a)
    middle = residues + sig_a * attn_branch

    norm_mid, inv_mid = layer_norm(middle)
    normed_t = (norm_mid * (1.0 + scale_t) + shift_t).astype(jnp.bfloat16)
    gate_up = jnp.dot(normed_t, gate_up_w, preferred_element_type=jnp.float32)
    gate_pre = gate_up[:, :ffn]
    up_pre = gate_up[:, ffn:]
    hidden = (jax.nn.silu(gate_pre) * up_pre).astype(jnp.bfloat16)
    ffn_part = jnp.dot(hidden, down_weight, preferred_element_type=jnp.float32).astype(jnp.bfloat16)
    ffn_branch = ffn_part.astype(jnp.float32) + swap_heads(ffn_part).astype(jnp.float32)
    sig_t = jax.nn.sigmoid(gate_t)
    layer_output = own_rows((middle + sig_t * ffn_branch).astype(jnp.bfloat16)[None], head, rows)

    grad_out = g_rows.astype(jnp.float32)
    d_ffn = (grad_out * sig_t).astype(jnp.bfloat16)
    d_gate_t = jnp.sum(grad_out * ffn_branch * sig_t * (1.0 - sig_t), axis=0, keepdims=True)
    down_grad_t = lax.dot_general(
        d_ffn, hidden, (((0,), (0,)), ((), ())), preferred_element_type=jnp.float32
    )
    d_hidden = lax.dot_general(
        d_ffn, down_weight, (((1,), (1,)), ((), ())), preferred_element_type=jnp.float32
    )
    d_gate = d_hidden * up_pre * silu_slope(gate_pre)
    d_up = d_hidden * jax.nn.silu(gate_pre)
    d_gate_up = jnp.concatenate([d_gate, d_up], axis=1).astype(jnp.bfloat16)
    gate_up_grad = lax.dot_general(
        normed_t, d_gate_up, (((0,), (0,)), ((), ())), preferred_element_type=jnp.float32
    )
    ffn_in_part = lax.dot_general(
        d_gate_up, gate_up_w, (((1,), (1,)), ((), ())), preferred_element_type=jnp.float32
    )
    d_normed_t = head_sum(ffn_in_part)
    d_middle = grad_out + norm_back(norm_mid, inv_mid, d_normed_t * (1.0 + scale_t))
    d_scale_t = jnp.sum(d_normed_t * norm_mid, axis=0, keepdims=True)
    d_shift_t = jnp.sum(d_normed_t, axis=0, keepdims=True)
    d_attn = d_middle * sig_a
    d_gate_a = jnp.sum(d_middle * attn_branch * sig_a * (1.0 - sig_a), axis=0, keepdims=True)
    d_out_bias = jnp.sum(d_attn, axis=0, keepdims=True)
    d_attn_low = d_attn.astype(jnp.bfloat16)

    out_weight_grad_t = lax.dot_general(
        d_attn_low, mixed, (((0,), (0,)), ((), ())), preferred_element_type=jnp.float32
    )
    d_mixed = head_split(
        lax.dot_general(
            d_attn_low, out_weight, (((1,), (1,)), ((), ())), preferred_element_type=jnp.float32
        ).astype(jnp.bfloat16)
    )
    d_values = jnp.einsum("hqk,qhe->khe", probs_low, d_mixed, preferred_element_type=jnp.float32)
    d_probs = jnp.einsum("qhe,khe->hqk", d_mixed, values, preferred_element_type=jnp.float32)
    d_scores = (
        attn_probs * (d_probs - jnp.sum(d_probs * attn_probs, axis=-1, keepdims=True))
    ).astype(jnp.bfloat16)
    d_queries = jnp.einsum(
        "hqk,khe->qhe", d_scores, keys, preferred_element_type=jnp.float32
    ) * DH ** (-0.5)
    d_keys = jnp.einsum(
        "hqk,qhe->khe", d_scores, queries, preferred_element_type=jnp.float32
    ) * DH ** (-0.5)
    d_qkv = jnp.concatenate(
        [d_queries.reshape(length, proj), d_keys.reshape(length, proj), d_values.reshape(length, proj)],
        axis=1,
    ).astype(jnp.bfloat16)
    qkv_grad = lax.dot_general(
        normed_a, d_qkv, (((0,), (0,)), ((), ())), preferred_element_type=jnp.float32
    )

    packed = jnp.zeros((width, 4 * proj + 3 * ffn), jnp.bfloat16)
    packed = lax.dynamic_update_slice(packed, gate_up_grad.astype(jnp.bfloat16), (0, 4 * proj))
    packed = lax.dynamic_update_slice(
        packed, down_grad_t.astype(jnp.bfloat16), (0, 4 * proj + 2 * ffn)
    )
    packed = lax.dynamic_update_slice(packed, out_weight_grad_t.astype(jnp.bfloat16), (0, 3 * proj))
    packed = lax.dynamic_update_slice(packed, qkv_grad.astype(jnp.bfloat16), (0, 0))
    reduced = lax.psum_scatter(packed, "dp", scatter_dimension=0, tiled=True).astype(jnp.float32)

    attn_in_part = lax.dot_general(
        d_qkv, qkv_w, (((1,), (1,)), ((), ())), preferred_element_type=jnp.float32
    ).astype(jnp.bfloat16)
    d_normed_a = attn_in_part.astype(jnp.float32) + swap_heads(attn_in_part).astype(jnp.float32)
    input_grad = own_rows(
        (d_middle + norm_back(norm_in, inv_in, d_normed_a * (1.0 + scale_a)))[None], head, rows
    )
    d_scale_a = jnp.sum(d_normed_a * norm_in, axis=0, keepdims=True)
    d_shift_a = jnp.sum(d_normed_a, axis=0, keepdims=True)
    d_modulation = jnp.concatenate(
        [d_scale_a, d_shift_a, d_gate_a, d_scale_t, d_shift_t, d_gate_t], axis=-1
    )

    d_bias_rows = trade_blocks(d_scores, head, rows, 1, 0)
    d_bias_flat = jnp.pad(d_bias_rows.reshape(heads_all, -1), ((0, HEAD_PAD - heads_all), (0, 0)))
    pair_grad, pair_wg, pair_gg = pair_backward(pair_flat, d_bias_flat, pair_gain_row, pair_wt)
    pair_grad = pair_grad.reshape(pair_input.shape)
    pair_weight_grad = pair_wg[:heads_all].T
    pair_gain_grad = pair_gg[0]

    pair_small = head_sum(
        jnp.concatenate([pair_weight_grad.reshape(-1), pair_gain_grad])[None]
    )
    small = jnp.concatenate([d_modulation, time_cond, d_out_bias], axis=-1)
    small_rows = dp_gather(small)
    mod_size = d_modulation.shape[-1]
    cond_size = time_cond.shape[-1]
    pw_size = pair_weight.size
    mod_chain = small_rows[:, :mod_size]
    cond_chain = small_rows[:, mod_size : mod_size + cond_size]
    out_bias_grad = jnp.sum(small_rows[:, mod_size + cond_size :], axis=0)
    pair_total = dp_sum(pair_small)[0]
    pair_weight_grad = pair_total[:pw_size].reshape(pair_weight.shape)
    pair_gain_grad = pair_total[pw_size:]
    cond_act = lax.optimization_barrier(jax.nn.silu(cond_chain).astype(jnp.bfloat16)).astype(
        jnp.float32
    )
    mod_weight_grad = jnp.dot(cond_act.T, mod_chain, precision=precise)
    mod_bias_grad = jnp.sum(mod_chain, axis=0)
    cond_grad = jnp.dot(
        d_modulation, mod_weight.astype(jnp.float32).T, precision=precise
    ) * silu_slope(time_cond)

    cuts = [0, 3 * proj, 4 * proj, 4 * proj + 2 * ffn, 4 * proj + 3 * ffn]
    pieces = [reduced[:, cuts[i] : cuts[i + 1]] for i in range(4)]
    qkv_grad = pieces[0].reshape(-1, 3, proj)
    out_weight_grad = pieces[1].T
    gate_up_grad = pieces[2].reshape(-1, 2, ffn)
    down_grad = pieces[3].T
    return (
        layer_output,
        input_grad,
        pair_grad,
        cond_grad,
        mod_weight_grad,
        mod_bias_grad,
        qkv_grad,
        pair_gain_grad,
        pair_weight_grad,
        out_weight_grad,
        out_bias_grad,
        gate_up_grad,
        down_grad,
    )


def solution(mesh):
    placed = (
        P("dp", "head", None),
        P("dp", "head", None, None),
        P("dp", None),
        P("dp"),
        P("dp", None),
        P(),
        P(),
        P(None, None, "head"),
        P(),
        P(),
        P("head", None),
        P(),
        P(None, None, "head"),
        P("head", None),
        P("dp", "head", None),
    )
    return jax.shard_map(
        shards,
        mesh=mesh,
        in_specs=placed,
        out_specs=(
            P("dp", "head", None),
            P("dp", "head", None),
            P("dp", "head", None, None),
            P("dp", None),
            P(),
            P(),
            P("dp", None, "head"),
            P(),
            P(),
            P("head", "dp"),
            P(),
            P("dp", None, "head"),
            P("head", "dp"),
        ),
        check_vma=False,
    )
```

```python
import jax
import jax.numpy as jnp
from jax import lax
from jax.experimental import pallas as pl
from jax.experimental.pallas import tpu as pltpu
from jax.sharding import PartitionSpec as P

DH = 64


epsilon = 1e-05
masked_score = -1000000000.0
precise = lax.Precision.HIGHEST
LANES = 128
PAIR_TILE = 4096
PAIR_BACK_TILE = 2048
HEAD_PAD = 16


def pair_stats(x):
    centred = x - jnp.mean(x, axis=-1, keepdims=True)
    inv_std = lax.rsqrt(jnp.mean(centred * centred, axis=-1, keepdims=True) + epsilon)
    return centred * inv_std, inv_std


def pair_forward_kernel(x_ref, gain_ref, wt_ref, bias_ref):
    normed, _ = pair_stats(x_ref[...].astype(jnp.float32))
    scaled = (normed * gain_ref[...]).astype(jnp.bfloat16)
    bias = lax.dot_general(
        wt_ref[...], scaled, (((1,), (1,)), ((), ())), preferred_element_type=jnp.float32
    )
    bias_ref[...] = bias[: bias_ref.shape[0]].astype(bias_ref.dtype)


def pair_forward(flat, gain, wt, heads):
    m, width = flat.shape
    tile = min(PAIR_TILE, m)
    return pl.pallas_call(
        pair_forward_kernel,
        grid=(m // tile,),
        in_specs=[
            pl.BlockSpec((tile, width), lambda i: (i, 0)),
            pl.BlockSpec((1, width), lambda i: (0, 0)),
            pl.BlockSpec(wt.shape, lambda i: (0, 0)),
        ],
        out_specs=pl.BlockSpec((heads, tile), lambda i: (0, i)),
        out_shape=jax.ShapeDtypeStruct((heads, m), jnp.bfloat16),
        cost_estimate=pl.CostEstimate(
            flops=m * width * (2 * HEAD_PAD + 10),
            transcendentals=m,
            bytes_accessed=m * width * 2 + heads * m * 2,
        ),
    )(flat, gain, wt)


def pair_backward_kernel(x_ref, ds_ref, gain_ref, wt_ref, grad_ref, wg_ref, gg_ref):
    step = pl.program_id(0)
    normed, inv_std = pair_stats(x_ref[...].astype(jnp.float32))
    gain = gain_ref[...]
    scaled = (normed * gain).astype(jnp.bfloat16)
    ds = ds_ref[...]
    d_scaled = lax.dot_general(
        ds, wt_ref[...], (((0,), (0,)), ((), ())), preferred_element_type=jnp.float32
    )
    wg = lax.dot_general(ds, scaled, (((1,), (0,)), ((), ())), preferred_element_type=jnp.float32)
    gg = jnp.sum(d_scaled * normed, axis=0, keepdims=True)
    d_normed = d_scaled * gain
    mean_grad = jnp.mean(d_normed, axis=-1, keepdims=True)
    mean_proj = jnp.mean(d_normed * normed, axis=-1, keepdims=True)
    grad_ref[...] = (inv_std * (d_normed - mean_grad - normed * mean_proj)).astype(grad_ref.dtype)

    @pl.when(step == 0)
    def _():
        wg_ref[...] = jnp.zeros_like(wg_ref)
        gg_ref[...] = jnp.zeros_like(gg_ref)

    wg_ref[...] += wg
    gg_ref[...] += gg


def pair_backward(flat, ds, gain, wt):
    m, width = flat.shape
    tile = min(PAIR_BACK_TILE, m)
    pad = ds.shape[0]
    return pl.pallas_call(
        pair_backward_kernel,
        grid=(m // tile,),
        in_specs=[
            pl.BlockSpec((tile, width), lambda i: (i, 0)),
            pl.BlockSpec((pad, tile), lambda i: (0, i)),
            pl.BlockSpec((1, width), lambda i: (0, 0)),
            pl.BlockSpec(wt.shape, lambda i: (0, 0)),
        ],
        out_specs=[
            pl.BlockSpec((tile, width), lambda i: (i, 0)),
            pl.BlockSpec((pad, width), lambda i: (0, 0)),
            pl.BlockSpec((1, width), lambda i: (0, 0)),
        ],
        out_shape=[
            jax.ShapeDtypeStruct((m, width), jnp.bfloat16),
            jax.ShapeDtypeStruct((pad, width), jnp.float32),
            jax.ShapeDtypeStruct((1, width), jnp.float32),
        ],
        compiler_params=pltpu.CompilerParams(dimension_semantics=("arbitrary",)),
        cost_estimate=pl.CostEstimate(
            flops=m * width * (4 * HEAD_PAD + 20),
            transcendentals=m,
            bytes_accessed=2 * m * width * 2 + pad * m * 2,
        ),
    )(flat, ds, gain, wt)


def layer_norm(values):
    centred = values - jnp.mean(values, axis=-1, keepdims=True)
    inv_std = lax.rsqrt(jnp.mean(centred * centred, axis=-1, keepdims=True) + epsilon)
    return (centred * inv_std, inv_std)


def norm_back(normed, inv_std, grad):
    mean_grad = jnp.mean(grad, axis=-1, keepdims=True)
    mean_proj = jnp.mean(grad * normed, axis=-1, keepdims=True)
    return inv_std * (grad - mean_grad - normed * mean_proj)


def silu_slope(values):
    sigma = jax.nn.sigmoid(values)
    return sigma * (1.0 + values * (1.0 - sigma))


def head_split(values):
    return values.reshape(values.shape[:-1] + (values.shape[-1] // DH, DH))


def swap_heads(values):
    return lax.ppermute(values, "head", [(0, 1), (1, 0)])


def whole_rows(own, first):
    other = swap_heads(own)
    return jnp.where(
        first,
        jnp.concatenate([own, other], axis=0),
        jnp.concatenate([other, own], axis=0),
    )


def dp_gather(values):
    count = lax.axis_size("dp")
    index = lax.axis_index("dp")
    block = values
    step = 1
    while step < count:
        other = lax.ppermute(block, "dp", [(i, i ^ step) for i in range(count)])
        block = jnp.where(
            (index & step) == 0,
            jnp.concatenate([block, other], axis=0),
            jnp.concatenate([other, block], axis=0),
        )
        step *= 2
    return block


def dp_sum(values):
    count = lax.axis_size("dp")
    index = lax.axis_index("dp")
    step = 1
    while step < count:
        other = lax.ppermute(values, "dp", [(i, i ^ step) for i in range(count)])
        values = jnp.where((index & step) == 0, values + other, other + values)
        step *= 2
    return values


def own_rows(values, head, rows):
    return lax.dynamic_slice_in_dim(values, head * rows, rows, 1)


def head_sum(part):
    return part + swap_heads(part)


def trade_blocks(values, head, size, axis, mine_axis):
    mine = lax.dynamic_slice_in_dim(values, head * size, size, axis)
    theirs = swap_heads(lax.dynamic_slice_in_dim(values, (1 - head) * size, size, axis))
    return jnp.where(
        head == 0,
        jnp.concatenate([mine, theirs], axis=mine_axis),
        jnp.concatenate([theirs, mine], axis=mine_axis),
    )


def attn_scores(queries, keys, biases, valid):
    scores = jnp.einsum("cqhe,ckhe->chqk", queries, keys, preferred_element_type=jnp.float32)
    scores = scores * DH ** (-0.5) + biases.astype(jnp.float32)
    return jnp.where(valid[:, None, None, :], scores, masked_score)


def to_chunks(values, parts):
    return values.reshape(parts, -1, LANES)


def shards(
    layer_input,
    pair_input,
    time_cond,
    chain_lengths,
    residue_mask,
    mod_weight,
    mod_bias,
    qkv_weight,
    pair_gain,
    pair_weight,
    out_weight,
    out_bias,
    gate_up_weight,
    down_weight,
    output_grad,
):
    assert layer_input.shape[0] == 1
    rows = layer_input.shape[1]
    width = layer_input.shape[2]
    length = residue_mask.shape[1]
    head = lax.axis_index("head")
    first = head == 0
    data_count = lax.axis_size("dp")
    proj = qkv_weight.shape[2]
    ffn = gate_up_weight.shape[2]
    qkv_w = qkv_weight.reshape(width, 3 * proj)
    gate_up_w = gate_up_weight.reshape(width, 2 * ffn)

    x_rows = whole_rows(layer_input[0], first)
    g_rows = whole_rows(output_grad[0], first)
    out_weight_all = whole_rows(out_weight, first)

    positions = jnp.arange(length, dtype=jnp.int32)
    valid = (positions < chain_lengths[0]) & ((residue_mask[0] == 1) | (positions == 0))
    silu_cond = jax.nn.silu(time_cond).astype(jnp.bfloat16)
    modulation = jnp.dot(silu_cond, mod_weight, preferred_element_type=jnp.float32) + mod_bias
    scale_a, shift_a, gate_a, scale_t, shift_t, gate_t = [
        modulation[:, section * width : (section + 1) * width] for section in range(6)
    ]

    heads_all = pair_weight.shape[1]
    pair_width = pair_input.shape[-1]
    pair_flat = pair_input.reshape(-1, pair_width)
    pair_wt = jnp.pad(pair_weight.T, ((0, HEAD_PAD - heads_all), (0, 0)))
    pair_gain_row = pair_gain.reshape(1, pair_width)
    bias_flat = pair_forward(pair_flat, pair_gain_row, pair_wt, heads_all)
    bias_rows = bias_flat.reshape(heads_all, rows, length)
    heads_own = proj // DH
    biases = trade_blocks(bias_rows, head, heads_own, 0, 1)

    residues = x_rows.astype(jnp.float32)
    norm_in, inv_in = layer_norm(residues)
    normed_a = (norm_in * (1.0 + scale_a) + shift_a).astype(jnp.bfloat16)
    projected = jnp.dot(normed_a, qkv_w, preferred_element_type=jnp.float32).astype(jnp.bfloat16)
    queries = head_split(projected[:, :proj])
    keys = head_split(projected[:, proj : 2 * proj])
    values = head_split(projected[:, 2 * proj :])
    scores = jnp.einsum("qhe,khe->hqk", queries, keys, preferred_element_type=jnp.float32)
    scores = scores * DH ** (-0.5) + biases.astype(jnp.float32)
    scores = jnp.where(valid[None, None, :], scores, masked_score)
    row_max = jnp.max(scores, axis=-1, keepdims=True)
    exp_scores = jnp.exp(scores - row_max)
    row_total = jnp.sum(exp_scores, axis=-1, keepdims=True)
    attn_probs = exp_scores / row_total
    probs_low = attn_probs.astype(jnp.bfloat16)
    mixed = jnp.einsum("hqk,khe->qhe", probs_low, values, preferred_element_type=jnp.float32)
    mixed = mixed.reshape(length, proj).astype(jnp.bfloat16)
    mixed_all = jnp.where(
        first,
        jnp.concatenate([mixed, swap_heads(mixed)], axis=1),
        jnp.concatenate([swap_heads(mixed), mixed], axis=1),
    )
    attn_branch = jnp.dot(mixed_all, out_weight_all, preferred_element_type=jnp.float32) + out_bias
    sig_a = jax.nn.sigmoid(gate_a)
    middle = residues + sig_a * attn_branch

    norm_mid, inv_mid = layer_norm(middle)
    normed_t = (norm_mid * (1.0 + scale_t) + shift_t).astype(jnp.bfloat16)
    gate_up = jnp.dot(normed_t, gate_up_w, preferred_element_type=jnp.float32)
    gate_pre = gate_up[:, :ffn]
    up_pre = gate_up[:, ffn:]
    hidden = (jax.nn.silu(gate_pre) * up_pre).astype(jnp.bfloat16)
    ffn_part = jnp.dot(hidden, down_weight, preferred_element_type=jnp.float32).astype(jnp.bfloat16)
    ffn_branch = ffn_part.astype(jnp.float32) + swap_heads(ffn_part).astype(jnp.float32)
    sig_t = jax.nn.sigmoid(gate_t)
    layer_output = own_rows((middle + sig_t * ffn_branch).astype(jnp.bfloat16)[None], head, rows)

    grad_out = g_rows.astype(jnp.float32)
    d_ffn = (grad_out * sig_t).astype(jnp.bfloat16)
    d_gate_t = jnp.sum(grad_out * ffn_branch * sig_t * (1.0 - sig_t), axis=0, keepdims=True)
    down_grad_t = lax.dot_general(
        d_ffn, hidden, (((0,), (0,)), ((), ())), preferred_element_type=jnp.float32
    )
    d_hidden = lax.dot_general(
        d_ffn, down_weight, (((1,), (1,)), ((), ())), preferred_element_type=jnp.float32
    )
    d_gate = d_hidden * up_pre * silu_slope(gate_pre)
    d_up = d_hidden * jax.nn.silu(gate_pre)
    d_gate_up = jnp.concatenate([d_gate, d_up], axis=1).astype(jnp.bfloat16)
    gate_up_grad = lax.dot_general(
        normed_t, d_gate_up, (((0,), (0,)), ((), ())), preferred_element_type=jnp.float32
    )
    ffn_in_part = lax.dot_general(
        d_gate_up, gate_up_w, (((1,), (1,)), ((), ())), preferred_element_type=jnp.float32
    )
    d_normed_t = head_sum(ffn_in_part)
    d_middle = grad_out + norm_back(norm_mid, inv_mid, d_normed_t * (1.0 + scale_t))
    d_scale_t = jnp.sum(d_normed_t * norm_mid, axis=0, keepdims=True)
    d_shift_t = jnp.sum(d_normed_t, axis=0, keepdims=True)
    d_attn = d_middle * sig_a
    d_gate_a = jnp.sum(d_middle * attn_branch * sig_a * (1.0 - sig_a), axis=0, keepdims=True)
    d_out_bias = jnp.sum(d_attn, axis=0, keepdims=True)
    d_attn_low = d_attn.astype(jnp.bfloat16)

    out_weight_grad_t = lax.dot_general(
        d_attn_low, mixed, (((0,), (0,)), ((), ())), preferred_element_type=jnp.float32
    )
    d_mixed = head_split(
        lax.dot_general(
            d_attn_low, out_weight, (((1,), (1,)), ((), ())), preferred_element_type=jnp.float32
        ).astype(jnp.bfloat16)
    )
    d_values = jnp.einsum("hqk,qhe->khe", probs_low, d_mixed, preferred_element_type=jnp.float32)
    d_probs = jnp.einsum("qhe,khe->hqk", d_mixed, values, preferred_element_type=jnp.float32)
    d_scores = (
        attn_probs * (d_probs - jnp.sum(d_probs * attn_probs, axis=-1, keepdims=True))
    ).astype(jnp.bfloat16)
    d_queries = jnp.einsum(
        "hqk,khe->qhe", d_scores, keys, preferred_element_type=jnp.float32
    ) * DH ** (-0.5)
    d_keys = jnp.einsum(
        "hqk,qhe->khe", d_scores, queries, preferred_element_type=jnp.float32
    ) * DH ** (-0.5)
    d_qkv = jnp.concatenate(
        [d_queries.reshape(length, proj), d_keys.reshape(length, proj), d_values.reshape(length, proj)],
        axis=1,
    ).astype(jnp.bfloat16)
    qkv_grad = lax.dot_general(
        normed_a, d_qkv, (((0,), (0,)), ((), ())), preferred_element_type=jnp.float32
    )

    packed = lax.optimization_barrier(jnp.zeros((width, 4 * proj + 3 * ffn), jnp.bfloat16))
    packed = lax.dynamic_update_slice(packed, gate_up_grad.astype(jnp.bfloat16), (0, 4 * proj))
    packed = lax.dynamic_update_slice(
        packed, down_grad_t.astype(jnp.bfloat16), (0, 4 * proj + 2 * ffn)
    )
    packed = lax.dynamic_update_slice(packed, out_weight_grad_t.astype(jnp.bfloat16), (0, 3 * proj))
    packed = lax.dynamic_update_slice(packed, qkv_grad.astype(jnp.bfloat16), (0, 0))
    reduced = lax.psum_scatter(packed, "dp", scatter_dimension=0, tiled=True).astype(jnp.float32)

    attn_in_part = lax.dot_general(
        d_qkv, qkv_w, (((1,), (1,)), ((), ())), preferred_element_type=jnp.float32
    ).astype(jnp.bfloat16)
    d_normed_a = attn_in_part.astype(jnp.float32) + swap_heads(attn_in_part).astype(jnp.float32)
    input_grad = own_rows(
        (d_middle + norm_back(norm_in, inv_in, d_normed_a * (1.0 + scale_a)))[None], head, rows
    )
    d_scale_a = jnp.sum(d_normed_a * norm_in, axis=0, keepdims=True)
    d_shift_a = jnp.sum(d_normed_a, axis=0, keepdims=True)
    d_modulation = jnp.concatenate(
        [d_scale_a, d_shift_a, d_gate_a, d_scale_t, d_shift_t, d_gate_t], axis=-1
    )

    d_bias_rows = trade_blocks(d_scores, head, rows, 1, 0)
    d_bias_flat = jnp.pad(d_bias_rows.reshape(heads_all, -1), ((0, HEAD_PAD - heads_all), (0, 0)))
    pair_grad, pair_wg, pair_gg = pair_backward(pair_flat, d_bias_flat, pair_gain_row, pair_wt)
    pair_grad = pair_grad.reshape(pair_input.shape)
    pair_weight_grad = pair_wg[:heads_all].T
    pair_gain_grad = pair_gg[0]

    pair_small = head_sum(
        jnp.concatenate([pair_weight_grad.reshape(-1), pair_gain_grad])[None]
    )
    small = jnp.concatenate([d_modulation, time_cond, d_out_bias], axis=-1)
    small_rows = dp_gather(small)
    mod_size = d_modulation.shape[-1]
    cond_size = time_cond.shape[-1]
    pw_size = pair_weight.size
    mod_chain = small_rows[:, :mod_size]
    cond_chain = small_rows[:, mod_size : mod_size + cond_size]
    out_bias_grad = jnp.sum(small_rows[:, mod_size + cond_size :], axis=0)
    pair_total = dp_sum(pair_small)[0]
    pair_weight_grad = pair_total[:pw_size].reshape(pair_weight.shape)
    pair_gain_grad = pair_total[pw_size:]
    cond_act = lax.optimization_barrier(jax.nn.silu(cond_chain).astype(jnp.bfloat16)).astype(
        jnp.float32
    )
    mod_weight_grad = jnp.dot(cond_act.T, mod_chain, precision=precise)
    mod_bias_grad = jnp.sum(mod_chain, axis=0)
    cond_grad = jnp.dot(
        d_modulation, mod_weight.astype(jnp.float32).T, precision=precise
    ) * silu_slope(time_cond)

    cuts = [0, 3 * proj, 4 * proj, 4 * proj + 2 * ffn, 4 * proj + 3 * ffn]
    pieces = [reduced[:, cuts[i] : cuts[i + 1]] for i in range(4)]
    qkv_grad = pieces[0].reshape(-1, 3, proj)
    out_weight_grad = pieces[1].T
    gate_up_grad = pieces[2].reshape(-1, 2, ffn)
    down_grad = pieces[3].T
    return (
        layer_output,
        input_grad,
        pair_grad,
        cond_grad,
        mod_weight_grad,
        mod_bias_grad,
        qkv_grad,
        pair_gain_grad,
        pair_weight_grad,
        out_weight_grad,
        out_bias_grad,
        gate_up_grad,
        down_grad,
    )


def solution(mesh):
    placed = (
        P("dp", "head", None),
        P("dp", "head", None, None),
        P("dp", None),
        P("dp"),
        P("dp", None),
        P(),
        P(),
        P(None, None, "head"),
        P(),
        P(),
        P("head", None),
        P(),
        P(None, None, "head"),
        P("head", None),
        P("dp", "head", None),
    )
    return jax.shard_map(
        shards,
        mesh=mesh,
        in_specs=placed,
        out_specs=(
            P("dp", "head", None),
            P("dp", "head", None),
            P("dp", "head", None, None),
            P("dp", None),
            P(),
            P(),
            P("dp", None, "head"),
            P(),
            P(),
            P("head", "dp"),
            P(),
            P("dp", None, "head"),
            P("head", "dp"),
        ),
        check_vma=False,
    )
```

```python
import jax
import jax.numpy as jnp
from jax import lax
from jax.experimental import pallas as pl
from jax.experimental.pallas import tpu as pltpu
from jax.sharding import PartitionSpec as P

DH = 64


epsilon = 1e-05
masked_score = -1000000000.0
precise = lax.Precision.HIGHEST
LANES = 128
PAIR_TILE = 4096
PAIR_BACK_TILE = 2048
HEAD_PAD = 16


def blank_kernel(out_ref):
    del out_ref


def blank(shape, dtype):
    return pl.pallas_call(
        blank_kernel,
        out_shape=jax.ShapeDtypeStruct(shape, dtype),
        out_specs=pl.BlockSpec(memory_space=pl.ANY),
    )()


def pair_stats(x):
    centred = x - jnp.mean(x, axis=-1, keepdims=True)
    inv_std = lax.rsqrt(jnp.mean(centred * centred, axis=-1, keepdims=True) + epsilon)
    return centred * inv_std, inv_std


def pair_forward_kernel(x_ref, gain_ref, wt_ref, bias_ref):
    normed, _ = pair_stats(x_ref[...].astype(jnp.float32))
    scaled = (normed * gain_ref[...]).astype(jnp.bfloat16)
    bias = lax.dot_general(
        wt_ref[...], scaled, (((1,), (1,)), ((), ())), preferred_element_type=jnp.float32
    )
    bias_ref[...] = bias[: bias_ref.shape[0]].astype(bias_ref.dtype)


def pair_forward(flat, gain, wt, heads):
    m, width = flat.shape
    tile = min(PAIR_TILE, m)
    return pl.pallas_call(
        pair_forward_kernel,
        grid=(m // tile,),
        in_specs=[
            pl.BlockSpec((tile, width), lambda i: (i, 0)),
            pl.BlockSpec((1, width), lambda i: (0, 0)),
            pl.BlockSpec(wt.shape, lambda i: (0, 0)),
        ],
        out_specs=pl.BlockSpec((heads, tile), lambda i: (0, i)),
        out_shape=jax.ShapeDtypeStruct((heads, m), jnp.bfloat16),
        cost_estimate=pl.CostEstimate(
            flops=m * width * (2 * HEAD_PAD + 10),
            transcendentals=m,
            bytes_accessed=m * width * 2 + heads * m * 2,
        ),
    )(flat, gain, wt)


def pair_backward_kernel(x_ref, ds_ref, gain_ref, wt_ref, grad_ref, wg_ref, gg_ref):
    step = pl.program_id(0)
    normed, inv_std = pair_stats(x_ref[...].astype(jnp.float32))
    gain = gain_ref[...]
    scaled = (normed * gain).astype(jnp.bfloat16)
    ds = ds_ref[...]
    d_scaled = lax.dot_general(
        ds, wt_ref[...], (((0,), (0,)), ((), ())), preferred_element_type=jnp.float32
    )
    wg = lax.dot_general(ds, scaled, (((1,), (0,)), ((), ())), preferred_element_type=jnp.float32)
    gg = jnp.sum(d_scaled * normed, axis=0, keepdims=True)
    d_normed = d_scaled * gain
    mean_grad = jnp.mean(d_normed, axis=-1, keepdims=True)
    mean_proj = jnp.mean(d_normed * normed, axis=-1, keepdims=True)
    grad_ref[...] = (inv_std * (d_normed - mean_grad - normed * mean_proj)).astype(grad_ref.dtype)

    @pl.when(step == 0)
    def _():
        wg_ref[...] = jnp.zeros_like(wg_ref)
        gg_ref[...] = jnp.zeros_like(gg_ref)

    wg_ref[...] += wg
    gg_ref[...] += gg


def pair_backward(flat, ds, gain, wt):
    m, width = flat.shape
    tile = min(PAIR_BACK_TILE, m)
    pad = ds.shape[0]
    return pl.pallas_call(
        pair_backward_kernel,
        grid=(m // tile,),
        in_specs=[
            pl.BlockSpec((tile, width), lambda i: (i, 0)),
            pl.BlockSpec((pad, tile), lambda i: (0, i)),
            pl.BlockSpec((1, width), lambda i: (0, 0)),
            pl.BlockSpec(wt.shape, lambda i: (0, 0)),
        ],
        out_specs=[
            pl.BlockSpec((tile, width), lambda i: (i, 0)),
            pl.BlockSpec((pad, width), lambda i: (0, 0)),
            pl.BlockSpec((1, width), lambda i: (0, 0)),
        ],
        out_shape=[
            jax.ShapeDtypeStruct((m, width), jnp.bfloat16),
            jax.ShapeDtypeStruct((pad, width), jnp.float32),
            jax.ShapeDtypeStruct((1, width), jnp.float32),
        ],
        compiler_params=pltpu.CompilerParams(dimension_semantics=("arbitrary",)),
        cost_estimate=pl.CostEstimate(
            flops=m * width * (4 * HEAD_PAD + 20),
            transcendentals=m,
            bytes_accessed=2 * m * width * 2 + pad * m * 2,
        ),
    )(flat, ds, gain, wt)


def layer_norm(values):
    centred = values - jnp.mean(values, axis=-1, keepdims=True)
    inv_std = lax.rsqrt(jnp.mean(centred * centred, axis=-1, keepdims=True) + epsilon)
    return (centred * inv_std, inv_std)


def norm_back(normed, inv_std, grad):
    mean_grad = jnp.mean(grad, axis=-1, keepdims=True)
    mean_proj = jnp.mean(grad * normed, axis=-1, keepdims=True)
    return inv_std * (grad - mean_grad - normed * mean_proj)


def silu_slope(values):
    sigma = jax.nn.sigmoid(values)
    return sigma * (1.0 + values * (1.0 - sigma))


def head_split(values):
    return values.reshape(values.shape[:-1] + (values.shape[-1] // DH, DH))


def swap_heads(values):
    return lax.ppermute(values, "head", [(0, 1), (1, 0)])


def whole_rows(own, first):
    other = swap_heads(own)
    return jnp.where(
        first,
        jnp.concatenate([own, other], axis=0),
        jnp.concatenate([other, own], axis=0),
    )


def dp_gather(values):
    count = lax.axis_size("dp")
    index = lax.axis_index("dp")
    block = values
    step = 1
    while step < count:
        other = lax.ppermute(block, "dp", [(i, i ^ step) for i in range(count)])
        block = jnp.where(
            (index & step) == 0,
            jnp.concatenate([block, other], axis=0),
            jnp.concatenate([other, block], axis=0),
        )
        step *= 2
    return block


def dp_sum(values):
    count = lax.axis_size("dp")
    index = lax.axis_index("dp")
    step = 1
    while step < count:
        other = lax.ppermute(values, "dp", [(i, i ^ step) for i in range(count)])
        values = jnp.where((index & step) == 0, values + other, other + values)
        step *= 2
    return values


def own_rows(values, head, rows):
    return lax.dynamic_slice_in_dim(values, head * rows, rows, 1)


def head_sum(part):
    return part + swap_heads(part)


def trade_blocks(values, head, size, axis, mine_axis):
    mine = lax.dynamic_slice_in_dim(values, head * size, size, axis)
    theirs = swap_heads(lax.dynamic_slice_in_dim(values, (1 - head) * size, size, axis))
    return jnp.where(
        head == 0,
        jnp.concatenate([mine, theirs], axis=mine_axis),
        jnp.concatenate([theirs, mine], axis=mine_axis),
    )


def attn_scores(queries, keys, biases, valid):
    scores = jnp.einsum("cqhe,ckhe->chqk", queries, keys, preferred_element_type=jnp.float32)
    scores = scores * DH ** (-0.5) + biases.astype(jnp.float32)
    return jnp.where(valid[:, None, None, :], scores, masked_score)


def to_chunks(values, parts):
    return values.reshape(parts, -1, LANES)


def shards(
    layer_input,
    pair_input,
    time_cond,
    chain_lengths,
    residue_mask,
    mod_weight,
    mod_bias,
    qkv_weight,
    pair_gain,
    pair_weight,
    out_weight,
    out_bias,
    gate_up_weight,
    down_weight,
    output_grad,
):
    assert layer_input.shape[0] == 1
    rows = layer_input.shape[1]
    width = layer_input.shape[2]
    length = residue_mask.shape[1]
    head = lax.axis_index("head")
    first = head == 0
    data_count = lax.axis_size("dp")
    proj = qkv_weight.shape[2]
    ffn = gate_up_weight.shape[2]
    qkv_w = qkv_weight.reshape(width, 3 * proj)
    gate_up_w = gate_up_weight.reshape(width, 2 * ffn)

    x_rows = whole_rows(layer_input[0], first)
    g_rows = whole_rows(output_grad[0], first)
    out_weight_all = whole_rows(out_weight, first)

    positions = jnp.arange(length, dtype=jnp.int32)
    valid = (positions < chain_lengths[0]) & ((residue_mask[0] == 1) | (positions == 0))
    silu_cond = jax.nn.silu(time_cond).astype(jnp.bfloat16)
    modulation = jnp.dot(silu_cond, mod_weight, preferred_element_type=jnp.float32) + mod_bias
    scale_a, shift_a, gate_a, scale_t, shift_t, gate_t = [
        modulation[:, section * width : (section + 1) * width] for section in range(6)
    ]

    heads_all = pair_weight.shape[1]
    pair_width = pair_input.shape[-1]
    pair_flat = pair_input.reshape(-1, pair_width)
    pair_wt = jnp.pad(pair_weight.T, ((0, HEAD_PAD - heads_all), (0, 0)))
    pair_gain_row = pair_gain.reshape(1, pair_width)
    bias_flat = pair_forward(pair_flat, pair_gain_row, pair_wt, heads_all)
    bias_rows = bias_flat.reshape(heads_all, rows, length)
    heads_own = proj // DH
    biases = trade_blocks(bias_rows, head, heads_own, 0, 1)

    residues = x_rows.astype(jnp.float32)
    norm_in, inv_in = layer_norm(residues)
    normed_a = (norm_in * (1.0 + scale_a) + shift_a).astype(jnp.bfloat16)
    projected = jnp.dot(normed_a, qkv_w, preferred_element_type=jnp.float32).astype(jnp.bfloat16)
    queries = head_split(projected[:, :proj])
    keys = head_split(projected[:, proj : 2 * proj])
    values = head_split(projected[:, 2 * proj :])
    scores = jnp.einsum("qhe,khe->hqk", queries, keys, preferred_element_type=jnp.float32)
    scores = scores * DH ** (-0.5) + biases.astype(jnp.float32)
    scores = jnp.where(valid[None, None, :], scores, masked_score)
    row_max = jnp.max(scores, axis=-1, keepdims=True)
    exp_scores = jnp.exp(scores - row_max)
    row_total = jnp.sum(exp_scores, axis=-1, keepdims=True)
    attn_probs = exp_scores / row_total
    probs_low = attn_probs.astype(jnp.bfloat16)
    mixed = jnp.einsum("hqk,khe->qhe", probs_low, values, preferred_element_type=jnp.float32)
    mixed = mixed.reshape(length, proj).astype(jnp.bfloat16)
    mixed_all = jnp.where(
        first,
        jnp.concatenate([mixed, swap_heads(mixed)], axis=1),
        jnp.concatenate([swap_heads(mixed), mixed], axis=1),
    )
    attn_branch = jnp.dot(mixed_all, out_weight_all, preferred_element_type=jnp.float32) + out_bias
    sig_a = jax.nn.sigmoid(gate_a)
    middle = residues + sig_a * attn_branch

    norm_mid, inv_mid = layer_norm(middle)
    normed_t = (norm_mid * (1.0 + scale_t) + shift_t).astype(jnp.bfloat16)
    gate_up = jnp.dot(normed_t, gate_up_w, preferred_element_type=jnp.float32)
    gate_pre = gate_up[:, :ffn]
    up_pre = gate_up[:, ffn:]
    hidden = (jax.nn.silu(gate_pre) * up_pre).astype(jnp.bfloat16)
    ffn_part = jnp.dot(hidden, down_weight, preferred_element_type=jnp.float32).astype(jnp.bfloat16)
    ffn_branch = ffn_part.astype(jnp.float32) + swap_heads(ffn_part).astype(jnp.float32)
    sig_t = jax.nn.sigmoid(gate_t)
    layer_output = own_rows((middle + sig_t * ffn_branch).astype(jnp.bfloat16)[None], head, rows)

    grad_out = g_rows.astype(jnp.float32)
    d_ffn = (grad_out * sig_t).astype(jnp.bfloat16)
    d_gate_t = jnp.sum(grad_out * ffn_branch * sig_t * (1.0 - sig_t), axis=0, keepdims=True)
    down_grad_t = lax.dot_general(
        d_ffn, hidden, (((0,), (0,)), ((), ())), preferred_element_type=jnp.float32
    )
    d_hidden = lax.dot_general(
        d_ffn, down_weight, (((1,), (1,)), ((), ())), preferred_element_type=jnp.float32
    )
    d_gate = d_hidden * up_pre * silu_slope(gate_pre)
    d_up = d_hidden * jax.nn.silu(gate_pre)
    d_gate_up = jnp.concatenate([d_gate, d_up], axis=1).astype(jnp.bfloat16)
    gate_up_grad = lax.dot_general(
        normed_t, d_gate_up, (((0,), (0,)), ((), ())), preferred_element_type=jnp.float32
    )
    ffn_in_part = lax.dot_general(
        d_gate_up, gate_up_w, (((1,), (1,)), ((), ())), preferred_element_type=jnp.float32
    )
    d_normed_t = head_sum(ffn_in_part)
    d_middle = grad_out + norm_back(norm_mid, inv_mid, d_normed_t * (1.0 + scale_t))
    d_scale_t = jnp.sum(d_normed_t * norm_mid, axis=0, keepdims=True)
    d_shift_t = jnp.sum(d_normed_t, axis=0, keepdims=True)
    d_attn = d_middle * sig_a
    d_gate_a = jnp.sum(d_middle * attn_branch * sig_a * (1.0 - sig_a), axis=0, keepdims=True)
    d_out_bias = jnp.sum(d_attn, axis=0, keepdims=True)
    d_attn_low = d_attn.astype(jnp.bfloat16)

    out_weight_grad_t = lax.dot_general(
        d_attn_low, mixed, (((0,), (0,)), ((), ())), preferred_element_type=jnp.float32
    )
    d_mixed = head_split(
        lax.dot_general(
            d_attn_low, out_weight, (((1,), (1,)), ((), ())), preferred_element_type=jnp.float32
        ).astype(jnp.bfloat16)
    )
    d_values = jnp.einsum("hqk,qhe->khe", probs_low, d_mixed, preferred_element_type=jnp.float32)
    d_probs = jnp.einsum("qhe,khe->hqk", d_mixed, values, preferred_element_type=jnp.float32)
    d_scores = (
        attn_probs * (d_probs - jnp.sum(d_probs * attn_probs, axis=-1, keepdims=True))
    ).astype(jnp.bfloat16)
    d_queries = jnp.einsum(
        "hqk,khe->qhe", d_scores, keys, preferred_element_type=jnp.float32
    ) * DH ** (-0.5)
    d_keys = jnp.einsum(
        "hqk,qhe->khe", d_scores, queries, preferred_element_type=jnp.float32
    ) * DH ** (-0.5)
    d_qkv = jnp.concatenate(
        [d_queries.reshape(length, proj), d_keys.reshape(length, proj), d_values.reshape(length, proj)],
        axis=1,
    ).astype(jnp.bfloat16)
    qkv_grad = lax.dot_general(
        normed_a, d_qkv, (((0,), (0,)), ((), ())), preferred_element_type=jnp.float32
    )

    packed = blank((width, 4 * proj + 3 * ffn), jnp.bfloat16)
    packed = lax.dynamic_update_slice(packed, gate_up_grad.astype(jnp.bfloat16), (0, 4 * proj))
    packed = lax.dynamic_update_slice(
        packed, down_grad_t.astype(jnp.bfloat16), (0, 4 * proj + 2 * ffn)
    )
    packed = lax.dynamic_update_slice(packed, out_weight_grad_t.astype(jnp.bfloat16), (0, 3 * proj))
    packed = lax.dynamic_update_slice(packed, qkv_grad.astype(jnp.bfloat16), (0, 0))
    reduced = lax.psum_scatter(packed, "dp", scatter_dimension=0, tiled=True).astype(jnp.float32)

    attn_in_part = lax.dot_general(
        d_qkv, qkv_w, (((1,), (1,)), ((), ())), preferred_element_type=jnp.float32
    ).astype(jnp.bfloat16)
    d_normed_a = attn_in_part.astype(jnp.float32) + swap_heads(attn_in_part).astype(jnp.float32)
    input_grad = own_rows(
        (d_middle + norm_back(norm_in, inv_in, d_normed_a * (1.0 + scale_a)))[None], head, rows
    )
    d_scale_a = jnp.sum(d_normed_a * norm_in, axis=0, keepdims=True)
    d_shift_a = jnp.sum(d_normed_a, axis=0, keepdims=True)
    d_modulation = jnp.concatenate(
        [d_scale_a, d_shift_a, d_gate_a, d_scale_t, d_shift_t, d_gate_t], axis=-1
    )

    d_bias_rows = trade_blocks(d_scores, head, rows, 1, 0)
    d_bias_flat = jnp.pad(d_bias_rows.reshape(heads_all, -1), ((0, HEAD_PAD - heads_all), (0, 0)))
    pair_grad, pair_wg, pair_gg = pair_backward(pair_flat, d_bias_flat, pair_gain_row, pair_wt)
    pair_grad = pair_grad.reshape(pair_input.shape)
    pair_weight_grad = pair_wg[:heads_all].T
    pair_gain_grad = pair_gg[0]

    pair_small = head_sum(
        jnp.concatenate([pair_weight_grad.reshape(-1), pair_gain_grad])[None]
    )
    small = jnp.concatenate([d_modulation, time_cond, d_out_bias], axis=-1)
    small_rows = dp_gather(small)
    mod_size = d_modulation.shape[-1]
    cond_size = time_cond.shape[-1]
    pw_size = pair_weight.size
    mod_chain = small_rows[:, :mod_size]
    cond_chain = small_rows[:, mod_size : mod_size + cond_size]
    out_bias_grad = jnp.sum(small_rows[:, mod_size + cond_size :], axis=0)
    pair_total = dp_sum(pair_small)[0]
    pair_weight_grad = pair_total[:pw_size].reshape(pair_weight.shape)
    pair_gain_grad = pair_total[pw_size:]
    cond_act = lax.optimization_barrier(jax.nn.silu(cond_chain).astype(jnp.bfloat16)).astype(
        jnp.float32
    )
    mod_weight_grad = jnp.dot(cond_act.T, mod_chain, precision=precise)
    mod_bias_grad = jnp.sum(mod_chain, axis=0)
    cond_grad = jnp.dot(
        d_modulation, mod_weight.astype(jnp.float32).T, precision=precise
    ) * silu_slope(time_cond)

    cuts = [0, 3 * proj, 4 * proj, 4 * proj + 2 * ffn, 4 * proj + 3 * ffn]
    pieces = [reduced[:, cuts[i] : cuts[i + 1]] for i in range(4)]
    qkv_grad = pieces[0].reshape(-1, 3, proj)
    out_weight_grad = pieces[1].T
    gate_up_grad = pieces[2].reshape(-1, 2, ffn)
    down_grad = pieces[3].T
    return (
        layer_output,
        input_grad,
        pair_grad,
        cond_grad,
        mod_weight_grad,
        mod_bias_grad,
        qkv_grad,
        pair_gain_grad,
        pair_weight_grad,
        out_weight_grad,
        out_bias_grad,
        gate_up_grad,
        down_grad,
    )


def solution(mesh):
    placed = (
        P("dp", "head", None),
        P("dp", "head", None, None),
        P("dp", None),
        P("dp"),
        P("dp", None),
        P(),
        P(),
        P(None, None, "head"),
        P(),
        P(),
        P("head", None),
        P(),
        P(None, None, "head"),
        P("head", None),
        P("dp", "head", None),
    )
    return jax.shard_map(
        shards,
        mesh=mesh,
        in_specs=placed,
        out_specs=(
            P("dp", "head", None),
            P("dp", "head", None),
            P("dp", "head", None, None),
            P("dp", None),
            P(),
            P(),
            P("dp", None, "head"),
            P(),
            P(),
            P("head", "dp"),
            P(),
            P("dp", None, "head"),
            P("head", "dp"),
        ),
        check_vma=False,
    )
```

```python
import jax
import jax.numpy as jnp
from jax import lax
from jax.experimental import pallas as pl
from jax.experimental.pallas import tpu as pltpu
from jax.sharding import PartitionSpec as P

DH = 64


epsilon = 1e-05
masked_score = -1000000000.0
precise = lax.Precision.HIGHEST
LANES = 128
PAIR_TILE = 4096
PAIR_BACK_TILE = 2048
HEAD_PAD = 16


def pair_stats(x):
    centred = x - jnp.mean(x, axis=-1, keepdims=True)
    inv_std = lax.rsqrt(jnp.mean(centred * centred, axis=-1, keepdims=True) + epsilon)
    return centred * inv_std, inv_std


def pair_forward_kernel(x_ref, gain_ref, wt_ref, bias_ref):
    normed, _ = pair_stats(x_ref[...].astype(jnp.float32))
    scaled = (normed * gain_ref[...]).astype(jnp.bfloat16)
    bias = lax.dot_general(
        wt_ref[...], scaled, (((1,), (1,)), ((), ())), preferred_element_type=jnp.float32
    )
    bias_ref[...] = bias[: bias_ref.shape[0]].astype(bias_ref.dtype)


def pair_forward(flat, gain, wt, heads):
    m, width = flat.shape
    tile = min(PAIR_TILE, m)
    return pl.pallas_call(
        pair_forward_kernel,
        grid=(m // tile,),
        in_specs=[
            pl.BlockSpec((tile, width), lambda i: (i, 0)),
            pl.BlockSpec((1, width), lambda i: (0, 0)),
            pl.BlockSpec(wt.shape, lambda i: (0, 0)),
        ],
        out_specs=pl.BlockSpec((heads, tile), lambda i: (0, i)),
        out_shape=jax.ShapeDtypeStruct((heads, m), jnp.bfloat16),
        cost_estimate=pl.CostEstimate(
            flops=m * width * (2 * HEAD_PAD + 10),
            transcendentals=m,
            bytes_accessed=m * width * 2 + heads * m * 2,
        ),
    )(flat, gain, wt)


def pair_backward_kernel(x_ref, ds_ref, gain_ref, wt_ref, grad_ref, wg_ref, gg_ref):
    step = pl.program_id(0)
    normed, inv_std = pair_stats(x_ref[...].astype(jnp.float32))
    gain = gain_ref[...]
    scaled = (normed * gain).astype(jnp.bfloat16)
    ds = ds_ref[...]
    d_scaled = lax.dot_general(
        ds, wt_ref[...], (((0,), (0,)), ((), ())), preferred_element_type=jnp.float32
    )
    wg = lax.dot_general(ds, scaled, (((1,), (0,)), ((), ())), preferred_element_type=jnp.float32)
    gg = jnp.sum(d_scaled * normed, axis=0, keepdims=True)
    d_normed = d_scaled * gain
    mean_grad = jnp.mean(d_normed, axis=-1, keepdims=True)
    mean_proj = jnp.mean(d_normed * normed, axis=-1, keepdims=True)
    grad_ref[...] = (inv_std * (d_normed - mean_grad - normed * mean_proj)).astype(grad_ref.dtype)

    @pl.when(step == 0)
    def _():
        wg_ref[...] = jnp.zeros_like(wg_ref)
        gg_ref[...] = jnp.zeros_like(gg_ref)

    wg_ref[...] += wg
    gg_ref[...] += gg


def pair_backward(flat, ds, gain, wt):
    m, width = flat.shape
    tile = min(PAIR_BACK_TILE, m)
    pad = ds.shape[0]
    return pl.pallas_call(
        pair_backward_kernel,
        grid=(m // tile,),
        in_specs=[
            pl.BlockSpec((tile, width), lambda i: (i, 0)),
            pl.BlockSpec((pad, tile), lambda i: (0, i)),
            pl.BlockSpec((1, width), lambda i: (0, 0)),
            pl.BlockSpec(wt.shape, lambda i: (0, 0)),
        ],
        out_specs=[
            pl.BlockSpec((tile, width), lambda i: (i, 0)),
            pl.BlockSpec((pad, width), lambda i: (0, 0)),
            pl.BlockSpec((1, width), lambda i: (0, 0)),
        ],
        out_shape=[
            jax.ShapeDtypeStruct((m, width), jnp.bfloat16),
            jax.ShapeDtypeStruct((pad, width), jnp.float32),
            jax.ShapeDtypeStruct((1, width), jnp.float32),
        ],
        compiler_params=pltpu.CompilerParams(dimension_semantics=("arbitrary",)),
        cost_estimate=pl.CostEstimate(
            flops=m * width * (4 * HEAD_PAD + 20),
            transcendentals=m,
            bytes_accessed=2 * m * width * 2 + pad * m * 2,
        ),
    )(flat, ds, gain, wt)


def layer_norm(values):
    centred = values - jnp.mean(values, axis=-1, keepdims=True)
    inv_std = lax.rsqrt(jnp.mean(centred * centred, axis=-1, keepdims=True) + epsilon)
    return (centred * inv_std, inv_std)


def norm_back(normed, inv_std, grad):
    mean_grad = jnp.mean(grad, axis=-1, keepdims=True)
    mean_proj = jnp.mean(grad * normed, axis=-1, keepdims=True)
    return inv_std * (grad - mean_grad - normed * mean_proj)


def silu_slope(values):
    sigma = jax.nn.sigmoid(values)
    return sigma * (1.0 + values * (1.0 - sigma))


def head_split(values):
    return values.reshape(values.shape[:-1] + (values.shape[-1] // DH, DH))


def swap_heads(values):
    return lax.ppermute(values, "head", [(0, 1), (1, 0)])


def whole_rows(own, first):
    other = swap_heads(own)
    return jnp.where(
        first,
        jnp.concatenate([own, other], axis=0),
        jnp.concatenate([other, own], axis=0),
    )


def dp_gather(values):
    count = lax.axis_size("dp")
    index = lax.axis_index("dp")
    block = values
    step = 1
    while step < count:
        other = lax.ppermute(block, "dp", [(i, i ^ step) for i in range(count)])
        block = jnp.where(
            (index & step) == 0,
            jnp.concatenate([block, other], axis=0),
            jnp.concatenate([other, block], axis=0),
        )
        step *= 2
    return block


def dp_sum(values):
    count = lax.axis_size("dp")
    index = lax.axis_index("dp")
    step = 1
    while step < count:
        other = lax.ppermute(values, "dp", [(i, i ^ step) for i in range(count)])
        values = jnp.where((index & step) == 0, values + other, other + values)
        step *= 2
    return values


def own_rows(values, head, rows):
    return lax.dynamic_slice_in_dim(values, head * rows, rows, 1)


def head_sum(part):
    return part + swap_heads(part)


def trade_blocks(values, head, size, axis, mine_axis):
    mine = lax.dynamic_slice_in_dim(values, head * size, size, axis)
    theirs = swap_heads(lax.dynamic_slice_in_dim(values, (1 - head) * size, size, axis))
    return jnp.where(
        head == 0,
        jnp.concatenate([mine, theirs], axis=mine_axis),
        jnp.concatenate([theirs, mine], axis=mine_axis),
    )


def attn_scores(queries, keys, biases, valid):
    scores = jnp.einsum("cqhe,ckhe->chqk", queries, keys, preferred_element_type=jnp.float32)
    scores = scores * DH ** (-0.5) + biases.astype(jnp.float32)
    return jnp.where(valid[:, None, None, :], scores, masked_score)


def to_chunks(values, parts):
    return values.reshape(parts, -1, LANES)


def shards(
    layer_input,
    pair_input,
    time_cond,
    chain_lengths,
    residue_mask,
    mod_weight,
    mod_bias,
    qkv_weight,
    pair_gain,
    pair_weight,
    out_weight,
    out_bias,
    gate_up_weight,
    down_weight,
    output_grad,
):
    assert layer_input.shape[0] == 1
    rows = layer_input.shape[1]
    width = layer_input.shape[2]
    length = residue_mask.shape[1]
    head = lax.axis_index("head")
    first = head == 0
    data_count = lax.axis_size("dp")
    proj = qkv_weight.shape[2]
    ffn = gate_up_weight.shape[2]
    qkv_w = qkv_weight.reshape(width, 3 * proj)
    gate_up_w = gate_up_weight.reshape(width, 2 * ffn)

    x_rows = whole_rows(layer_input[0], first)
    g_rows = whole_rows(output_grad[0], first)
    out_weight_all = whole_rows(out_weight, first)

    positions = jnp.arange(length, dtype=jnp.int32)
    valid = (positions < chain_lengths[0]) & ((residue_mask[0] == 1) | (positions == 0))
    silu_cond = jax.nn.silu(time_cond).astype(jnp.bfloat16)
    modulation = jnp.dot(silu_cond, mod_weight, preferred_element_type=jnp.float32) + mod_bias
    scale_a, shift_a, gate_a, scale_t, shift_t, gate_t = [
        modulation[:, section * width : (section + 1) * width] for section in range(6)
    ]

    heads_all = pair_weight.shape[1]
    pair_width = pair_input.shape[-1]
    pair_flat = pair_input.reshape(-1, pair_width)
    pair_wt = jnp.pad(pair_weight.T, ((0, HEAD_PAD - heads_all), (0, 0)))
    pair_gain_row = pair_gain.reshape(1, pair_width)
    bias_flat = pair_forward(pair_flat, pair_gain_row, pair_wt, heads_all)
    bias_rows = bias_flat.reshape(heads_all, rows, length)
    heads_own = proj // DH
    biases = trade_blocks(bias_rows, head, heads_own, 0, 1)

    residues = x_rows.astype(jnp.float32)
    norm_in, inv_in = layer_norm(residues)
    normed_a = (norm_in * (1.0 + scale_a) + shift_a).astype(jnp.bfloat16)
    projected = jnp.dot(normed_a, qkv_w, preferred_element_type=jnp.float32).astype(jnp.bfloat16)
    queries = head_split(projected[:, :proj])
    keys = head_split(projected[:, proj : 2 * proj])
    values = head_split(projected[:, 2 * proj :])
    scores = jnp.einsum("qhe,khe->hqk", queries, keys, preferred_element_type=jnp.float32)
    scores = scores * DH ** (-0.5) + biases.astype(jnp.float32)
    scores = jnp.where(valid[None, None, :], scores, masked_score)
    row_max = jnp.max(scores, axis=-1, keepdims=True)
    exp_scores = jnp.exp(scores - row_max)
    row_total = jnp.sum(exp_scores, axis=-1, keepdims=True)
    attn_probs = exp_scores / row_total
    probs_low = attn_probs.astype(jnp.bfloat16)
    mixed = jnp.einsum("hqk,khe->qhe", probs_low, values, preferred_element_type=jnp.float32)
    mixed = mixed.reshape(length, proj).astype(jnp.bfloat16)
    mixed_all = jnp.where(
        first,
        jnp.concatenate([mixed, swap_heads(mixed)], axis=1),
        jnp.concatenate([swap_heads(mixed), mixed], axis=1),
    )
    attn_branch = jnp.dot(mixed_all, out_weight_all, preferred_element_type=jnp.float32) + out_bias
    sig_a = jax.nn.sigmoid(gate_a)
    middle = residues + sig_a * attn_branch

    norm_mid, inv_mid = layer_norm(middle)
    normed_t = (norm_mid * (1.0 + scale_t) + shift_t).astype(jnp.bfloat16)
    gate_up = jnp.dot(normed_t, gate_up_w, preferred_element_type=jnp.float32)
    gate_pre = gate_up[:, :ffn]
    up_pre = gate_up[:, ffn:]
    hidden = (jax.nn.silu(gate_pre) * up_pre).astype(jnp.bfloat16)
    ffn_part = jnp.dot(hidden, down_weight, preferred_element_type=jnp.float32).astype(jnp.bfloat16)
    ffn_branch = ffn_part.astype(jnp.float32) + swap_heads(ffn_part).astype(jnp.float32)
    sig_t = jax.nn.sigmoid(gate_t)
    layer_output = own_rows((middle + sig_t * ffn_branch).astype(jnp.bfloat16)[None], head, rows)

    grad_out = g_rows.astype(jnp.float32)
    d_ffn = (grad_out * sig_t).astype(jnp.bfloat16)
    d_gate_t = jnp.sum(grad_out * ffn_branch * sig_t * (1.0 - sig_t), axis=0, keepdims=True)
    down_grad_t = lax.dot_general(
        d_ffn, hidden, (((0,), (0,)), ((), ())), preferred_element_type=jnp.float32
    )
    d_hidden = lax.dot_general(
        d_ffn, down_weight, (((1,), (1,)), ((), ())), preferred_element_type=jnp.float32
    )
    d_gate = d_hidden * up_pre * silu_slope(gate_pre)
    d_up = d_hidden * jax.nn.silu(gate_pre)
    d_gate_up = jnp.concatenate([d_gate, d_up], axis=1).astype(jnp.bfloat16)
    gate_up_grad = lax.dot_general(
        normed_t, d_gate_up, (((0,), (0,)), ((), ())), preferred_element_type=jnp.float32
    )
    ffn_in_part = lax.dot_general(
        d_gate_up, gate_up_w, (((1,), (1,)), ((), ())), preferred_element_type=jnp.float32
    )
    d_normed_t = head_sum(ffn_in_part)
    d_middle = grad_out + norm_back(norm_mid, inv_mid, d_normed_t * (1.0 + scale_t))
    d_scale_t = jnp.sum(d_normed_t * norm_mid, axis=0, keepdims=True)
    d_shift_t = jnp.sum(d_normed_t, axis=0, keepdims=True)
    d_attn = d_middle * sig_a
    d_gate_a = jnp.sum(d_middle * attn_branch * sig_a * (1.0 - sig_a), axis=0, keepdims=True)
    d_out_bias = jnp.sum(d_attn, axis=0, keepdims=True)
    d_attn_low = d_attn.astype(jnp.bfloat16)

    out_weight_grad_t = lax.dot_general(
        d_attn_low, mixed, (((0,), (0,)), ((), ())), preferred_element_type=jnp.float32
    )
    d_mixed = head_split(
        lax.dot_general(
            d_attn_low, out_weight, (((1,), (1,)), ((), ())), preferred_element_type=jnp.float32
        ).astype(jnp.bfloat16)
    )
    d_values = jnp.einsum("hqk,qhe->khe", probs_low, d_mixed, preferred_element_type=jnp.float32)
    d_probs = jnp.einsum("qhe,khe->hqk", d_mixed, values, preferred_element_type=jnp.float32)
    d_scores = (
        attn_probs * (d_probs - jnp.sum(d_probs * attn_probs, axis=-1, keepdims=True))
    ).astype(jnp.bfloat16)
    d_queries = jnp.einsum(
        "hqk,khe->qhe", d_scores, keys, preferred_element_type=jnp.float32
    ) * DH ** (-0.5)
    d_keys = jnp.einsum(
        "hqk,qhe->khe", d_scores, queries, preferred_element_type=jnp.float32
    ) * DH ** (-0.5)
    d_qkv = jnp.concatenate(
        [d_queries.reshape(length, proj), d_keys.reshape(length, proj), d_values.reshape(length, proj)],
        axis=1,
    ).astype(jnp.bfloat16)
    qkv_grad = lax.dot_general(
        normed_a, d_qkv, (((0,), (0,)), ((), ())), preferred_element_type=jnp.float32
    )

    packed = lax.optimization_barrier(jnp.zeros((width, 4 * proj + 3 * ffn), jnp.bfloat16))
    packed = lax.dynamic_update_slice(packed, gate_up_grad.astype(jnp.bfloat16), (0, 4 * proj))
    packed = lax.dynamic_update_slice(
        packed, down_grad_t.astype(jnp.bfloat16), (0, 4 * proj + 2 * ffn)
    )
    packed = lax.dynamic_update_slice(packed, out_weight_grad_t.astype(jnp.bfloat16), (0, 3 * proj))
    packed = lax.dynamic_update_slice(packed, qkv_grad.astype(jnp.bfloat16), (0, 0))
    reduced = lax.psum_scatter(packed, "dp", scatter_dimension=0, tiled=True).astype(jnp.float32)

    attn_in_part = lax.dot_general(
        d_qkv, qkv_w, (((1,), (1,)), ((), ())), preferred_element_type=jnp.float32
    ).astype(jnp.bfloat16)
    d_normed_a = attn_in_part.astype(jnp.float32) + swap_heads(attn_in_part).astype(jnp.float32)
    input_grad = own_rows(
        (d_middle + norm_back(norm_in, inv_in, d_normed_a * (1.0 + scale_a)))[None], head, rows
    )
    d_scale_a = jnp.sum(d_normed_a * norm_in, axis=0, keepdims=True)
    d_shift_a = jnp.sum(d_normed_a, axis=0, keepdims=True)
    d_modulation = jnp.concatenate(
        [d_scale_a, d_shift_a, d_gate_a, d_scale_t, d_shift_t, d_gate_t], axis=-1
    )

    d_bias_rows = trade_blocks(d_scores, head, rows, 1, 0)
    d_bias_flat = jnp.pad(d_bias_rows.reshape(heads_all, -1), ((0, HEAD_PAD - heads_all), (0, 0)))
    pair_grad, pair_wg, pair_gg = pair_backward(pair_flat, d_bias_flat, pair_gain_row, pair_wt)
    pair_grad = pair_grad.reshape(pair_input.shape)
    pair_weight_grad = pair_wg[:heads_all].T
    pair_gain_grad = pair_gg[0]

    pair_small = head_sum(
        jnp.concatenate([pair_weight_grad.reshape(-1), pair_gain_grad])[None]
    )
    small = jnp.concatenate([d_modulation, time_cond, pair_small, d_out_bias], axis=-1)
    small_rows = dp_gather(small)
    mod_size = d_modulation.shape[-1]
    cond_size = time_cond.shape[-1]
    pw_size = pair_weight.size
    pg_size = pair_gain.size
    mod_chain = small_rows[:, :mod_size]
    cond_chain = small_rows[:, mod_size : mod_size + cond_size]
    rest = jnp.sum(small_rows[:, mod_size + cond_size :], axis=0)
    pair_weight_grad = rest[:pw_size].reshape(pair_weight.shape)
    pair_gain_grad = rest[pw_size : pw_size + pg_size]
    out_bias_grad = rest[pw_size + pg_size :]
    cond_act = lax.optimization_barrier(jax.nn.silu(cond_chain).astype(jnp.bfloat16)).astype(
        jnp.float32
    )
    mod_weight_grad = jnp.dot(cond_act.T, mod_chain, precision=precise)
    mod_bias_grad = jnp.sum(mod_chain, axis=0)
    cond_grad = jnp.dot(
        d_modulation, mod_weight.astype(jnp.float32).T, precision=precise
    ) * silu_slope(time_cond)

    cuts = [0, 3 * proj, 4 * proj, 4 * proj + 2 * ffn, 4 * proj + 3 * ffn]
    pieces = [reduced[:, cuts[i] : cuts[i + 1]] for i in range(4)]
    qkv_grad = pieces[0].reshape(-1, 3, proj)
    out_weight_grad = pieces[1].T
    gate_up_grad = pieces[2].reshape(-1, 2, ffn)
    down_grad = pieces[3].T
    return (
        layer_output,
        input_grad,
        pair_grad,
        cond_grad,
        mod_weight_grad,
        mod_bias_grad,
        qkv_grad,
        pair_gain_grad,
        pair_weight_grad,
        out_weight_grad,
        out_bias_grad,
        gate_up_grad,
        down_grad,
    )


def solution(mesh):
    placed = (
        P("dp", "head", None),
        P("dp", "head", None, None),
        P("dp", None),
        P("dp"),
        P("dp", None),
        P(),
        P(),
        P(None, None, "head"),
        P(),
        P(),
        P("head", None),
        P(),
        P(None, None, "head"),
        P("head", None),
        P("dp", "head", None),
    )
    return jax.shard_map(
        shards,
        mesh=mesh,
        in_specs=placed,
        out_specs=(
            P("dp", "head", None),
            P("dp", "head", None),
            P("dp", "head", None, None),
            P("dp", None),
            P(),
            P(),
            P("dp", None, "head"),
            P(),
            P(),
            P("head", "dp"),
            P(),
            P("dp", None, "head"),
            P("head", "dp"),
        ),
        check_vma=False,
    )
```

```python
import jax
import jax.numpy as jnp
from jax import lax
from jax.experimental import pallas as pl
from jax.experimental.pallas import tpu as pltpu
from jax.sharding import PartitionSpec as P

DH = 64


epsilon = 1e-05
masked_score = -1000000000.0
precise = lax.Precision.HIGHEST
LANES = 128
PAIR_TILE = 4096
PAIR_BACK_TILE = 2048
HEAD_PAD = 16


def pair_stats(x):
    centred = x - jnp.mean(x, axis=-1, keepdims=True)
    inv_std = lax.rsqrt(jnp.mean(centred * centred, axis=-1, keepdims=True) + epsilon)
    return centred * inv_std, inv_std


def pair_forward_kernel(x_ref, gain_ref, wt_ref, bias_ref):
    normed, _ = pair_stats(x_ref[...].astype(jnp.float32))
    scaled = (normed * gain_ref[...]).astype(jnp.bfloat16)
    bias = lax.dot_general(
        wt_ref[...], scaled, (((1,), (1,)), ((), ())), preferred_element_type=jnp.float32
    )
    bias_ref[...] = bias[: bias_ref.shape[0]].astype(bias_ref.dtype)


def pair_forward(flat, gain, wt, heads):
    m, width = flat.shape
    tile = min(PAIR_TILE, m)
    return pl.pallas_call(
        pair_forward_kernel,
        grid=(m // tile,),
        in_specs=[
            pl.BlockSpec((tile, width), lambda i: (i, 0)),
            pl.BlockSpec((1, width), lambda i: (0, 0)),
            pl.BlockSpec(wt.shape, lambda i: (0, 0)),
        ],
        out_specs=pl.BlockSpec((heads, tile), lambda i: (0, i)),
        out_shape=jax.ShapeDtypeStruct((heads, m), jnp.bfloat16),
        cost_estimate=pl.CostEstimate(
            flops=m * width * (2 * HEAD_PAD + 10),
            transcendentals=m,
            bytes_accessed=m * width * 2 + heads * m * 2,
        ),
    )(flat, gain, wt)


def pair_backward_kernel(x_ref, ds_ref, gain_ref, wt_ref, grad_ref, wg_ref, gg_ref):
    step = pl.program_id(0)
    normed, inv_std = pair_stats(x_ref[...].astype(jnp.float32))
    gain = gain_ref[...]
    scaled = (normed * gain).astype(jnp.bfloat16)
    ds = ds_ref[...]
    d_scaled = lax.dot_general(
        ds, wt_ref[...], (((0,), (0,)), ((), ())), preferred_element_type=jnp.float32
    )
    wg = lax.dot_general(ds, scaled, (((1,), (0,)), ((), ())), preferred_element_type=jnp.float32)
    gg = jnp.sum(d_scaled * normed, axis=0, keepdims=True)
    d_normed = d_scaled * gain
    mean_grad = jnp.mean(d_normed, axis=-1, keepdims=True)
    mean_proj = jnp.mean(d_normed * normed, axis=-1, keepdims=True)
    grad_ref[...] = (inv_std * (d_normed - mean_grad - normed * mean_proj)).astype(grad_ref.dtype)

    @pl.when(step == 0)
    def _():
        wg_ref[...] = jnp.zeros_like(wg_ref)
        gg_ref[...] = jnp.zeros_like(gg_ref)

    wg_ref[...] += wg
    gg_ref[...] += gg


def pair_backward(flat, ds, gain, wt):
    m, width = flat.shape
    tile = min(PAIR_BACK_TILE, m)
    pad = ds.shape[0]
    return pl.pallas_call(
        pair_backward_kernel,
        grid=(m // tile,),
        in_specs=[
            pl.BlockSpec((tile, width), lambda i: (i, 0)),
            pl.BlockSpec((pad, tile), lambda i: (0, i)),
            pl.BlockSpec((1, width), lambda i: (0, 0)),
            pl.BlockSpec(wt.shape, lambda i: (0, 0)),
        ],
        out_specs=[
            pl.BlockSpec((tile, width), lambda i: (i, 0)),
            pl.BlockSpec((pad, width), lambda i: (0, 0)),
            pl.BlockSpec((1, width), lambda i: (0, 0)),
        ],
        out_shape=[
            jax.ShapeDtypeStruct((m, width), jnp.bfloat16),
            jax.ShapeDtypeStruct((pad, width), jnp.float32),
            jax.ShapeDtypeStruct((1, width), jnp.float32),
        ],
        compiler_params=pltpu.CompilerParams(dimension_semantics=("arbitrary",)),
        cost_estimate=pl.CostEstimate(
            flops=m * width * (4 * HEAD_PAD + 20),
            transcendentals=m,
            bytes_accessed=2 * m * width * 2 + pad * m * 2,
        ),
    )(flat, ds, gain, wt)


def layer_norm(values):
    centred = values - jnp.mean(values, axis=-1, keepdims=True)
    inv_std = lax.rsqrt(jnp.mean(centred * centred, axis=-1, keepdims=True) + epsilon)
    return (centred * inv_std, inv_std)


def norm_back(normed, inv_std, grad):
    mean_grad = jnp.mean(grad, axis=-1, keepdims=True)
    mean_proj = jnp.mean(grad * normed, axis=-1, keepdims=True)
    return inv_std * (grad - mean_grad - normed * mean_proj)


def silu_slope(values):
    sigma = jax.nn.sigmoid(values)
    return sigma * (1.0 + values * (1.0 - sigma))


def head_split(values):
    return values.reshape(values.shape[:-1] + (values.shape[-1] // DH, DH))


def swap_heads(values):
    return lax.ppermute(values, "head", [(0, 1), (1, 0)])


def whole_rows(own, first):
    other = swap_heads(own)
    return jnp.where(
        first,
        jnp.concatenate([own, other], axis=0),
        jnp.concatenate([other, own], axis=0),
    )


def bit_reverse(value, bits):
    out = 0
    for bit in range(bits):
        out |= ((value >> bit) & 1) << (bits - 1 - bit)
    return out


def dp_gather(values):
    count = lax.axis_size("dp")
    index = lax.axis_index("dp")
    bits = count.bit_length() - 1
    block = values
    step = count // 2
    while step >= 1:
        other = lax.ppermute(block, "dp", [(i, i ^ step) for i in range(count)])
        block = jnp.where(
            (index & step) == 0,
            jnp.concatenate([block, other], axis=0),
            jnp.concatenate([other, block], axis=0),
        )
        step //= 2
    order = [bit_reverse(i, bits) for i in range(count)]
    return block[jnp.array(order)]


def dp_reduce_rows(values):
    count = lax.axis_size("dp")
    index = lax.axis_index("dp")
    rows_each = values.shape[0] // count
    block = values.astype(jnp.float32)
    step = 1
    while step < count:
        pairs = block.reshape(-1, 2, rows_each, block.shape[-1])
        even = pairs[:, 0].reshape(-1, block.shape[-1])
        odd = pairs[:, 1].reshape(-1, block.shape[-1])
        upper = (index & step) != 0
        keep = jnp.where(upper, odd, even)
        send = jnp.where(upper, even, odd).astype(jnp.bfloat16)
        got = lax.ppermute(send, "dp", [(i, i ^ step) for i in range(count)])
        block = keep + got.astype(jnp.float32)
        step *= 2
    return block


def own_rows(values, head, rows):
    return lax.dynamic_slice_in_dim(values, head * rows, rows, 1)


def head_sum(part):
    return part + swap_heads(part)


def trade_blocks(values, head, size, axis, mine_axis):
    mine = lax.dynamic_slice_in_dim(values, head * size, size, axis)
    theirs = swap_heads(lax.dynamic_slice_in_dim(values, (1 - head) * size, size, axis))
    return jnp.where(
        head == 0,
        jnp.concatenate([mine, theirs], axis=mine_axis),
        jnp.concatenate([theirs, mine], axis=mine_axis),
    )


def attn_scores(queries, keys, biases, valid):
    scores = jnp.einsum("cqhe,ckhe->chqk", queries, keys, preferred_element_type=jnp.float32)
    scores = scores * DH ** (-0.5) + biases.astype(jnp.float32)
    return jnp.where(valid[:, None, None, :], scores, masked_score)


def to_chunks(values, parts):
    return values.reshape(parts, -1, LANES)


def shards(
    layer_input,
    pair_input,
    time_cond,
    chain_lengths,
    residue_mask,
    mod_weight,
    mod_bias,
    qkv_weight,
    pair_gain,
    pair_weight,
    out_weight,
    out_bias,
    gate_up_weight,
    down_weight,
    output_grad,
):
    assert layer_input.shape[0] == 1
    rows = layer_input.shape[1]
    width = layer_input.shape[2]
    length = residue_mask.shape[1]
    head = lax.axis_index("head")
    first = head == 0
    data_count = lax.axis_size("dp")
    proj = qkv_weight.shape[2]
    ffn = gate_up_weight.shape[2]
    qkv_w = qkv_weight.reshape(width, 3 * proj)
    gate_up_w = gate_up_weight.reshape(width, 2 * ffn)

    x_rows = whole_rows(layer_input[0], first)
    g_rows = whole_rows(output_grad[0], first)
    out_weight_all = whole_rows(out_weight, first)

    positions = jnp.arange(length, dtype=jnp.int32)
    valid = (positions < chain_lengths[0]) & ((residue_mask[0] == 1) | (positions == 0))
    silu_cond = jax.nn.silu(time_cond).astype(jnp.bfloat16)
    modulation = jnp.dot(silu_cond, mod_weight, preferred_element_type=jnp.float32) + mod_bias
    scale_a, shift_a, gate_a, scale_t, shift_t, gate_t = [
        modulation[:, section * width : (section + 1) * width] for section in range(6)
    ]

    heads_all = pair_weight.shape[1]
    pair_width = pair_input.shape[-1]
    pair_flat = pair_input.reshape(-1, pair_width)
    pair_wt = jnp.pad(pair_weight.T, ((0, HEAD_PAD - heads_all), (0, 0)))
    pair_gain_row = pair_gain.reshape(1, pair_width)
    bias_flat = pair_forward(pair_flat, pair_gain_row, pair_wt, heads_all)
    bias_rows = bias_flat.reshape(heads_all, rows, length)
    heads_own = proj // DH
    biases = trade_blocks(bias_rows, head, heads_own, 0, 1)

    residues = x_rows.astype(jnp.float32)
    norm_in, inv_in = layer_norm(residues)
    normed_a = (norm_in * (1.0 + scale_a) + shift_a).astype(jnp.bfloat16)
    projected = jnp.dot(normed_a, qkv_w, preferred_element_type=jnp.float32).astype(jnp.bfloat16)
    queries = head_split(projected[:, :proj])
    keys = head_split(projected[:, proj : 2 * proj])
    values = head_split(projected[:, 2 * proj :])
    scores = jnp.einsum("qhe,khe->hqk", queries, keys, preferred_element_type=jnp.float32)
    scores = scores * DH ** (-0.5) + biases.astype(jnp.float32)
    scores = jnp.where(valid[None, None, :], scores, masked_score)
    row_max = jnp.max(scores, axis=-1, keepdims=True)
    exp_scores = jnp.exp(scores - row_max)
    row_total = jnp.sum(exp_scores, axis=-1, keepdims=True)
    attn_probs = exp_scores / row_total
    probs_low = attn_probs.astype(jnp.bfloat16)
    mixed = jnp.einsum("hqk,khe->qhe", probs_low, values, preferred_element_type=jnp.float32)
    mixed = mixed.reshape(length, proj).astype(jnp.bfloat16)
    mixed_all = jnp.where(
        first,
        jnp.concatenate([mixed, swap_heads(mixed)], axis=1),
        jnp.concatenate([swap_heads(mixed), mixed], axis=1),
    )
    attn_branch = jnp.dot(mixed_all, out_weight_all, preferred_element_type=jnp.float32) + out_bias
    sig_a = jax.nn.sigmoid(gate_a)
    middle = residues + sig_a * attn_branch

    norm_mid, inv_mid = layer_norm(middle)
    normed_t = (norm_mid * (1.0 + scale_t) + shift_t).astype(jnp.bfloat16)
    gate_up = jnp.dot(normed_t, gate_up_w, preferred_element_type=jnp.float32)
    gate_pre = gate_up[:, :ffn]
    up_pre = gate_up[:, ffn:]
    hidden = (jax.nn.silu(gate_pre) * up_pre).astype(jnp.bfloat16)
    ffn_part = jnp.dot(hidden, down_weight, preferred_element_type=jnp.float32).astype(jnp.bfloat16)
    ffn_branch = ffn_part.astype(jnp.float32) + swap_heads(ffn_part).astype(jnp.float32)
    sig_t = jax.nn.sigmoid(gate_t)
    layer_output = own_rows((middle + sig_t * ffn_branch).astype(jnp.bfloat16)[None], head, rows)

    grad_out = g_rows.astype(jnp.float32)
    d_ffn = (grad_out * sig_t).astype(jnp.bfloat16)
    d_gate_t = jnp.sum(grad_out * ffn_branch * sig_t * (1.0 - sig_t), axis=0, keepdims=True)
    down_grad_t = lax.dot_general(
        d_ffn, hidden, (((0,), (0,)), ((), ())), preferred_element_type=jnp.float32
    )
    d_hidden = lax.dot_general(
        d_ffn, down_weight, (((1,), (1,)), ((), ())), preferred_element_type=jnp.float32
    )
    d_gate = d_hidden * up_pre * silu_slope(gate_pre)
    d_up = d_hidden * jax.nn.silu(gate_pre)
    d_gate_up = jnp.concatenate([d_gate, d_up], axis=1).astype(jnp.bfloat16)
    gate_up_grad = lax.dot_general(
        normed_t, d_gate_up, (((0,), (0,)), ((), ())), preferred_element_type=jnp.float32
    )
    ffn_in_part = lax.dot_general(
        d_gate_up, gate_up_w, (((1,), (1,)), ((), ())), preferred_element_type=jnp.float32
    )
    d_normed_t = head_sum(ffn_in_part)
    d_middle = grad_out + norm_back(norm_mid, inv_mid, d_normed_t * (1.0 + scale_t))
    d_scale_t = jnp.sum(d_normed_t * norm_mid, axis=0, keepdims=True)
    d_shift_t = jnp.sum(d_normed_t, axis=0, keepdims=True)
    d_attn = d_middle * sig_a
    d_gate_a = jnp.sum(d_middle * attn_branch * sig_a * (1.0 - sig_a), axis=0, keepdims=True)
    d_out_bias = jnp.sum(d_attn, axis=0, keepdims=True)
    d_attn_low = d_attn.astype(jnp.bfloat16)

    out_weight_grad_t = lax.dot_general(
        d_attn_low, mixed, (((0,), (0,)), ((), ())), preferred_element_type=jnp.float32
    )
    packed = lax.optimization_barrier(jnp.zeros((width, proj + 3 * ffn), jnp.bfloat16))
    packed = lax.dynamic_update_slice(packed, gate_up_grad.astype(jnp.bfloat16), (0, proj))
    packed = lax.dynamic_update_slice(packed, down_grad_t.astype(jnp.bfloat16), (0, proj + 2 * ffn))
    packed = lax.dynamic_update_slice(packed, out_weight_grad_t.astype(jnp.bfloat16), (0, 0))
    reduced = lax.psum_scatter(packed, "dp", scatter_dimension=0, tiled=True).astype(jnp.float32)
    d_mixed = head_split(
        lax.dot_general(
            d_attn_low, out_weight, (((1,), (1,)), ((), ())), preferred_element_type=jnp.float32
        ).astype(jnp.bfloat16)
    )
    d_values = jnp.einsum("hqk,qhe->khe", probs_low, d_mixed, preferred_element_type=jnp.float32)
    d_probs = jnp.einsum("qhe,khe->hqk", d_mixed, values, preferred_element_type=jnp.float32)
    d_scores = (
        attn_probs * (d_probs - jnp.sum(d_probs * attn_probs, axis=-1, keepdims=True))
    ).astype(jnp.bfloat16)
    d_queries = jnp.einsum(
        "hqk,khe->qhe", d_scores, keys, preferred_element_type=jnp.float32
    ) * DH ** (-0.5)
    d_keys = jnp.einsum(
        "hqk,qhe->khe", d_scores, queries, preferred_element_type=jnp.float32
    ) * DH ** (-0.5)
    d_qkv = jnp.concatenate(
        [d_queries.reshape(length, proj), d_keys.reshape(length, proj), d_values.reshape(length, proj)],
        axis=1,
    ).astype(jnp.bfloat16)
    qkv_grad = lax.dot_general(
        normed_a, d_qkv, (((0,), (0,)), ((), ())), preferred_element_type=jnp.float32
    )


    qkv_grad = dp_reduce_rows(qkv_grad.astype(jnp.bfloat16))

    attn_in_part = lax.dot_general(
        d_qkv, qkv_w, (((1,), (1,)), ((), ())), preferred_element_type=jnp.float32
    ).astype(jnp.bfloat16)
    d_normed_a = attn_in_part.astype(jnp.float32) + swap_heads(attn_in_part).astype(jnp.float32)
    input_grad = own_rows(
        (d_middle + norm_back(norm_in, inv_in, d_normed_a * (1.0 + scale_a)))[None], head, rows
    )
    d_scale_a = jnp.sum(d_normed_a * norm_in, axis=0, keepdims=True)
    d_shift_a = jnp.sum(d_normed_a, axis=0, keepdims=True)
    d_modulation = jnp.concatenate(
        [d_scale_a, d_shift_a, d_gate_a, d_scale_t, d_shift_t, d_gate_t], axis=-1
    )

    d_bias_rows = trade_blocks(d_scores, head, rows, 1, 0)
    d_bias_flat = jnp.pad(d_bias_rows.reshape(heads_all, -1), ((0, HEAD_PAD - heads_all), (0, 0)))
    pair_grad, pair_wg, pair_gg = pair_backward(pair_flat, d_bias_flat, pair_gain_row, pair_wt)
    pair_grad = pair_grad.reshape(pair_input.shape)
    pair_weight_grad = pair_wg[:heads_all].T
    pair_gain_grad = pair_gg[0]

    pair_small = head_sum(
        jnp.concatenate([pair_weight_grad.reshape(-1), pair_gain_grad])[None]
    )
    small = jnp.concatenate([d_modulation, time_cond, pair_small, d_out_bias], axis=-1)
    small_rows = dp_gather(small)
    mod_size = d_modulation.shape[-1]
    cond_size = time_cond.shape[-1]
    pw_size = pair_weight.size
    pg_size = pair_gain.size
    mod_chain = small_rows[:, :mod_size]
    cond_chain = small_rows[:, mod_size : mod_size + cond_size]
    rest = jnp.sum(small_rows[:, mod_size + cond_size :], axis=0)
    pair_weight_grad = rest[:pw_size].reshape(pair_weight.shape)
    pair_gain_grad = rest[pw_size : pw_size + pg_size]
    out_bias_grad = rest[pw_size + pg_size :]
    cond_act = lax.optimization_barrier(jax.nn.silu(cond_chain).astype(jnp.bfloat16)).astype(
        jnp.float32
    )
    mod_weight_grad = jnp.dot(cond_act.T, mod_chain, precision=precise)
    mod_bias_grad = jnp.sum(mod_chain, axis=0)
    cond_grad = jnp.dot(
        d_modulation, mod_weight.astype(jnp.float32).T, precision=precise
    ) * silu_slope(time_cond)

    cuts = [0, proj, proj + 2 * ffn, proj + 3 * ffn]
    pieces = [reduced[:, cuts[i] : cuts[i + 1]] for i in range(3)]
    qkv_grad = qkv_grad.reshape(-1, 3, proj)
    out_weight_grad = pieces[0].T
    gate_up_grad = pieces[1].reshape(-1, 2, ffn)
    down_grad = pieces[2].T
    return (
        layer_output,
        input_grad,
        pair_grad,
        cond_grad,
        mod_weight_grad,
        mod_bias_grad,
        qkv_grad,
        pair_gain_grad,
        pair_weight_grad,
        out_weight_grad,
        out_bias_grad,
        gate_up_grad,
        down_grad,
    )


def solution(mesh):
    placed = (
        P("dp", "head", None),
        P("dp", "head", None, None),
        P("dp", None),
        P("dp"),
        P("dp", None),
        P(),
        P(),
        P(None, None, "head"),
        P(),
        P(),
        P("head", None),
        P(),
        P(None, None, "head"),
        P("head", None),
        P("dp", "head", None),
    )
    return jax.shard_map(
        shards,
        mesh=mesh,
        in_specs=placed,
        out_specs=(
            P("dp", "head", None),
            P("dp", "head", None),
            P("dp", "head", None, None),
            P("dp", None),
            P(),
            P(),
            P("dp", None, "head"),
            P(),
            P(),
            P("head", "dp"),
            P(),
            P("dp", None, "head"),
            P("head", "dp"),
        ),
        check_vma=False,
    )
```

```python
import jax
import jax.numpy as jnp
from jax import lax
from jax.experimental import pallas as pl
from jax.experimental.pallas import tpu as pltpu
from jax.sharding import PartitionSpec as P

DH = 64


epsilon = 1e-05
masked_score = -1000000000.0
precise = lax.Precision.HIGHEST
LANES = 128
PAIR_TILE = 4096
PAIR_BACK_TILE = 2048
HEAD_PAD = 16


def pair_stats(x):
    centred = x - jnp.mean(x, axis=-1, keepdims=True)
    inv_std = lax.rsqrt(jnp.mean(centred * centred, axis=-1, keepdims=True) + epsilon)
    return centred * inv_std, inv_std


def pair_forward_kernel(x_ref, gain_ref, wt_ref, bias_ref):
    normed, _ = pair_stats(x_ref[...].astype(jnp.float32))
    scaled = (normed * gain_ref[...]).astype(jnp.bfloat16)
    bias = lax.dot_general(
        wt_ref[...], scaled, (((1,), (1,)), ((), ())), preferred_element_type=jnp.float32
    )
    bias_ref[...] = bias[: bias_ref.shape[0]].astype(bias_ref.dtype)


def pair_forward(flat, gain, wt, heads):
    m, width = flat.shape
    tile = min(PAIR_TILE, m)
    return pl.pallas_call(
        pair_forward_kernel,
        grid=(m // tile,),
        in_specs=[
            pl.BlockSpec((tile, width), lambda i: (i, 0)),
            pl.BlockSpec((1, width), lambda i: (0, 0)),
            pl.BlockSpec(wt.shape, lambda i: (0, 0)),
        ],
        out_specs=pl.BlockSpec((heads, tile), lambda i: (0, i)),
        out_shape=jax.ShapeDtypeStruct((heads, m), jnp.bfloat16),
        cost_estimate=pl.CostEstimate(
            flops=m * width * (2 * HEAD_PAD + 10),
            transcendentals=m,
            bytes_accessed=m * width * 2 + heads * m * 2,
        ),
    )(flat, gain, wt)


def pair_backward_kernel(x_ref, ds_ref, gain_ref, wt_ref, grad_ref, wg_ref, gg_ref):
    step = pl.program_id(0)
    normed, inv_std = pair_stats(x_ref[...].astype(jnp.float32))
    gain = gain_ref[...]
    scaled = (normed * gain).astype(jnp.bfloat16)
    ds = ds_ref[...]
    d_scaled = lax.dot_general(
        ds, wt_ref[...], (((0,), (0,)), ((), ())), preferred_element_type=jnp.float32
    )
    wg = lax.dot_general(ds, scaled, (((1,), (0,)), ((), ())), preferred_element_type=jnp.float32)
    gg = jnp.sum(d_scaled * normed, axis=0, keepdims=True)
    d_normed = d_scaled * gain
    mean_grad = jnp.mean(d_normed, axis=-1, keepdims=True)
    mean_proj = jnp.mean(d_normed * normed, axis=-1, keepdims=True)
    grad_ref[...] = (inv_std * (d_normed - mean_grad - normed * mean_proj)).astype(grad_ref.dtype)

    @pl.when(step == 0)
    def _():
        wg_ref[...] = jnp.zeros_like(wg_ref)
        gg_ref[...] = jnp.zeros_like(gg_ref)

    wg_ref[...] += wg
    gg_ref[...] += gg


def pair_backward(flat, ds, gain, wt):
    m, width = flat.shape
    tile = min(PAIR_BACK_TILE, m)
    pad = ds.shape[0]
    return pl.pallas_call(
        pair_backward_kernel,
        grid=(m // tile,),
        in_specs=[
            pl.BlockSpec((tile, width), lambda i: (i, 0)),
            pl.BlockSpec((pad, tile), lambda i: (0, i)),
            pl.BlockSpec((1, width), lambda i: (0, 0)),
            pl.BlockSpec(wt.shape, lambda i: (0, 0)),
        ],
        out_specs=[
            pl.BlockSpec((tile, width), lambda i: (i, 0)),
            pl.BlockSpec((pad, width), lambda i: (0, 0)),
            pl.BlockSpec((1, width), lambda i: (0, 0)),
        ],
        out_shape=[
            jax.ShapeDtypeStruct((m, width), jnp.bfloat16),
            jax.ShapeDtypeStruct((pad, width), jnp.float32),
            jax.ShapeDtypeStruct((1, width), jnp.float32),
        ],
        compiler_params=pltpu.CompilerParams(dimension_semantics=("arbitrary",)),
        cost_estimate=pl.CostEstimate(
            flops=m * width * (4 * HEAD_PAD + 20),
            transcendentals=m,
            bytes_accessed=2 * m * width * 2 + pad * m * 2,
        ),
    )(flat, ds, gain, wt)


def layer_norm(values):
    centred = values - jnp.mean(values, axis=-1, keepdims=True)
    inv_std = lax.rsqrt(jnp.mean(centred * centred, axis=-1, keepdims=True) + epsilon)
    return (centred * inv_std, inv_std)


def norm_back(normed, inv_std, grad):
    mean_grad = jnp.mean(grad, axis=-1, keepdims=True)
    mean_proj = jnp.mean(grad * normed, axis=-1, keepdims=True)
    return inv_std * (grad - mean_grad - normed * mean_proj)


def silu_slope(values):
    sigma = jax.nn.sigmoid(values)
    return sigma * (1.0 + values * (1.0 - sigma))


def head_split(values):
    return values.reshape(values.shape[:-1] + (values.shape[-1] // DH, DH))


def swap_heads(values):
    return lax.ppermute(values, "head", [(0, 1), (1, 0)])


def whole_rows(own, first):
    other = swap_heads(own)
    return jnp.where(
        first,
        jnp.concatenate([own, other], axis=0),
        jnp.concatenate([other, own], axis=0),
    )


def dp_gather(values):
    count = lax.axis_size("dp")
    index = lax.axis_index("dp")
    block = values
    step = 1
    while step < count:
        other = lax.ppermute(block, "dp", [(i, i ^ step) for i in range(count)])
        block = jnp.where(
            (index & step) == 0,
            jnp.concatenate([block, other], axis=0),
            jnp.concatenate([other, block], axis=0),
        )
        step *= 2
    return block


def dp_sum(values):
    count = lax.axis_size("dp")
    index = lax.axis_index("dp")
    step = 1
    while step < count:
        other = lax.ppermute(values, "dp", [(i, i ^ step) for i in range(count)])
        values = jnp.where((index & step) == 0, values + other, other + values)
        step *= 2
    return values


def own_rows(values, head, rows):
    return lax.dynamic_slice_in_dim(values, head * rows, rows, 1)


def head_sum(part):
    return part + swap_heads(part)


def trade_blocks(values, head, size, axis, mine_axis):
    mine = lax.dynamic_slice_in_dim(values, head * size, size, axis)
    theirs = swap_heads(lax.dynamic_slice_in_dim(values, (1 - head) * size, size, axis))
    return jnp.where(
        head == 0,
        jnp.concatenate([mine, theirs], axis=mine_axis),
        jnp.concatenate([theirs, mine], axis=mine_axis),
    )


def attn_scores(queries, keys, biases, valid):
    scores = jnp.einsum("cqhe,ckhe->chqk", queries, keys, preferred_element_type=jnp.float32)
    scores = scores * DH ** (-0.5) + biases.astype(jnp.float32)
    return jnp.where(valid[:, None, None, :], scores, masked_score)


def to_chunks(values, parts):
    return values.reshape(parts, -1, LANES)


def shards(
    layer_input,
    pair_input,
    time_cond,
    chain_lengths,
    residue_mask,
    mod_weight,
    mod_bias,
    qkv_weight,
    pair_gain,
    pair_weight,
    out_weight,
    out_bias,
    gate_up_weight,
    down_weight,
    output_grad,
):
    assert layer_input.shape[0] == 1
    rows = layer_input.shape[1]
    width = layer_input.shape[2]
    length = residue_mask.shape[1]
    head = lax.axis_index("head")
    first = head == 0
    data_count = lax.axis_size("dp")
    proj = qkv_weight.shape[2]
    ffn = gate_up_weight.shape[2]
    qkv_w = qkv_weight.reshape(width, 3 * proj)
    gate_up_w = gate_up_weight.reshape(width, 2 * ffn)

    bundle = jnp.concatenate([layer_input[0], output_grad[0], out_weight], axis=0)
    bundle_other = swap_heads(bundle)

    def joined(start, size):
        own = bundle[start : start + size]
        other = bundle_other[start : start + size]
        return jnp.where(
            first, jnp.concatenate([own, other], axis=0), jnp.concatenate([other, own], axis=0)
        )

    x_rows = joined(0, rows)
    g_rows = joined(rows, rows)
    out_weight_all = joined(2 * rows, out_weight.shape[0])

    positions = jnp.arange(length, dtype=jnp.int32)
    valid = (positions < chain_lengths[0]) & ((residue_mask[0] == 1) | (positions == 0))
    silu_cond = jax.nn.silu(time_cond).astype(jnp.bfloat16)
    modulation = jnp.dot(silu_cond, mod_weight, preferred_element_type=jnp.float32) + mod_bias
    scale_a, shift_a, gate_a, scale_t, shift_t, gate_t = [
        modulation[:, section * width : (section + 1) * width] for section in range(6)
    ]

    heads_all = pair_weight.shape[1]
    pair_width = pair_input.shape[-1]
    pair_flat = pair_input.reshape(-1, pair_width)
    pair_wt = jnp.pad(pair_weight.T, ((0, HEAD_PAD - heads_all), (0, 0)))
    pair_gain_row = pair_gain.reshape(1, pair_width)
    bias_flat = pair_forward(pair_flat, pair_gain_row, pair_wt, heads_all)
    bias_rows = bias_flat.reshape(heads_all, rows, length)
    heads_own = proj // DH
    biases = trade_blocks(bias_rows, head, heads_own, 0, 1)

    residues = x_rows.astype(jnp.float32)
    norm_in, inv_in = layer_norm(residues)
    normed_a = (norm_in * (1.0 + scale_a) + shift_a).astype(jnp.bfloat16)
    projected = jnp.dot(normed_a, qkv_w, preferred_element_type=jnp.float32).astype(jnp.bfloat16)
    queries = head_split(projected[:, :proj])
    keys = head_split(projected[:, proj : 2 * proj])
    values = head_split(projected[:, 2 * proj :])
    scores = jnp.einsum("qhe,khe->hqk", queries, keys, preferred_element_type=jnp.float32)
    scores = scores * DH ** (-0.5) + biases.astype(jnp.float32)
    scores = jnp.where(valid[None, None, :], scores, masked_score)
    row_max = jnp.max(scores, axis=-1, keepdims=True)
    exp_scores = jnp.exp(scores - row_max)
    row_total = jnp.sum(exp_scores, axis=-1, keepdims=True)
    attn_probs = exp_scores / row_total
    probs_low = attn_probs.astype(jnp.bfloat16)
    mixed = jnp.einsum("hqk,khe->qhe", probs_low, values, preferred_element_type=jnp.float32)
    mixed = mixed.reshape(length, proj).astype(jnp.bfloat16)
    mixed_all = jnp.where(
        first,
        jnp.concatenate([mixed, swap_heads(mixed)], axis=1),
        jnp.concatenate([swap_heads(mixed), mixed], axis=1),
    )
    attn_branch = jnp.dot(mixed_all, out_weight_all, preferred_element_type=jnp.float32) + out_bias
    sig_a = jax.nn.sigmoid(gate_a)
    middle = residues + sig_a * attn_branch

    norm_mid, inv_mid = layer_norm(middle)
    normed_t = (norm_mid * (1.0 + scale_t) + shift_t).astype(jnp.bfloat16)
    gate_up = jnp.dot(normed_t, gate_up_w, preferred_element_type=jnp.float32)
    gate_pre = gate_up[:, :ffn]
    up_pre = gate_up[:, ffn:]
    hidden = (jax.nn.silu(gate_pre) * up_pre).astype(jnp.bfloat16)
    ffn_part = jnp.dot(hidden, down_weight, preferred_element_type=jnp.float32).astype(jnp.bfloat16)
    ffn_branch = ffn_part.astype(jnp.float32) + swap_heads(ffn_part).astype(jnp.float32)
    sig_t = jax.nn.sigmoid(gate_t)
    layer_output = own_rows((middle + sig_t * ffn_branch).astype(jnp.bfloat16)[None], head, rows)

    grad_out = g_rows.astype(jnp.float32)
    d_ffn = (grad_out * sig_t).astype(jnp.bfloat16)
    d_gate_t = jnp.sum(grad_out * ffn_branch * sig_t * (1.0 - sig_t), axis=0, keepdims=True)
    down_grad_t = lax.dot_general(
        d_ffn, hidden, (((0,), (0,)), ((), ())), preferred_element_type=jnp.float32
    )
    d_hidden = lax.dot_general(
        d_ffn, down_weight, (((1,), (1,)), ((), ())), preferred_element_type=jnp.float32
    )
    d_gate = d_hidden * up_pre * silu_slope(gate_pre)
    d_up = d_hidden * jax.nn.silu(gate_pre)
    d_gate_up = jnp.concatenate([d_gate, d_up], axis=1).astype(jnp.bfloat16)
    gate_up_grad = lax.dot_general(
        normed_t, d_gate_up, (((0,), (0,)), ((), ())), preferred_element_type=jnp.float32
    )
    ffn_in_part = lax.dot_general(
        d_gate_up, gate_up_w, (((1,), (1,)), ((), ())), preferred_element_type=jnp.float32
    )
    d_normed_t = head_sum(ffn_in_part)
    d_middle = grad_out + norm_back(norm_mid, inv_mid, d_normed_t * (1.0 + scale_t))
    d_scale_t = jnp.sum(d_normed_t * norm_mid, axis=0, keepdims=True)
    d_shift_t = jnp.sum(d_normed_t, axis=0, keepdims=True)
    d_attn = d_middle * sig_a
    d_gate_a = jnp.sum(d_middle * attn_branch * sig_a * (1.0 - sig_a), axis=0, keepdims=True)
    d_out_bias = jnp.sum(d_attn, axis=0, keepdims=True)
    d_attn_low = d_attn.astype(jnp.bfloat16)

    out_weight_grad_t = lax.dot_general(
        d_attn_low, mixed, (((0,), (0,)), ((), ())), preferred_element_type=jnp.float32
    )
    d_mixed = head_split(
        lax.dot_general(
            d_attn_low, out_weight, (((1,), (1,)), ((), ())), preferred_element_type=jnp.float32
        ).astype(jnp.bfloat16)
    )
    d_values = jnp.einsum("hqk,qhe->khe", probs_low, d_mixed, preferred_element_type=jnp.float32)
    d_probs = jnp.einsum("qhe,khe->hqk", d_mixed, values, preferred_element_type=jnp.float32)
    d_scores = (
        attn_probs * (d_probs - jnp.sum(d_probs * attn_probs, axis=-1, keepdims=True))
    ).astype(jnp.bfloat16)
    d_queries = jnp.einsum(
        "hqk,khe->qhe", d_scores, keys, preferred_element_type=jnp.float32
    ) * DH ** (-0.5)
    d_keys = jnp.einsum(
        "hqk,qhe->khe", d_scores, queries, preferred_element_type=jnp.float32
    ) * DH ** (-0.5)
    d_qkv = jnp.concatenate(
        [d_queries.reshape(length, proj), d_keys.reshape(length, proj), d_values.reshape(length, proj)],
        axis=1,
    ).astype(jnp.bfloat16)
    qkv_grad = lax.dot_general(
        normed_a, d_qkv, (((0,), (0,)), ((), ())), preferred_element_type=jnp.float32
    )

    packed = lax.optimization_barrier(jnp.zeros((width, 4 * proj + 3 * ffn), jnp.bfloat16))
    packed = lax.dynamic_update_slice(packed, gate_up_grad.astype(jnp.bfloat16), (0, 4 * proj))
    packed = lax.dynamic_update_slice(
        packed, down_grad_t.astype(jnp.bfloat16), (0, 4 * proj + 2 * ffn)
    )
    packed = lax.dynamic_update_slice(packed, out_weight_grad_t.astype(jnp.bfloat16), (0, 3 * proj))
    packed = lax.dynamic_update_slice(packed, qkv_grad.astype(jnp.bfloat16), (0, 0))
    reduced = lax.psum_scatter(packed, "dp", scatter_dimension=0, tiled=True).astype(jnp.float32)

    attn_in_part = lax.dot_general(
        d_qkv, qkv_w, (((1,), (1,)), ((), ())), preferred_element_type=jnp.float32
    ).astype(jnp.bfloat16)
    d_normed_a = attn_in_part.astype(jnp.float32) + swap_heads(attn_in_part).astype(jnp.float32)
    input_grad = own_rows(
        (d_middle + norm_back(norm_in, inv_in, d_normed_a * (1.0 + scale_a)))[None], head, rows
    )
    d_scale_a = jnp.sum(d_normed_a * norm_in, axis=0, keepdims=True)
    d_shift_a = jnp.sum(d_normed_a, axis=0, keepdims=True)
    d_modulation = jnp.concatenate(
        [d_scale_a, d_shift_a, d_gate_a, d_scale_t, d_shift_t, d_gate_t], axis=-1
    )

    d_bias_rows = trade_blocks(d_scores, head, rows, 1, 0)
    d_bias_flat = jnp.pad(d_bias_rows.reshape(heads_all, -1), ((0, HEAD_PAD - heads_all), (0, 0)))
    pair_grad, pair_wg, pair_gg = pair_backward(pair_flat, d_bias_flat, pair_gain_row, pair_wt)
    pair_grad = pair_grad.reshape(pair_input.shape)
    pair_weight_grad = pair_wg[:heads_all].T
    pair_gain_grad = pair_gg[0]

    pair_small = head_sum(
        jnp.concatenate([pair_weight_grad.reshape(-1), pair_gain_grad])[None]
    )
    small = jnp.concatenate([d_modulation, time_cond, d_out_bias], axis=-1)
    small_rows = dp_gather(small)
    mod_size = d_modulation.shape[-1]
    cond_size = time_cond.shape[-1]
    pw_size = pair_weight.size
    mod_chain = small_rows[:, :mod_size]
    cond_chain = small_rows[:, mod_size : mod_size + cond_size]
    out_bias_grad = jnp.sum(small_rows[:, mod_size + cond_size :], axis=0)
    pair_total = dp_sum(pair_small)[0]
    pair_weight_grad = pair_total[:pw_size].reshape(pair_weight.shape)
    pair_gain_grad = pair_total[pw_size:]
    cond_act = lax.optimization_barrier(jax.nn.silu(cond_chain).astype(jnp.bfloat16)).astype(
        jnp.float32
    )
    mod_weight_grad = jnp.dot(cond_act.T, mod_chain, precision=precise)
    mod_bias_grad = jnp.sum(mod_chain, axis=0)
    cond_grad = jnp.dot(
        d_modulation, mod_weight.astype(jnp.float32).T, precision=precise
    ) * silu_slope(time_cond)

    cuts = [0, 3 * proj, 4 * proj, 4 * proj + 2 * ffn, 4 * proj + 3 * ffn]
    pieces = [reduced[:, cuts[i] : cuts[i + 1]] for i in range(4)]
    qkv_grad = pieces[0].reshape(-1, 3, proj)
    out_weight_grad = pieces[1].T
    gate_up_grad = pieces[2].reshape(-1, 2, ffn)
    down_grad = pieces[3].T
    return (
        layer_output,
        input_grad,
        pair_grad,
        cond_grad,
        mod_weight_grad,
        mod_bias_grad,
        qkv_grad,
        pair_gain_grad,
        pair_weight_grad,
        out_weight_grad,
        out_bias_grad,
        gate_up_grad,
        down_grad,
    )


def solution(mesh):
    placed = (
        P("dp", "head", None),
        P("dp", "head", None, None),
        P("dp", None),
        P("dp"),
        P("dp", None),
        P(),
        P(),
        P(None, None, "head"),
        P(),
        P(),
        P("head", None),
        P(),
        P(None, None, "head"),
        P("head", None),
        P("dp", "head", None),
    )
    return jax.shard_map(
        shards,
        mesh=mesh,
        in_specs=placed,
        out_specs=(
            P("dp", "head", None),
            P("dp", "head", None),
            P("dp", "head", None, None),
            P("dp", None),
            P(),
            P(),
            P("dp", None, "head"),
            P(),
            P(),
            P("head", "dp"),
            P(),
            P("dp", None, "head"),
            P("head", "dp"),
        ),
        check_vma=False,
    )
```

```python
import jax
import jax.numpy as jnp
from jax import lax
from jax.experimental import pallas as pl
from jax.experimental.pallas import tpu as pltpu
from jax.sharding import PartitionSpec as P

DH = 64


epsilon = 1e-05
masked_score = -1000000000.0
precise = lax.Precision.HIGHEST
LANES = 128
PAIR_TILE = 4096
PAIR_BACK_TILE = 2048
HEAD_PAD = 16


def pair_stats(x):
    centred = x - jnp.mean(x, axis=-1, keepdims=True)
    inv_std = lax.rsqrt(jnp.mean(centred * centred, axis=-1, keepdims=True) + epsilon)
    return centred * inv_std, inv_std


def pair_forward_kernel(x_ref, gain_ref, wt_ref, bias_ref):
    normed, _ = pair_stats(x_ref[...].astype(jnp.float32))
    scaled = (normed * gain_ref[...]).astype(jnp.bfloat16)
    bias = lax.dot_general(
        wt_ref[...], scaled, (((1,), (1,)), ((), ())), preferred_element_type=jnp.float32
    )
    bias_ref[...] = bias[: bias_ref.shape[0]].astype(bias_ref.dtype)


def pair_forward(flat, gain, wt, heads):
    m, width = flat.shape
    tile = min(PAIR_TILE, m)
    return pl.pallas_call(
        pair_forward_kernel,
        grid=(m // tile,),
        in_specs=[
            pl.BlockSpec((tile, width), lambda i: (i, 0)),
            pl.BlockSpec((1, width), lambda i: (0, 0)),
            pl.BlockSpec(wt.shape, lambda i: (0, 0)),
        ],
        out_specs=pl.BlockSpec((heads, tile), lambda i: (0, i)),
        out_shape=jax.ShapeDtypeStruct((heads, m), jnp.bfloat16),
        cost_estimate=pl.CostEstimate(
            flops=m * width * (2 * HEAD_PAD + 10),
            transcendentals=m,
            bytes_accessed=m * width * 2 + heads * m * 2,
        ),
    )(flat, gain, wt)


def pair_backward_kernel(x_ref, ds_ref, gain_ref, wt_ref, grad_ref, wg_ref, gg_ref):
    step = pl.program_id(0)
    normed, inv_std = pair_stats(x_ref[...].astype(jnp.float32))
    gain = gain_ref[...]
    scaled = (normed * gain).astype(jnp.bfloat16)
    ds = ds_ref[...]
    d_scaled = lax.dot_general(
        ds, wt_ref[...], (((0,), (0,)), ((), ())), preferred_element_type=jnp.float32
    )
    wg = lax.dot_general(ds, scaled, (((1,), (0,)), ((), ())), preferred_element_type=jnp.float32)
    gg = jnp.sum(d_scaled * normed, axis=0, keepdims=True)
    d_normed = d_scaled * gain
    mean_grad = jnp.mean(d_normed, axis=-1, keepdims=True)
    mean_proj = jnp.mean(d_normed * normed, axis=-1, keepdims=True)
    grad_ref[...] = (inv_std * (d_normed - mean_grad - normed * mean_proj)).astype(grad_ref.dtype)

    @pl.when(step == 0)
    def _():
        wg_ref[...] = jnp.zeros_like(wg_ref)
        gg_ref[...] = jnp.zeros_like(gg_ref)

    wg_ref[...] += wg
    gg_ref[...] += gg


def pair_backward(flat, ds, gain, wt):
    m, width = flat.shape
    tile = min(PAIR_BACK_TILE, m)
    pad = ds.shape[0]
    return pl.pallas_call(
        pair_backward_kernel,
        grid=(m // tile,),
        in_specs=[
            pl.BlockSpec((tile, width), lambda i: (i, 0)),
            pl.BlockSpec((pad, tile), lambda i: (0, i)),
            pl.BlockSpec((1, width), lambda i: (0, 0)),
            pl.BlockSpec(wt.shape, lambda i: (0, 0)),
        ],
        out_specs=[
            pl.BlockSpec((tile, width), lambda i: (i, 0)),
            pl.BlockSpec((pad, width), lambda i: (0, 0)),
            pl.BlockSpec((1, width), lambda i: (0, 0)),
        ],
        out_shape=[
            jax.ShapeDtypeStruct((m, width), jnp.bfloat16),
            jax.ShapeDtypeStruct((pad, width), jnp.float32),
            jax.ShapeDtypeStruct((1, width), jnp.float32),
        ],
        compiler_params=pltpu.CompilerParams(dimension_semantics=("arbitrary",)),
        cost_estimate=pl.CostEstimate(
            flops=m * width * (4 * HEAD_PAD + 20),
            transcendentals=m,
            bytes_accessed=2 * m * width * 2 + pad * m * 2,
        ),
    )(flat, ds, gain, wt)


def layer_norm(values):
    centred = values - jnp.mean(values, axis=-1, keepdims=True)
    inv_std = lax.rsqrt(jnp.mean(centred * centred, axis=-1, keepdims=True) + epsilon)
    return (centred * inv_std, inv_std)


def norm_back(normed, inv_std, grad):
    mean_grad = jnp.mean(grad, axis=-1, keepdims=True)
    mean_proj = jnp.mean(grad * normed, axis=-1, keepdims=True)
    return inv_std * (grad - mean_grad - normed * mean_proj)


def silu_slope(values):
    sigma = jax.nn.sigmoid(values)
    return sigma * (1.0 + values * (1.0 - sigma))


def head_split(values):
    return values.reshape(values.shape[:-1] + (values.shape[-1] // DH, DH))


def swap_heads(values):
    return lax.ppermute(values, "head", [(0, 1), (1, 0)])


def whole_rows(own, first):
    other = swap_heads(own)
    return jnp.where(
        first,
        jnp.concatenate([own, other], axis=0),
        jnp.concatenate([other, own], axis=0),
    )


def dp_gather(values):
    count = lax.axis_size("dp")
    index = lax.axis_index("dp")
    block = values
    step = 1
    while step < count:
        other = lax.ppermute(block, "dp", [(i, i ^ step) for i in range(count)])
        block = jnp.where(
            (index & step) == 0,
            jnp.concatenate([block, other], axis=0),
            jnp.concatenate([other, block], axis=0),
        )
        step *= 2
    return block


def dp_sum(values):
    count = lax.axis_size("dp")
    index = lax.axis_index("dp")
    step = 1
    while step < count:
        other = lax.ppermute(values, "dp", [(i, i ^ step) for i in range(count)])
        values = jnp.where((index & step) == 0, values + other, other + values)
        step *= 2
    return values


def own_rows(values, head, rows):
    return lax.dynamic_slice_in_dim(values, head * rows, rows, 1)


def head_sum(part):
    return part + swap_heads(part)


def head_sum_low(part):
    low = part.astype(jnp.bfloat16)
    return low.astype(jnp.float32) + swap_heads(low).astype(jnp.float32)


def trade_blocks(values, head, size, axis, mine_axis):
    mine = lax.dynamic_slice_in_dim(values, head * size, size, axis)
    theirs = swap_heads(lax.dynamic_slice_in_dim(values, (1 - head) * size, size, axis))
    return jnp.where(
        head == 0,
        jnp.concatenate([mine, theirs], axis=mine_axis),
        jnp.concatenate([theirs, mine], axis=mine_axis),
    )


def attn_scores(queries, keys, biases, valid):
    scores = jnp.einsum("cqhe,ckhe->chqk", queries, keys, preferred_element_type=jnp.float32)
    scores = scores * DH ** (-0.5) + biases.astype(jnp.float32)
    return jnp.where(valid[:, None, None, :], scores, masked_score)


def to_chunks(values, parts):
    return values.reshape(parts, -1, LANES)


def shards(
    layer_input,
    pair_input,
    time_cond,
    chain_lengths,
    residue_mask,
    mod_weight,
    mod_bias,
    qkv_weight,
    pair_gain,
    pair_weight,
    out_weight,
    out_bias,
    gate_up_weight,
    down_weight,
    output_grad,
):
    assert layer_input.shape[0] == 1
    rows = layer_input.shape[1]
    width = layer_input.shape[2]
    length = residue_mask.shape[1]
    head = lax.axis_index("head")
    first = head == 0
    data_count = lax.axis_size("dp")
    proj = qkv_weight.shape[2]
    ffn = gate_up_weight.shape[2]
    qkv_w = qkv_weight.reshape(width, 3 * proj)
    gate_up_w = gate_up_weight.reshape(width, 2 * ffn)

    x_rows = whole_rows(layer_input[0], first)
    g_rows = whole_rows(output_grad[0], first)
    out_weight_all = whole_rows(out_weight, first)

    positions = jnp.arange(length, dtype=jnp.int32)
    valid = (positions < chain_lengths[0]) & ((residue_mask[0] == 1) | (positions == 0))
    silu_cond = jax.nn.silu(time_cond).astype(jnp.bfloat16)
    modulation = jnp.dot(silu_cond, mod_weight, preferred_element_type=jnp.float32) + mod_bias
    scale_a, shift_a, gate_a, scale_t, shift_t, gate_t = [
        modulation[:, section * width : (section + 1) * width] for section in range(6)
    ]

    heads_all = pair_weight.shape[1]
    pair_width = pair_input.shape[-1]
    pair_flat = pair_input.reshape(-1, pair_width)
    pair_wt = jnp.pad(pair_weight.T, ((0, HEAD_PAD - heads_all), (0, 0)))
    pair_gain_row = pair_gain.reshape(1, pair_width)
    bias_flat = pair_forward(pair_flat, pair_gain_row, pair_wt, heads_all)
    bias_rows = bias_flat.reshape(heads_all, rows, length)
    heads_own = proj // DH
    biases = trade_blocks(bias_rows, head, heads_own, 0, 1)

    residues = x_rows.astype(jnp.float32)
    norm_in, inv_in = layer_norm(residues)
    normed_a = (norm_in * (1.0 + scale_a) + shift_a).astype(jnp.bfloat16)
    projected = jnp.dot(normed_a, qkv_w, preferred_element_type=jnp.float32).astype(jnp.bfloat16)
    queries = head_split(projected[:, :proj])
    keys = head_split(projected[:, proj : 2 * proj])
    values = head_split(projected[:, 2 * proj :])
    scores = jnp.einsum("qhe,khe->hqk", queries, keys, preferred_element_type=jnp.float32)
    scores = scores * DH ** (-0.5) + biases.astype(jnp.float32)
    scores = jnp.where(valid[None, None, :], scores, masked_score)
    row_max = jnp.max(scores, axis=-1, keepdims=True)
    exp_scores = jnp.exp(scores - row_max)
    row_total = jnp.sum(exp_scores, axis=-1, keepdims=True)
    attn_probs = exp_scores / row_total
    probs_low = attn_probs.astype(jnp.bfloat16)
    mixed = jnp.einsum("hqk,khe->qhe", probs_low, values, preferred_element_type=jnp.float32)
    mixed = mixed.reshape(length, proj).astype(jnp.bfloat16)
    mixed_all = jnp.where(
        first,
        jnp.concatenate([mixed, swap_heads(mixed)], axis=1),
        jnp.concatenate([swap_heads(mixed), mixed], axis=1),
    )
    attn_branch = jnp.dot(mixed_all, out_weight_all, preferred_element_type=jnp.float32) + out_bias
    sig_a = jax.nn.sigmoid(gate_a)
    middle = residues + sig_a * attn_branch

    norm_mid, inv_mid = layer_norm(middle)
    normed_t = (norm_mid * (1.0 + scale_t) + shift_t).astype(jnp.bfloat16)
    gate_up = jnp.dot(normed_t, gate_up_w, preferred_element_type=jnp.float32)
    gate_pre = gate_up[:, :ffn]
    up_pre = gate_up[:, ffn:]
    hidden = (jax.nn.silu(gate_pre) * up_pre).astype(jnp.bfloat16)
    ffn_part = jnp.dot(hidden, down_weight, preferred_element_type=jnp.float32).astype(jnp.bfloat16)
    ffn_branch = ffn_part.astype(jnp.float32) + swap_heads(ffn_part).astype(jnp.float32)
    sig_t = jax.nn.sigmoid(gate_t)
    layer_output = own_rows((middle + sig_t * ffn_branch).astype(jnp.bfloat16)[None], head, rows)

    grad_out = g_rows.astype(jnp.float32)
    d_ffn = (grad_out * sig_t).astype(jnp.bfloat16)
    d_gate_t = jnp.sum(grad_out * ffn_branch * sig_t * (1.0 - sig_t), axis=0, keepdims=True)
    down_grad_t = lax.dot_general(
        d_ffn, hidden, (((0,), (0,)), ((), ())), preferred_element_type=jnp.float32
    )
    d_hidden = lax.dot_general(
        d_ffn, down_weight, (((1,), (1,)), ((), ())), preferred_element_type=jnp.float32
    )
    d_gate = d_hidden * up_pre * silu_slope(gate_pre)
    d_up = d_hidden * jax.nn.silu(gate_pre)
    d_gate_up = jnp.concatenate([d_gate, d_up], axis=1).astype(jnp.bfloat16)
    gate_up_grad = lax.dot_general(
        normed_t, d_gate_up, (((0,), (0,)), ((), ())), preferred_element_type=jnp.float32
    )
    ffn_in_part = lax.dot_general(
        d_gate_up, gate_up_w, (((1,), (1,)), ((), ())), preferred_element_type=jnp.float32
    )
    d_normed_t = head_sum_low(ffn_in_part)
    d_middle = grad_out + norm_back(norm_mid, inv_mid, d_normed_t * (1.0 + scale_t))
    d_scale_t = jnp.sum(d_normed_t * norm_mid, axis=0, keepdims=True)
    d_shift_t = jnp.sum(d_normed_t, axis=0, keepdims=True)
    d_attn = d_middle * sig_a
    d_gate_a = jnp.sum(d_middle * attn_branch * sig_a * (1.0 - sig_a), axis=0, keepdims=True)
    d_out_bias = jnp.sum(d_attn, axis=0, keepdims=True)
    d_attn_low = d_attn.astype(jnp.bfloat16)

    out_weight_grad_t = lax.dot_general(
        d_attn_low, mixed, (((0,), (0,)), ((), ())), preferred_element_type=jnp.float32
    )
    d_mixed = head_split(
        lax.dot_general(
            d_attn_low, out_weight, (((1,), (1,)), ((), ())), preferred_element_type=jnp.float32
        ).astype(jnp.bfloat16)
    )
    d_values = jnp.einsum("hqk,qhe->khe", probs_low, d_mixed, preferred_element_type=jnp.float32)
    d_probs = jnp.einsum("qhe,khe->hqk", d_mixed, values, preferred_element_type=jnp.float32)
    d_scores = (
        attn_probs * (d_probs - jnp.sum(d_probs * attn_probs, axis=-1, keepdims=True))
    ).astype(jnp.bfloat16)
    d_queries = jnp.einsum(
        "hqk,khe->qhe", d_scores, keys, preferred_element_type=jnp.float32
    ) * DH ** (-0.5)
    d_keys = jnp.einsum(
        "hqk,qhe->khe", d_scores, queries, preferred_element_type=jnp.float32
    ) * DH ** (-0.5)
    d_qkv = jnp.concatenate(
        [d_queries.reshape(length, proj), d_keys.reshape(length, proj), d_values.reshape(length, proj)],
        axis=1,
    ).astype(jnp.bfloat16)
    qkv_grad = lax.dot_general(
        normed_a, d_qkv, (((0,), (0,)), ((), ())), preferred_element_type=jnp.float32
    )

    packed = lax.optimization_barrier(jnp.zeros((width, 4 * proj + 3 * ffn), jnp.bfloat16))
    packed = lax.dynamic_update_slice(packed, gate_up_grad.astype(jnp.bfloat16), (0, 4 * proj))
    packed = lax.dynamic_update_slice(
        packed, down_grad_t.astype(jnp.bfloat16), (0, 4 * proj + 2 * ffn)
    )
    packed = lax.dynamic_update_slice(packed, out_weight_grad_t.astype(jnp.bfloat16), (0, 3 * proj))
    packed = lax.dynamic_update_slice(packed, qkv_grad.astype(jnp.bfloat16), (0, 0))
    reduced = lax.psum_scatter(packed, "dp", scatter_dimension=0, tiled=True).astype(jnp.float32)

    attn_in_part = lax.dot_general(
        d_qkv, qkv_w, (((1,), (1,)), ((), ())), preferred_element_type=jnp.float32
    ).astype(jnp.bfloat16)
    d_normed_a = attn_in_part.astype(jnp.float32) + swap_heads(attn_in_part).astype(jnp.float32)
    input_grad = own_rows(
        (d_middle + norm_back(norm_in, inv_in, d_normed_a * (1.0 + scale_a)))[None], head, rows
    )
    d_scale_a = jnp.sum(d_normed_a * norm_in, axis=0, keepdims=True)
    d_shift_a = jnp.sum(d_normed_a, axis=0, keepdims=True)
    d_modulation = jnp.concatenate(
        [d_scale_a, d_shift_a, d_gate_a, d_scale_t, d_shift_t, d_gate_t], axis=-1
    )

    d_bias_rows = trade_blocks(d_scores, head, rows, 1, 0)
    d_bias_flat = jnp.pad(d_bias_rows.reshape(heads_all, -1), ((0, HEAD_PAD - heads_all), (0, 0)))
    pair_grad, pair_wg, pair_gg = pair_backward(pair_flat, d_bias_flat, pair_gain_row, pair_wt)
    pair_grad = pair_grad.reshape(pair_input.shape)
    pair_weight_grad = pair_wg[:heads_all].T
    pair_gain_grad = pair_gg[0]

    pair_small = head_sum(
        jnp.concatenate([pair_weight_grad.reshape(-1), pair_gain_grad])[None]
    )
    small = jnp.concatenate([d_modulation, time_cond, d_out_bias], axis=-1)
    small_rows = dp_gather(small)
    mod_size = d_modulation.shape[-1]
    cond_size = time_cond.shape[-1]
    pw_size = pair_weight.size
    mod_chain = small_rows[:, :mod_size]
    cond_chain = small_rows[:, mod_size : mod_size + cond_size]
    out_bias_grad = jnp.sum(small_rows[:, mod_size + cond_size :], axis=0)
    pair_total = dp_sum(pair_small)[0]
    pair_weight_grad = pair_total[:pw_size].reshape(pair_weight.shape)
    pair_gain_grad = pair_total[pw_size:]
    cond_act = lax.optimization_barrier(jax.nn.silu(cond_chain).astype(jnp.bfloat16)).astype(
        jnp.float32
    )
    mod_weight_grad = jnp.dot(cond_act.T, mod_chain, precision=precise)
    mod_bias_grad = jnp.sum(mod_chain, axis=0)
    cond_grad = jnp.dot(
        d_modulation, mod_weight.astype(jnp.float32).T, precision=precise
    ) * silu_slope(time_cond)

    cuts = [0, 3 * proj, 4 * proj, 4 * proj + 2 * ffn, 4 * proj + 3 * ffn]
    pieces = [reduced[:, cuts[i] : cuts[i + 1]] for i in range(4)]
    qkv_grad = pieces[0].reshape(-1, 3, proj)
    out_weight_grad = pieces[1].T
    gate_up_grad = pieces[2].reshape(-1, 2, ffn)
    down_grad = pieces[3].T
    return (
        layer_output,
        input_grad,
        pair_grad,
        cond_grad,
        mod_weight_grad,
        mod_bias_grad,
        qkv_grad,
        pair_gain_grad,
        pair_weight_grad,
        out_weight_grad,
        out_bias_grad,
        gate_up_grad,
        down_grad,
    )


def solution(mesh):
    placed = (
        P("dp", "head", None),
        P("dp", "head", None, None),
        P("dp", None),
        P("dp"),
        P("dp", None),
        P(),
        P(),
        P(None, None, "head"),
        P(),
        P(),
        P("head", None),
        P(),
        P(None, None, "head"),
        P("head", None),
        P("dp", "head", None),
    )
    return jax.shard_map(
        shards,
        mesh=mesh,
        in_specs=placed,
        out_specs=(
            P("dp", "head", None),
            P("dp", "head", None),
            P("dp", "head", None, None),
            P("dp", None),
            P(),
            P(),
            P("dp", None, "head"),
            P(),
            P(),
            P("head", "dp"),
            P(),
            P("dp", None, "head"),
            P("head", "dp"),
        ),
        check_vma=False,
    )
```

```python
import jax
import jax.numpy as jnp
from jax import lax
from jax.experimental import pallas as pl
from jax.experimental.pallas import tpu as pltpu
from jax.experimental.layout import Layout, with_layout_constraint
from jax.sharding import PartitionSpec as P

DH = 64


epsilon = 1e-05
masked_score = -1000000000.0
precise = lax.Precision.HIGHEST
LANES = 128
PAIR_TILE = 4096
PAIR_BACK_TILE = 2048
HEAD_PAD = 16


def pair_stats(x):
    centred = x - jnp.mean(x, axis=-1, keepdims=True)
    inv_std = lax.rsqrt(jnp.mean(centred * centred, axis=-1, keepdims=True) + epsilon)
    return centred * inv_std, inv_std


def pair_forward_kernel(x_ref, gain_ref, wt_ref, bias_ref):
    normed, _ = pair_stats(x_ref[...].astype(jnp.float32))
    scaled = (normed * gain_ref[...]).astype(jnp.bfloat16)
    bias = lax.dot_general(
        wt_ref[...], scaled, (((1,), (1,)), ((), ())), preferred_element_type=jnp.float32
    )
    bias_ref[...] = bias[: bias_ref.shape[0]].astype(bias_ref.dtype)


def pair_forward(flat, gain, wt, heads):
    m, width = flat.shape
    tile = min(PAIR_TILE, m)
    return pl.pallas_call(
        pair_forward_kernel,
        grid=(m // tile,),
        in_specs=[
            pl.BlockSpec((tile, width), lambda i: (i, 0)),
            pl.BlockSpec((1, width), lambda i: (0, 0)),
            pl.BlockSpec(wt.shape, lambda i: (0, 0)),
        ],
        out_specs=pl.BlockSpec((heads, tile), lambda i: (0, i)),
        out_shape=jax.ShapeDtypeStruct((heads, m), jnp.bfloat16),
        cost_estimate=pl.CostEstimate(
            flops=m * width * (2 * HEAD_PAD + 10),
            transcendentals=m,
            bytes_accessed=m * width * 2 + heads * m * 2,
        ),
    )(flat, gain, wt)


def pair_backward_kernel(x_ref, ds_ref, gain_ref, wt_ref, grad_ref, wg_ref, gg_ref):
    step = pl.program_id(0)
    normed, inv_std = pair_stats(x_ref[...].astype(jnp.float32))
    gain = gain_ref[...]
    scaled = (normed * gain).astype(jnp.bfloat16)
    ds = ds_ref[...]
    d_scaled = lax.dot_general(
        ds, wt_ref[...], (((0,), (0,)), ((), ())), preferred_element_type=jnp.float32
    )
    wg = lax.dot_general(ds, scaled, (((1,), (0,)), ((), ())), preferred_element_type=jnp.float32)
    gg = jnp.sum(d_scaled * normed, axis=0, keepdims=True)
    d_normed = d_scaled * gain
    mean_grad = jnp.mean(d_normed, axis=-1, keepdims=True)
    mean_proj = jnp.mean(d_normed * normed, axis=-1, keepdims=True)
    grad_ref[...] = (inv_std * (d_normed - mean_grad - normed * mean_proj)).astype(grad_ref.dtype)

    @pl.when(step == 0)
    def _():
        wg_ref[...] = jnp.zeros_like(wg_ref)
        gg_ref[...] = jnp.zeros_like(gg_ref)

    wg_ref[...] += wg
    gg_ref[...] += gg


def pair_backward(flat, ds, gain, wt):
    m, width = flat.shape
    tile = min(PAIR_BACK_TILE, m)
    pad = ds.shape[0]
    return pl.pallas_call(
        pair_backward_kernel,
        grid=(m // tile,),
        in_specs=[
            pl.BlockSpec((tile, width), lambda i: (i, 0)),
            pl.BlockSpec((pad, tile), lambda i: (0, i)),
            pl.BlockSpec((1, width), lambda i: (0, 0)),
            pl.BlockSpec(wt.shape, lambda i: (0, 0)),
        ],
        out_specs=[
            pl.BlockSpec((tile, width), lambda i: (i, 0)),
            pl.BlockSpec((pad, width), lambda i: (0, 0)),
            pl.BlockSpec((1, width), lambda i: (0, 0)),
        ],
        out_shape=[
            jax.ShapeDtypeStruct((m, width), jnp.bfloat16),
            jax.ShapeDtypeStruct((pad, width), jnp.float32),
            jax.ShapeDtypeStruct((1, width), jnp.float32),
        ],
        compiler_params=pltpu.CompilerParams(dimension_semantics=("arbitrary",)),
        cost_estimate=pl.CostEstimate(
            flops=m * width * (4 * HEAD_PAD + 20),
            transcendentals=m,
            bytes_accessed=2 * m * width * 2 + pad * m * 2,
        ),
    )(flat, ds, gain, wt)


def layer_norm(values):
    centred = values - jnp.mean(values, axis=-1, keepdims=True)
    inv_std = lax.rsqrt(jnp.mean(centred * centred, axis=-1, keepdims=True) + epsilon)
    return (centred * inv_std, inv_std)


def norm_back(normed, inv_std, grad):
    mean_grad = jnp.mean(grad, axis=-1, keepdims=True)
    mean_proj = jnp.mean(grad * normed, axis=-1, keepdims=True)
    return inv_std * (grad - mean_grad - normed * mean_proj)


def silu_slope(values):
    sigma = jax.nn.sigmoid(values)
    return sigma * (1.0 + values * (1.0 - sigma))


def head_split(values):
    return values.reshape(values.shape[:-1] + (values.shape[-1] // DH, DH))


def swap_heads(values):
    return lax.ppermute(values, "head", [(0, 1), (1, 0)])


def whole_rows(own, first):
    other = swap_heads(own)
    return jnp.where(
        first,
        jnp.concatenate([own, other], axis=0),
        jnp.concatenate([other, own], axis=0),
    )


def dp_gather(values):
    count = lax.axis_size("dp")
    index = lax.axis_index("dp")
    block = values
    step = 1
    while step < count:
        other = lax.ppermute(block, "dp", [(i, i ^ step) for i in range(count)])
        block = jnp.where(
            (index & step) == 0,
            jnp.concatenate([block, other], axis=0),
            jnp.concatenate([other, block], axis=0),
        )
        step *= 2
    return block


def dp_sum(values):
    count = lax.axis_size("dp")
    index = lax.axis_index("dp")
    step = 1
    while step < count:
        other = lax.ppermute(values, "dp", [(i, i ^ step) for i in range(count)])
        values = jnp.where((index & step) == 0, values + other, other + values)
        step *= 2
    return values


def own_rows(values, head, rows):
    return lax.dynamic_slice_in_dim(values, head * rows, rows, 1)


def head_sum(part):
    return part + swap_heads(part)


def head_sum_low(part):
    low = part.astype(jnp.bfloat16)
    return low.astype(jnp.float32) + swap_heads(low).astype(jnp.float32)


def trade_blocks(values, head, size, axis, mine_axis):
    mine = lax.dynamic_slice_in_dim(values, head * size, size, axis)
    theirs = swap_heads(lax.dynamic_slice_in_dim(values, (1 - head) * size, size, axis))
    return jnp.where(
        head == 0,
        jnp.concatenate([mine, theirs], axis=mine_axis),
        jnp.concatenate([theirs, mine], axis=mine_axis),
    )


def attn_scores(queries, keys, biases, valid):
    scores = jnp.einsum("cqhe,ckhe->chqk", queries, keys, preferred_element_type=jnp.float32)
    scores = scores * DH ** (-0.5) + biases.astype(jnp.float32)
    return jnp.where(valid[:, None, None, :], scores, masked_score)


def to_chunks(values, parts):
    return values.reshape(parts, -1, LANES)


def shards(
    layer_input,
    pair_input,
    time_cond,
    chain_lengths,
    residue_mask,
    mod_weight,
    mod_bias,
    qkv_weight,
    pair_gain,
    pair_weight,
    out_weight,
    out_bias,
    gate_up_weight,
    down_weight,
    output_grad,
):
    assert layer_input.shape[0] == 1
    rows = layer_input.shape[1]
    width = layer_input.shape[2]
    length = residue_mask.shape[1]
    head = lax.axis_index("head")
    first = head == 0
    data_count = lax.axis_size("dp")
    proj = qkv_weight.shape[2]
    ffn = gate_up_weight.shape[2]
    qkv_w = qkv_weight.reshape(width, 3 * proj)
    gate_up_w = gate_up_weight.reshape(width, 2 * ffn)

    x_rows = whole_rows(layer_input[0], first)
    g_rows = whole_rows(output_grad[0], first)
    out_weight_all = whole_rows(out_weight, first)

    positions = jnp.arange(length, dtype=jnp.int32)
    valid = (positions < chain_lengths[0]) & ((residue_mask[0] == 1) | (positions == 0))
    silu_cond = jax.nn.silu(time_cond).astype(jnp.bfloat16)
    modulation = jnp.dot(silu_cond, mod_weight, preferred_element_type=jnp.float32) + mod_bias
    scale_a, shift_a, gate_a, scale_t, shift_t, gate_t = [
        modulation[:, section * width : (section + 1) * width] for section in range(6)
    ]

    heads_all = pair_weight.shape[1]
    pair_width = pair_input.shape[-1]
    pair_flat = pair_input.reshape(-1, pair_width)
    pair_wt = jnp.pad(pair_weight.T, ((0, HEAD_PAD - heads_all), (0, 0)))
    pair_gain_row = pair_gain.reshape(1, pair_width)
    bias_flat = pair_forward(pair_flat, pair_gain_row, pair_wt, heads_all)
    bias_rows = bias_flat.reshape(heads_all, rows, length)
    heads_own = proj // DH
    biases = trade_blocks(bias_rows, head, heads_own, 0, 1)

    residues = x_rows.astype(jnp.float32)
    norm_in, inv_in = layer_norm(residues)
    normed_a = (norm_in * (1.0 + scale_a) + shift_a).astype(jnp.bfloat16)
    projected = jnp.dot(normed_a, qkv_w, preferred_element_type=jnp.float32).astype(jnp.bfloat16)
    queries = head_split(projected[:, :proj])
    keys = head_split(projected[:, proj : 2 * proj])
    values = head_split(projected[:, 2 * proj :])
    scores = jnp.einsum("qhe,khe->hqk", queries, keys, preferred_element_type=jnp.float32)
    scores = scores * DH ** (-0.5) + biases.astype(jnp.float32)
    scores = jnp.where(valid[None, None, :], scores, masked_score)
    scores = with_layout_constraint(scores, Layout(major_to_minor=(0, 1, 2)))
    row_max = jnp.max(scores, axis=-1, keepdims=True)
    exp_scores = jnp.exp(scores - row_max)
    row_total = jnp.sum(exp_scores, axis=-1, keepdims=True)
    attn_probs = exp_scores / row_total
    probs_low = attn_probs.astype(jnp.bfloat16)
    mixed = jnp.einsum("hqk,khe->qhe", probs_low, values, preferred_element_type=jnp.float32)
    mixed = mixed.reshape(length, proj).astype(jnp.bfloat16)
    mixed_all = jnp.where(
        first,
        jnp.concatenate([mixed, swap_heads(mixed)], axis=1),
        jnp.concatenate([swap_heads(mixed), mixed], axis=1),
    )
    attn_branch = jnp.dot(mixed_all, out_weight_all, preferred_element_type=jnp.float32) + out_bias
    sig_a = jax.nn.sigmoid(gate_a)
    middle = residues + sig_a * attn_branch

    norm_mid, inv_mid = layer_norm(middle)
    normed_t = (norm_mid * (1.0 + scale_t) + shift_t).astype(jnp.bfloat16)
    gate_up = jnp.dot(normed_t, gate_up_w, preferred_element_type=jnp.float32)
    gate_pre = gate_up[:, :ffn]
    up_pre = gate_up[:, ffn:]
    hidden = (jax.nn.silu(gate_pre) * up_pre).astype(jnp.bfloat16)
    ffn_part = jnp.dot(hidden, down_weight, preferred_element_type=jnp.float32).astype(jnp.bfloat16)
    ffn_branch = ffn_part.astype(jnp.float32) + swap_heads(ffn_part).astype(jnp.float32)
    sig_t = jax.nn.sigmoid(gate_t)
    layer_output = own_rows((middle + sig_t * ffn_branch).astype(jnp.bfloat16)[None], head, rows)

    grad_out = g_rows.astype(jnp.float32)
    d_ffn = (grad_out * sig_t).astype(jnp.bfloat16)
    d_gate_t = jnp.sum(grad_out * ffn_branch * sig_t * (1.0 - sig_t), axis=0, keepdims=True)
    down_grad_t = lax.dot_general(
        d_ffn, hidden, (((0,), (0,)), ((), ())), preferred_element_type=jnp.float32
    )
    d_hidden = lax.dot_general(
        d_ffn, down_weight, (((1,), (1,)), ((), ())), preferred_element_type=jnp.float32
    )
    d_gate = d_hidden * up_pre * silu_slope(gate_pre)
    d_up = d_hidden * jax.nn.silu(gate_pre)
    d_gate_up = jnp.concatenate([d_gate, d_up], axis=1).astype(jnp.bfloat16)
    gate_up_grad = lax.dot_general(
        normed_t, d_gate_up, (((0,), (0,)), ((), ())), preferred_element_type=jnp.float32
    )
    ffn_in_part = lax.dot_general(
        d_gate_up, gate_up_w, (((1,), (1,)), ((), ())), preferred_element_type=jnp.float32
    )
    d_normed_t = head_sum_low(ffn_in_part)
    d_middle = grad_out + norm_back(norm_mid, inv_mid, d_normed_t * (1.0 + scale_t))
    d_scale_t = jnp.sum(d_normed_t * norm_mid, axis=0, keepdims=True)
    d_shift_t = jnp.sum(d_normed_t, axis=0, keepdims=True)
    d_attn = d_middle * sig_a
    d_gate_a = jnp.sum(d_middle * attn_branch * sig_a * (1.0 - sig_a), axis=0, keepdims=True)
    d_out_bias = jnp.sum(d_attn, axis=0, keepdims=True)
    d_attn_low = d_attn.astype(jnp.bfloat16)

    out_weight_grad_t = lax.dot_general(
        d_attn_low, mixed, (((0,), (0,)), ((), ())), preferred_element_type=jnp.float32
    )
    d_mixed = head_split(
        lax.dot_general(
            d_attn_low, out_weight, (((1,), (1,)), ((), ())), preferred_element_type=jnp.float32
        ).astype(jnp.bfloat16)
    )
    d_values = jnp.einsum("hqk,qhe->khe", probs_low, d_mixed, preferred_element_type=jnp.float32)
    d_probs = jnp.einsum("qhe,khe->hqk", d_mixed, values, preferred_element_type=jnp.float32)
    d_scores = (
        attn_probs * (d_probs - jnp.sum(d_probs * attn_probs, axis=-1, keepdims=True))
    ).astype(jnp.bfloat16)
    d_queries = jnp.einsum(
        "hqk,khe->qhe", d_scores, keys, preferred_element_type=jnp.float32
    ) * DH ** (-0.5)
    d_keys = jnp.einsum(
        "hqk,qhe->khe", d_scores, queries, preferred_element_type=jnp.float32
    ) * DH ** (-0.5)
    d_qkv = jnp.concatenate(
        [d_queries.reshape(length, proj), d_keys.reshape(length, proj), d_values.reshape(length, proj)],
        axis=1,
    ).astype(jnp.bfloat16)
    qkv_grad = lax.dot_general(
        normed_a, d_qkv, (((0,), (0,)), ((), ())), preferred_element_type=jnp.float32
    )

    packed = lax.optimization_barrier(jnp.zeros((width, 4 * proj + 3 * ffn), jnp.bfloat16))
    packed = lax.dynamic_update_slice(packed, gate_up_grad.astype(jnp.bfloat16), (0, 4 * proj))
    packed = lax.dynamic_update_slice(
        packed, down_grad_t.astype(jnp.bfloat16), (0, 4 * proj + 2 * ffn)
    )
    packed = lax.dynamic_update_slice(packed, out_weight_grad_t.astype(jnp.bfloat16), (0, 3 * proj))
    packed = lax.dynamic_update_slice(packed, qkv_grad.astype(jnp.bfloat16), (0, 0))
    reduced = lax.psum_scatter(packed, "dp", scatter_dimension=0, tiled=True).astype(jnp.float32)

    attn_in_part = lax.dot_general(
        d_qkv, qkv_w, (((1,), (1,)), ((), ())), preferred_element_type=jnp.float32
    ).astype(jnp.bfloat16)
    d_normed_a = attn_in_part.astype(jnp.float32) + swap_heads(attn_in_part).astype(jnp.float32)
    input_grad = own_rows(
        (d_middle + norm_back(norm_in, inv_in, d_normed_a * (1.0 + scale_a)))[None], head, rows
    )
    d_scale_a = jnp.sum(d_normed_a * norm_in, axis=0, keepdims=True)
    d_shift_a = jnp.sum(d_normed_a, axis=0, keepdims=True)
    d_modulation = jnp.concatenate(
        [d_scale_a, d_shift_a, d_gate_a, d_scale_t, d_shift_t, d_gate_t], axis=-1
    )

    d_bias_rows = trade_blocks(d_scores, head, rows, 1, 0)
    d_bias_flat = jnp.pad(d_bias_rows.reshape(heads_all, -1), ((0, HEAD_PAD - heads_all), (0, 0)))
    pair_grad, pair_wg, pair_gg = pair_backward(pair_flat, d_bias_flat, pair_gain_row, pair_wt)
    pair_grad = pair_grad.reshape(pair_input.shape)
    pair_weight_grad = pair_wg[:heads_all].T
    pair_gain_grad = pair_gg[0]

    pair_small = head_sum(
        jnp.concatenate([pair_weight_grad.reshape(-1), pair_gain_grad])[None]
    )
    small = jnp.concatenate([d_modulation, time_cond, d_out_bias], axis=-1)
    small_rows = dp_gather(small)
    mod_size = d_modulation.shape[-1]
    cond_size = time_cond.shape[-1]
    pw_size = pair_weight.size
    mod_chain = small_rows[:, :mod_size]
    cond_chain = small_rows[:, mod_size : mod_size + cond_size]
    out_bias_grad = jnp.sum(small_rows[:, mod_size + cond_size :], axis=0)
    pair_total = dp_sum(pair_small)[0]
    pair_weight_grad = pair_total[:pw_size].reshape(pair_weight.shape)
    pair_gain_grad = pair_total[pw_size:]
    cond_act = lax.optimization_barrier(jax.nn.silu(cond_chain).astype(jnp.bfloat16)).astype(
        jnp.float32
    )
    mod_weight_grad = jnp.dot(cond_act.T, mod_chain, precision=precise)
    mod_bias_grad = jnp.sum(mod_chain, axis=0)
    cond_grad = jnp.dot(
        d_modulation, mod_weight.astype(jnp.float32).T, precision=precise
    ) * silu_slope(time_cond)

    cuts = [0, 3 * proj, 4 * proj, 4 * proj + 2 * ffn, 4 * proj + 3 * ffn]
    pieces = [reduced[:, cuts[i] : cuts[i + 1]] for i in range(4)]
    qkv_grad = pieces[0].reshape(-1, 3, proj)
    out_weight_grad = pieces[1].T
    gate_up_grad = pieces[2].reshape(-1, 2, ffn)
    down_grad = pieces[3].T
    return (
        layer_output,
        input_grad,
        pair_grad,
        cond_grad,
        mod_weight_grad,
        mod_bias_grad,
        qkv_grad,
        pair_gain_grad,
        pair_weight_grad,
        out_weight_grad,
        out_bias_grad,
        gate_up_grad,
        down_grad,
    )


def solution(mesh):
    placed = (
        P("dp", "head", None),
        P("dp", "head", None, None),
        P("dp", None),
        P("dp"),
        P("dp", None),
        P(),
        P(),
        P(None, None, "head"),
        P(),
        P(),
        P("head", None),
        P(),
        P(None, None, "head"),
        P("head", None),
        P("dp", "head", None),
    )
    return jax.shard_map(
        shards,
        mesh=mesh,
        in_specs=placed,
        out_specs=(
            P("dp", "head", None),
            P("dp", "head", None),
            P("dp", "head", None, None),
            P("dp", None),
            P(),
            P(),
            P("dp", None, "head"),
            P(),
            P(),
            P("head", "dp"),
            P(),
            P("dp", None, "head"),
            P("head", "dp"),
        ),
        check_vma=False,
    )
```

```python
import jax
import jax.numpy as jnp
from jax import lax
from jax.experimental import pallas as pl
from jax.experimental.pallas import tpu as pltpu
from jax.sharding import PartitionSpec as P

DH = 64


epsilon = 1e-05
masked_score = -1000000000.0
precise = lax.Precision.HIGHEST
LANES = 128
PAIR_TILE = 4096
PAIR_BACK_TILE = 2048
HEAD_PAD = 16


def blank_kernel(out_ref):
    del out_ref


def blank(shape, dtype):
    return pl.pallas_call(
        blank_kernel,
        out_shape=jax.ShapeDtypeStruct(shape, dtype),
        out_specs=pl.BlockSpec(memory_space=pl.ANY),
    )()


def pair_stats(x):
    centred = x - jnp.mean(x, axis=-1, keepdims=True)
    inv_std = lax.rsqrt(jnp.mean(centred * centred, axis=-1, keepdims=True) + epsilon)
    return centred * inv_std, inv_std


def pair_forward_kernel(x_ref, gain_ref, wt_ref, bias_ref):
    normed, _ = pair_stats(x_ref[...].astype(jnp.float32))
    scaled = (normed * gain_ref[...]).astype(jnp.bfloat16)
    bias = lax.dot_general(
        wt_ref[...], scaled, (((1,), (1,)), ((), ())), preferred_element_type=jnp.float32
    )
    bias_ref[...] = bias[: bias_ref.shape[0]].astype(bias_ref.dtype)


def pair_forward(flat, gain, wt, heads):
    m, width = flat.shape
    tile = min(PAIR_TILE, m)
    return pl.pallas_call(
        pair_forward_kernel,
        grid=(m // tile,),
        in_specs=[
            pl.BlockSpec((tile, width), lambda i: (i, 0)),
            pl.BlockSpec((1, width), lambda i: (0, 0)),
            pl.BlockSpec(wt.shape, lambda i: (0, 0)),
        ],
        out_specs=pl.BlockSpec((heads, tile), lambda i: (0, i)),
        out_shape=jax.ShapeDtypeStruct((heads, m), jnp.bfloat16),
        cost_estimate=pl.CostEstimate(
            flops=m * width * (2 * HEAD_PAD + 10),
            transcendentals=m,
            bytes_accessed=m * width * 2 + heads * m * 2,
        ),
    )(flat, gain, wt)


def pair_backward_kernel(x_ref, ds_ref, gain_ref, wt_ref, grad_ref, wg_ref, gg_ref):
    step = pl.program_id(0)
    normed, inv_std = pair_stats(x_ref[...].astype(jnp.float32))
    gain = gain_ref[...]
    scaled = (normed * gain).astype(jnp.bfloat16)
    ds = ds_ref[...]
    d_scaled = lax.dot_general(
        ds, wt_ref[...], (((0,), (0,)), ((), ())), preferred_element_type=jnp.float32
    )
    wg = lax.dot_general(ds, scaled, (((1,), (0,)), ((), ())), preferred_element_type=jnp.float32)
    gg = jnp.sum(d_scaled * normed, axis=0, keepdims=True)
    d_normed = d_scaled * gain
    mean_grad = jnp.mean(d_normed, axis=-1, keepdims=True)
    mean_proj = jnp.mean(d_normed * normed, axis=-1, keepdims=True)
    grad_ref[...] = (inv_std * (d_normed - mean_grad - normed * mean_proj)).astype(grad_ref.dtype)

    @pl.when(step == 0)
    def _():
        wg_ref[...] = jnp.zeros_like(wg_ref)
        gg_ref[...] = jnp.zeros_like(gg_ref)

    wg_ref[...] += wg
    gg_ref[...] += gg


def pair_backward(flat, ds, gain, wt):
    m, width = flat.shape
    tile = min(PAIR_BACK_TILE, m)
    pad = ds.shape[0]
    return pl.pallas_call(
        pair_backward_kernel,
        grid=(m // tile,),
        in_specs=[
            pl.BlockSpec((tile, width), lambda i: (i, 0)),
            pl.BlockSpec((pad, tile), lambda i: (0, i)),
            pl.BlockSpec((1, width), lambda i: (0, 0)),
            pl.BlockSpec(wt.shape, lambda i: (0, 0)),
        ],
        out_specs=[
            pl.BlockSpec((tile, width), lambda i: (i, 0)),
            pl.BlockSpec((pad, width), lambda i: (0, 0)),
            pl.BlockSpec((1, width), lambda i: (0, 0)),
        ],
        out_shape=[
            jax.ShapeDtypeStruct((m, width), jnp.bfloat16),
            jax.ShapeDtypeStruct((pad, width), jnp.float32),
            jax.ShapeDtypeStruct((1, width), jnp.float32),
        ],
        compiler_params=pltpu.CompilerParams(dimension_semantics=("arbitrary",)),
        cost_estimate=pl.CostEstimate(
            flops=m * width * (4 * HEAD_PAD + 20),
            transcendentals=m,
            bytes_accessed=2 * m * width * 2 + pad * m * 2,
        ),
    )(flat, ds, gain, wt)


def layer_norm(values):
    centred = values - jnp.mean(values, axis=-1, keepdims=True)
    inv_std = lax.rsqrt(jnp.mean(centred * centred, axis=-1, keepdims=True) + epsilon)
    return (centred * inv_std, inv_std)


def norm_back(normed, inv_std, grad):
    mean_grad = jnp.mean(grad, axis=-1, keepdims=True)
    mean_proj = jnp.mean(grad * normed, axis=-1, keepdims=True)
    return inv_std * (grad - mean_grad - normed * mean_proj)


def silu_slope(values):
    sigma = jax.nn.sigmoid(values)
    return sigma * (1.0 + values * (1.0 - sigma))


def head_split(values):
    return values.reshape(values.shape[:-1] + (values.shape[-1] // DH, DH))


def swap_heads(values):
    return lax.ppermute(values, "head", [(0, 1), (1, 0)])


def whole_rows(own, first):
    other = swap_heads(own)
    return jnp.where(
        first,
        jnp.concatenate([own, other], axis=0),
        jnp.concatenate([other, own], axis=0),
    )


def dp_gather(values):
    count = lax.axis_size("dp")
    index = lax.axis_index("dp")
    block = values
    step = 1
    while step < count:
        other = lax.ppermute(block, "dp", [(i, i ^ step) for i in range(count)])
        block = jnp.where(
            (index & step) == 0,
            jnp.concatenate([block, other], axis=0),
            jnp.concatenate([other, block], axis=0),
        )
        step *= 2
    return block


def dp_sum(values):
    count = lax.axis_size("dp")
    index = lax.axis_index("dp")
    step = 1
    while step < count:
        other = lax.ppermute(values, "dp", [(i, i ^ step) for i in range(count)])
        values = jnp.where((index & step) == 0, values + other, other + values)
        step *= 2
    return values


def own_rows(values, head, rows):
    return lax.dynamic_slice_in_dim(values, head * rows, rows, 1)


def head_sum(part):
    return part + swap_heads(part)


def head_sum_low(part):
    low = part.astype(jnp.bfloat16)
    return low.astype(jnp.float32) + swap_heads(low).astype(jnp.float32)


def trade_blocks(values, head, size, axis, mine_axis):
    mine = lax.dynamic_slice_in_dim(values, head * size, size, axis)
    theirs = swap_heads(lax.dynamic_slice_in_dim(values, (1 - head) * size, size, axis))
    return jnp.where(
        head == 0,
        jnp.concatenate([mine, theirs], axis=mine_axis),
        jnp.concatenate([theirs, mine], axis=mine_axis),
    )


def attn_scores(queries, keys, biases, valid):
    scores = jnp.einsum("cqhe,ckhe->chqk", queries, keys, preferred_element_type=jnp.float32)
    scores = scores * DH ** (-0.5) + biases.astype(jnp.float32)
    return jnp.where(valid[:, None, None, :], scores, masked_score)


def to_chunks(values, parts):
    return values.reshape(parts, -1, LANES)


def shards(
    layer_input,
    pair_input,
    time_cond,
    chain_lengths,
    residue_mask,
    mod_weight,
    mod_bias,
    qkv_weight,
    pair_gain,
    pair_weight,
    out_weight,
    out_bias,
    gate_up_weight,
    down_weight,
    output_grad,
):
    assert layer_input.shape[0] == 1
    rows = layer_input.shape[1]
    width = layer_input.shape[2]
    length = residue_mask.shape[1]
    head = lax.axis_index("head")
    first = head == 0
    data_count = lax.axis_size("dp")
    proj = qkv_weight.shape[2]
    ffn = gate_up_weight.shape[2]
    qkv_w = qkv_weight.reshape(width, 3 * proj)
    gate_up_w = gate_up_weight.reshape(width, 2 * ffn)

    x_rows = whole_rows(layer_input[0], first)
    g_rows = whole_rows(output_grad[0], first)
    out_weight_all = whole_rows(out_weight, first)

    positions = jnp.arange(length, dtype=jnp.int32)
    valid = (positions < chain_lengths[0]) & ((residue_mask[0] == 1) | (positions == 0))
    silu_cond = jax.nn.silu(time_cond).astype(jnp.bfloat16)
    modulation = jnp.dot(silu_cond, mod_weight, preferred_element_type=jnp.float32) + mod_bias
    scale_a, shift_a, gate_a, scale_t, shift_t, gate_t = [
        modulation[:, section * width : (section + 1) * width] for section in range(6)
    ]

    heads_all = pair_weight.shape[1]
    pair_width = pair_input.shape[-1]
    pair_flat = pair_input.reshape(-1, pair_width)
    pair_wt = jnp.pad(pair_weight.T, ((0, HEAD_PAD - heads_all), (0, 0)))
    pair_gain_row = pair_gain.reshape(1, pair_width)
    bias_flat = pair_forward(pair_flat, pair_gain_row, pair_wt, heads_all)
    bias_rows = bias_flat.reshape(heads_all, rows, length)
    heads_own = proj // DH
    biases = trade_blocks(bias_rows, head, heads_own, 0, 1)

    residues = x_rows.astype(jnp.float32)
    norm_in, inv_in = layer_norm(residues)
    normed_a = (norm_in * (1.0 + scale_a) + shift_a).astype(jnp.bfloat16)
    projected = jnp.dot(normed_a, qkv_w, preferred_element_type=jnp.float32).astype(jnp.bfloat16)
    queries = head_split(projected[:, :proj])
    keys = head_split(projected[:, proj : 2 * proj])
    values = head_split(projected[:, 2 * proj :])
    scores = jnp.einsum("qhe,khe->hqk", queries, keys, preferred_element_type=jnp.float32)
    scores = scores * DH ** (-0.5) + biases.astype(jnp.float32)
    scores = jnp.where(valid[None, None, :], scores, masked_score)
    row_max = jnp.max(scores, axis=-1, keepdims=True)
    exp_scores = jnp.exp(scores - row_max)
    row_total = jnp.sum(exp_scores, axis=-1, keepdims=True)
    attn_probs = exp_scores / row_total
    probs_low = attn_probs.astype(jnp.bfloat16)
    mixed = jnp.einsum("hqk,khe->qhe", probs_low, values, preferred_element_type=jnp.float32)
    mixed = mixed.reshape(length, proj).astype(jnp.bfloat16)
    mixed_all = jnp.where(
        first,
        jnp.concatenate([mixed, swap_heads(mixed)], axis=1),
        jnp.concatenate([swap_heads(mixed), mixed], axis=1),
    )
    attn_branch = jnp.dot(mixed_all, out_weight_all, preferred_element_type=jnp.float32) + out_bias
    sig_a = jax.nn.sigmoid(gate_a)
    middle = residues + sig_a * attn_branch

    norm_mid, inv_mid = layer_norm(middle)
    normed_t = (norm_mid * (1.0 + scale_t) + shift_t).astype(jnp.bfloat16)
    gate_up = jnp.dot(normed_t, gate_up_w, preferred_element_type=jnp.float32)
    gate_pre = gate_up[:, :ffn]
    up_pre = gate_up[:, ffn:]
    hidden = (jax.nn.silu(gate_pre) * up_pre).astype(jnp.bfloat16)
    ffn_part = jnp.dot(hidden, down_weight, preferred_element_type=jnp.float32).astype(jnp.bfloat16)
    ffn_branch = ffn_part.astype(jnp.float32) + swap_heads(ffn_part).astype(jnp.float32)
    sig_t = jax.nn.sigmoid(gate_t)
    layer_output = own_rows((middle + sig_t * ffn_branch).astype(jnp.bfloat16)[None], head, rows)

    grad_out = g_rows.astype(jnp.float32)
    d_ffn = (grad_out * sig_t).astype(jnp.bfloat16)
    d_gate_t = jnp.sum(grad_out * ffn_branch * sig_t * (1.0 - sig_t), axis=0, keepdims=True)
    down_grad_t = lax.dot_general(
        d_ffn, hidden, (((0,), (0,)), ((), ())), preferred_element_type=jnp.float32
    )
    d_hidden = lax.dot_general(
        d_ffn, down_weight, (((1,), (1,)), ((), ())), preferred_element_type=jnp.float32
    )
    d_gate = d_hidden * up_pre * silu_slope(gate_pre)
    d_up = d_hidden * jax.nn.silu(gate_pre)
    d_gate_up = jnp.concatenate([d_gate, d_up], axis=1).astype(jnp.bfloat16)
    gate_up_grad = lax.dot_general(
        normed_t, d_gate_up, (((0,), (0,)), ((), ())), preferred_element_type=jnp.float32
    )
    ffn_in_part = lax.dot_general(
        d_gate_up, gate_up_w, (((1,), (1,)), ((), ())), preferred_element_type=jnp.float32
    )
    d_normed_t = head_sum_low(ffn_in_part)
    d_middle = grad_out + norm_back(norm_mid, inv_mid, d_normed_t * (1.0 + scale_t))
    d_scale_t = jnp.sum(d_normed_t * norm_mid, axis=0, keepdims=True)
    d_shift_t = jnp.sum(d_normed_t, axis=0, keepdims=True)
    d_attn = d_middle * sig_a
    d_gate_a = jnp.sum(d_middle * attn_branch * sig_a * (1.0 - sig_a), axis=0, keepdims=True)
    d_out_bias = jnp.sum(d_attn, axis=0, keepdims=True)
    d_attn_low = d_attn.astype(jnp.bfloat16)

    out_weight_grad_t = lax.dot_general(
        d_attn_low, mixed, (((0,), (0,)), ((), ())), preferred_element_type=jnp.float32
    )
    d_mixed = head_split(
        lax.dot_general(
            d_attn_low, out_weight, (((1,), (1,)), ((), ())), preferred_element_type=jnp.float32
        ).astype(jnp.bfloat16)
    )
    d_values = jnp.einsum("hqk,qhe->khe", probs_low, d_mixed, preferred_element_type=jnp.float32)
    d_probs = jnp.einsum("qhe,khe->hqk", d_mixed, values, preferred_element_type=jnp.float32)
    d_scores = (
        attn_probs * (d_probs - jnp.sum(d_probs * attn_probs, axis=-1, keepdims=True))
    ).astype(jnp.bfloat16)
    d_queries = jnp.einsum(
        "hqk,khe->qhe", d_scores, keys, preferred_element_type=jnp.float32
    ) * DH ** (-0.5)
    d_keys = jnp.einsum(
        "hqk,qhe->khe", d_scores, queries, preferred_element_type=jnp.float32
    ) * DH ** (-0.5)
    d_qkv = jnp.concatenate(
        [d_queries.reshape(length, proj), d_keys.reshape(length, proj), d_values.reshape(length, proj)],
        axis=1,
    ).astype(jnp.bfloat16)
    qkv_grad = lax.dot_general(
        normed_a, d_qkv, (((0,), (0,)), ((), ())), preferred_element_type=jnp.float32
    )

    packed = blank((width, 4 * proj + 3 * ffn), jnp.bfloat16)
    packed = lax.dynamic_update_slice(packed, gate_up_grad.astype(jnp.bfloat16), (0, 4 * proj))
    packed = lax.dynamic_update_slice(
        packed, down_grad_t.astype(jnp.bfloat16), (0, 4 * proj + 2 * ffn)
    )
    packed = lax.dynamic_update_slice(packed, out_weight_grad_t.astype(jnp.bfloat16), (0, 3 * proj))
    packed = lax.dynamic_update_slice(packed, qkv_grad.astype(jnp.bfloat16), (0, 0))
    reduced = lax.psum_scatter(packed, "dp", scatter_dimension=0, tiled=True).astype(jnp.float32)

    attn_in_part = lax.dot_general(
        d_qkv, qkv_w, (((1,), (1,)), ((), ())), preferred_element_type=jnp.float32
    ).astype(jnp.bfloat16)
    d_normed_a = attn_in_part.astype(jnp.float32) + swap_heads(attn_in_part).astype(jnp.float32)
    input_grad = own_rows(
        (d_middle + norm_back(norm_in, inv_in, d_normed_a * (1.0 + scale_a)))[None], head, rows
    )
    d_scale_a = jnp.sum(d_normed_a * norm_in, axis=0, keepdims=True)
    d_shift_a = jnp.sum(d_normed_a, axis=0, keepdims=True)
    d_modulation = jnp.concatenate(
        [d_scale_a, d_shift_a, d_gate_a, d_scale_t, d_shift_t, d_gate_t], axis=-1
    )

    d_bias_rows = trade_blocks(d_scores, head, rows, 1, 0)
    d_bias_flat = jnp.pad(d_bias_rows.reshape(heads_all, -1), ((0, HEAD_PAD - heads_all), (0, 0)))
    pair_grad, pair_wg, pair_gg = pair_backward(pair_flat, d_bias_flat, pair_gain_row, pair_wt)
    pair_grad = pair_grad.reshape(pair_input.shape)
    pair_weight_grad = pair_wg[:heads_all].T
    pair_gain_grad = pair_gg[0]

    pair_small = head_sum(
        jnp.concatenate([pair_weight_grad.reshape(-1), pair_gain_grad])[None]
    )
    small = jnp.concatenate([d_modulation, time_cond, d_out_bias], axis=-1)
    small_rows = dp_gather(small)
    mod_size = d_modulation.shape[-1]
    cond_size = time_cond.shape[-1]
    pw_size = pair_weight.size
    mod_chain = small_rows[:, :mod_size]
    cond_chain = small_rows[:, mod_size : mod_size + cond_size]
    out_bias_grad = jnp.sum(small_rows[:, mod_size + cond_size :], axis=0)
    pair_total = dp_sum(pair_small)[0]
    pair_weight_grad = pair_total[:pw_size].reshape(pair_weight.shape)
    pair_gain_grad = pair_total[pw_size:]
    cond_act = lax.optimization_barrier(jax.nn.silu(cond_chain).astype(jnp.bfloat16)).astype(
        jnp.float32
    )
    mod_weight_grad = jnp.dot(cond_act.T, mod_chain, precision=precise)
    mod_bias_grad = jnp.sum(mod_chain, axis=0)
    cond_grad = jnp.dot(
        d_modulation, mod_weight.astype(jnp.float32).T, precision=precise
    ) * silu_slope(time_cond)

    cuts = [0, 3 * proj, 4 * proj, 4 * proj + 2 * ffn, 4 * proj + 3 * ffn]
    pieces = [reduced[:, cuts[i] : cuts[i + 1]] for i in range(4)]
    qkv_grad = pieces[0].reshape(-1, 3, proj)
    out_weight_grad = pieces[1].T
    gate_up_grad = pieces[2].reshape(-1, 2, ffn)
    down_grad = pieces[3].T
    return (
        layer_output,
        input_grad,
        pair_grad,
        cond_grad,
        mod_weight_grad,
        mod_bias_grad,
        qkv_grad,
        pair_gain_grad,
        pair_weight_grad,
        out_weight_grad,
        out_bias_grad,
        gate_up_grad,
        down_grad,
    )


def solution(mesh):
    placed = (
        P("dp", "head", None),
        P("dp", "head", None, None),
        P("dp", None),
        P("dp"),
        P("dp", None),
        P(),
        P(),
        P(None, None, "head"),
        P(),
        P(),
        P("head", None),
        P(),
        P(None, None, "head"),
        P("head", None),
        P("dp", "head", None),
    )
    return jax.shard_map(
        shards,
        mesh=mesh,
        in_specs=placed,
        out_specs=(
            P("dp", "head", None),
            P("dp", "head", None),
            P("dp", "head", None, None),
            P("dp", None),
            P(),
            P(),
            P("dp", None, "head"),
            P(),
            P(),
            P("head", "dp"),
            P(),
            P("dp", None, "head"),
            P("head", "dp"),
        ),
        check_vma=False,
    )
```

```python
import jax
import jax.numpy as jnp
from jax import lax
from jax.experimental import pallas as pl
from jax.experimental.pallas import tpu as pltpu
from jax.sharding import PartitionSpec as P

DH = 64


epsilon = 1e-05
masked_score = -1000000000.0
precise = lax.Precision.HIGHEST
LANES = 128
PAIR_TILE = 4096
PAIR_BACK_TILE = 2048
HEAD_PAD = 16


def matmul_kernel(a_ref, b_ref, o_ref):
    o_ref[...] = jnp.dot(a_ref[...], b_ref[...], preferred_element_type=jnp.float32).astype(
        o_ref.dtype
    )


def matmul(a, b, dtype, cols):
    m, k = a.shape
    n = b.shape[1]
    return pl.pallas_call(
        matmul_kernel,
        grid=(n // cols,),
        in_specs=[
            pl.BlockSpec((m, k), lambda j: (0, 0)),
            pl.BlockSpec((k, cols), lambda j: (0, j)),
        ],
        out_specs=pl.BlockSpec((m, cols), lambda j: (0, j)),
        out_shape=jax.ShapeDtypeStruct((m, n), dtype),
        cost_estimate=pl.CostEstimate(
            flops=2 * m * k * n,
            transcendentals=0,
            bytes_accessed=2 * (m * k + k * n) + m * n * jnp.dtype(dtype).itemsize,
        ),
    )(a, b)


def blank_kernel(out_ref):
    del out_ref


def blank(shape, dtype):
    return pl.pallas_call(
        blank_kernel,
        out_shape=jax.ShapeDtypeStruct(shape, dtype),
        out_specs=pl.BlockSpec(memory_space=pl.ANY),
    )()


def pair_stats(x):
    centred = x - jnp.mean(x, axis=-1, keepdims=True)
    inv_std = lax.rsqrt(jnp.mean(centred * centred, axis=-1, keepdims=True) + epsilon)
    return centred * inv_std, inv_std


def pair_forward_kernel(x_ref, gain_ref, wt_ref, bias_ref):
    normed, _ = pair_stats(x_ref[...].astype(jnp.float32))
    scaled = (normed * gain_ref[...]).astype(jnp.bfloat16)
    bias = lax.dot_general(
        wt_ref[...], scaled, (((1,), (1,)), ((), ())), preferred_element_type=jnp.float32
    )
    bias_ref[...] = bias[: bias_ref.shape[0]].astype(bias_ref.dtype)


def pair_forward(flat, gain, wt, heads):
    m, width = flat.shape
    tile = min(PAIR_TILE, m)
    return pl.pallas_call(
        pair_forward_kernel,
        grid=(m // tile,),
        in_specs=[
            pl.BlockSpec((tile, width), lambda i: (i, 0)),
            pl.BlockSpec((1, width), lambda i: (0, 0)),
            pl.BlockSpec(wt.shape, lambda i: (0, 0)),
        ],
        out_specs=pl.BlockSpec((heads, tile), lambda i: (0, i)),
        out_shape=jax.ShapeDtypeStruct((heads, m), jnp.bfloat16),
        cost_estimate=pl.CostEstimate(
            flops=m * width * (2 * HEAD_PAD + 10),
            transcendentals=m,
            bytes_accessed=m * width * 2 + heads * m * 2,
        ),
    )(flat, gain, wt)


def pair_backward_kernel(x_ref, ds_ref, gain_ref, wt_ref, grad_ref, wg_ref, gg_ref):
    step = pl.program_id(0)
    normed, inv_std = pair_stats(x_ref[...].astype(jnp.float32))
    gain = gain_ref[...]
    scaled = (normed * gain).astype(jnp.bfloat16)
    ds = ds_ref[...]
    d_scaled = lax.dot_general(
        ds, wt_ref[...], (((0,), (0,)), ((), ())), preferred_element_type=jnp.float32
    )
    wg = lax.dot_general(ds, scaled, (((1,), (0,)), ((), ())), preferred_element_type=jnp.float32)
    gg = jnp.sum(d_scaled * normed, axis=0, keepdims=True)
    d_normed = d_scaled * gain
    mean_grad = jnp.mean(d_normed, axis=-1, keepdims=True)
    mean_proj = jnp.mean(d_normed * normed, axis=-1, keepdims=True)
    grad_ref[...] = (inv_std * (d_normed - mean_grad - normed * mean_proj)).astype(grad_ref.dtype)

    @pl.when(step == 0)
    def _():
        wg_ref[...] = jnp.zeros_like(wg_ref)
        gg_ref[...] = jnp.zeros_like(gg_ref)

    wg_ref[...] += wg
    gg_ref[...] += gg


def pair_backward(flat, ds, gain, wt):
    m, width = flat.shape
    tile = min(PAIR_BACK_TILE, m)
    pad = ds.shape[0]
    return pl.pallas_call(
        pair_backward_kernel,
        grid=(m // tile,),
        in_specs=[
            pl.BlockSpec((tile, width), lambda i: (i, 0)),
            pl.BlockSpec((pad, tile), lambda i: (0, i)),
            pl.BlockSpec((1, width), lambda i: (0, 0)),
            pl.BlockSpec(wt.shape, lambda i: (0, 0)),
        ],
        out_specs=[
            pl.BlockSpec((tile, width), lambda i: (i, 0)),
            pl.BlockSpec((pad, width), lambda i: (0, 0)),
            pl.BlockSpec((1, width), lambda i: (0, 0)),
        ],
        out_shape=[
            jax.ShapeDtypeStruct((m, width), jnp.bfloat16),
            jax.ShapeDtypeStruct((pad, width), jnp.float32),
            jax.ShapeDtypeStruct((1, width), jnp.float32),
        ],
        compiler_params=pltpu.CompilerParams(dimension_semantics=("arbitrary",)),
        cost_estimate=pl.CostEstimate(
            flops=m * width * (4 * HEAD_PAD + 20),
            transcendentals=m,
            bytes_accessed=2 * m * width * 2 + pad * m * 2,
        ),
    )(flat, ds, gain, wt)


def layer_norm(values):
    centred = values - jnp.mean(values, axis=-1, keepdims=True)
    inv_std = lax.rsqrt(jnp.mean(centred * centred, axis=-1, keepdims=True) + epsilon)
    return (centred * inv_std, inv_std)


def norm_back(normed, inv_std, grad):
    mean_grad = jnp.mean(grad, axis=-1, keepdims=True)
    mean_proj = jnp.mean(grad * normed, axis=-1, keepdims=True)
    return inv_std * (grad - mean_grad - normed * mean_proj)


def silu_slope(values):
    sigma = jax.nn.sigmoid(values)
    return sigma * (1.0 + values * (1.0 - sigma))


def head_split(values):
    return values.reshape(values.shape[:-1] + (values.shape[-1] // DH, DH))


def swap_heads(values):
    return lax.ppermute(values, "head", [(0, 1), (1, 0)])


def whole_rows(own, first):
    other = swap_heads(own)
    return jnp.where(
        first,
        jnp.concatenate([own, other], axis=0),
        jnp.concatenate([other, own], axis=0),
    )


def dp_gather(values):
    count = lax.axis_size("dp")
    index = lax.axis_index("dp")
    block = values
    step = 1
    while step < count:
        other = lax.ppermute(block, "dp", [(i, i ^ step) for i in range(count)])
        block = jnp.where(
            (index & step) == 0,
            jnp.concatenate([block, other], axis=0),
            jnp.concatenate([other, block], axis=0),
        )
        step *= 2
    return block


def dp_sum(values):
    count = lax.axis_size("dp")
    index = lax.axis_index("dp")
    step = 1
    while step < count:
        other = lax.ppermute(values, "dp", [(i, i ^ step) for i in range(count)])
        values = jnp.where((index & step) == 0, values + other, other + values)
        step *= 2
    return values


def own_rows(values, head, rows):
    return lax.dynamic_slice_in_dim(values, head * rows, rows, 1)


def head_sum(part):
    return part + swap_heads(part)


def head_sum_low(part):
    low = part.astype(jnp.bfloat16)
    return low.astype(jnp.float32) + swap_heads(low).astype(jnp.float32)


def trade_blocks(values, head, size, axis, mine_axis):
    mine = lax.dynamic_slice_in_dim(values, head * size, size, axis)
    theirs = swap_heads(lax.dynamic_slice_in_dim(values, (1 - head) * size, size, axis))
    return jnp.where(
        head == 0,
        jnp.concatenate([mine, theirs], axis=mine_axis),
        jnp.concatenate([theirs, mine], axis=mine_axis),
    )


def attn_scores(queries, keys, biases, valid):
    scores = jnp.einsum("cqhe,ckhe->chqk", queries, keys, preferred_element_type=jnp.float32)
    scores = scores * DH ** (-0.5) + biases.astype(jnp.float32)
    return jnp.where(valid[:, None, None, :], scores, masked_score)


def to_chunks(values, parts):
    return values.reshape(parts, -1, LANES)


def shards(
    layer_input,
    pair_input,
    time_cond,
    chain_lengths,
    residue_mask,
    mod_weight,
    mod_bias,
    qkv_weight,
    pair_gain,
    pair_weight,
    out_weight,
    out_bias,
    gate_up_weight,
    down_weight,
    output_grad,
):
    assert layer_input.shape[0] == 1
    rows = layer_input.shape[1]
    width = layer_input.shape[2]
    length = residue_mask.shape[1]
    head = lax.axis_index("head")
    first = head == 0
    data_count = lax.axis_size("dp")
    proj = qkv_weight.shape[2]
    ffn = gate_up_weight.shape[2]
    qkv_w = qkv_weight.reshape(width, 3 * proj)
    gate_up_w = gate_up_weight.reshape(width, 2 * ffn)

    x_rows = whole_rows(layer_input[0], first)
    g_rows = whole_rows(output_grad[0], first)
    out_weight_all = whole_rows(out_weight, first)

    positions = jnp.arange(length, dtype=jnp.int32)
    valid = (positions < chain_lengths[0]) & ((residue_mask[0] == 1) | (positions == 0))
    silu_cond = jax.nn.silu(time_cond).astype(jnp.bfloat16)
    modulation = jnp.dot(silu_cond, mod_weight, preferred_element_type=jnp.float32) + mod_bias
    scale_a, shift_a, gate_a, scale_t, shift_t, gate_t = [
        modulation[:, section * width : (section + 1) * width] for section in range(6)
    ]

    heads_all = pair_weight.shape[1]
    pair_width = pair_input.shape[-1]
    pair_flat = pair_input.reshape(-1, pair_width)
    pair_wt = jnp.pad(pair_weight.T, ((0, HEAD_PAD - heads_all), (0, 0)))
    pair_gain_row = pair_gain.reshape(1, pair_width)
    bias_flat = pair_forward(pair_flat, pair_gain_row, pair_wt, heads_all)
    bias_rows = bias_flat.reshape(heads_all, rows, length)
    heads_own = proj // DH
    biases = trade_blocks(bias_rows, head, heads_own, 0, 1)

    residues = x_rows.astype(jnp.float32)
    norm_in, inv_in = layer_norm(residues)
    normed_a = (norm_in * (1.0 + scale_a) + shift_a).astype(jnp.bfloat16)
    projected = matmul(normed_a, qkv_w, jnp.bfloat16, proj)
    queries = head_split(projected[:, :proj])
    keys = head_split(projected[:, proj : 2 * proj])
    values = head_split(projected[:, 2 * proj :])
    scores = jnp.einsum("qhe,khe->hqk", queries, keys, preferred_element_type=jnp.float32)
    scores = scores * DH ** (-0.5) + biases.astype(jnp.float32)
    scores = jnp.where(valid[None, None, :], scores, masked_score)
    row_max = jnp.max(scores, axis=-1, keepdims=True)
    exp_scores = jnp.exp(scores - row_max)
    row_total = jnp.sum(exp_scores, axis=-1, keepdims=True)
    attn_probs = exp_scores / row_total
    probs_low = attn_probs.astype(jnp.bfloat16)
    mixed = jnp.einsum("hqk,khe->qhe", probs_low, values, preferred_element_type=jnp.float32)
    mixed = mixed.reshape(length, proj).astype(jnp.bfloat16)
    mixed_all = jnp.where(
        first,
        jnp.concatenate([mixed, swap_heads(mixed)], axis=1),
        jnp.concatenate([swap_heads(mixed), mixed], axis=1),
    )
    attn_branch = jnp.dot(mixed_all, out_weight_all, preferred_element_type=jnp.float32) + out_bias
    sig_a = jax.nn.sigmoid(gate_a)
    middle = residues + sig_a * attn_branch

    norm_mid, inv_mid = layer_norm(middle)
    normed_t = (norm_mid * (1.0 + scale_t) + shift_t).astype(jnp.bfloat16)
    gate_up = matmul(normed_t, gate_up_w, jnp.float32, ffn // 2)
    gate_pre = gate_up[:, :ffn]
    up_pre = gate_up[:, ffn:]
    hidden = (jax.nn.silu(gate_pre) * up_pre).astype(jnp.bfloat16)
    ffn_part = jnp.dot(hidden, down_weight, preferred_element_type=jnp.float32).astype(jnp.bfloat16)
    ffn_branch = ffn_part.astype(jnp.float32) + swap_heads(ffn_part).astype(jnp.float32)
    sig_t = jax.nn.sigmoid(gate_t)
    layer_output = own_rows((middle + sig_t * ffn_branch).astype(jnp.bfloat16)[None], head, rows)

    grad_out = g_rows.astype(jnp.float32)
    d_ffn = (grad_out * sig_t).astype(jnp.bfloat16)
    d_gate_t = jnp.sum(grad_out * ffn_branch * sig_t * (1.0 - sig_t), axis=0, keepdims=True)
    down_grad_t = lax.dot_general(
        d_ffn, hidden, (((0,), (0,)), ((), ())), preferred_element_type=jnp.float32
    )
    d_hidden = lax.dot_general(
        d_ffn, down_weight, (((1,), (1,)), ((), ())), preferred_element_type=jnp.float32
    )
    d_gate = d_hidden * up_pre * silu_slope(gate_pre)
    d_up = d_hidden * jax.nn.silu(gate_pre)
    d_gate_up = jnp.concatenate([d_gate, d_up], axis=1).astype(jnp.bfloat16)
    gate_up_grad = lax.dot_general(
        normed_t, d_gate_up, (((0,), (0,)), ((), ())), preferred_element_type=jnp.float32
    )
    ffn_in_part = lax.dot_general(
        d_gate_up, gate_up_w, (((1,), (1,)), ((), ())), preferred_element_type=jnp.float32
    )
    d_normed_t = head_sum_low(ffn_in_part)
    d_middle = grad_out + norm_back(norm_mid, inv_mid, d_normed_t * (1.0 + scale_t))
    d_scale_t = jnp.sum(d_normed_t * norm_mid, axis=0, keepdims=True)
    d_shift_t = jnp.sum(d_normed_t, axis=0, keepdims=True)
    d_attn = d_middle * sig_a
    d_gate_a = jnp.sum(d_middle * attn_branch * sig_a * (1.0 - sig_a), axis=0, keepdims=True)
    d_out_bias = jnp.sum(d_attn, axis=0, keepdims=True)
    d_attn_low = d_attn.astype(jnp.bfloat16)

    out_weight_grad_t = lax.dot_general(
        d_attn_low, mixed, (((0,), (0,)), ((), ())), preferred_element_type=jnp.float32
    )
    d_mixed = head_split(
        lax.dot_general(
            d_attn_low, out_weight, (((1,), (1,)), ((), ())), preferred_element_type=jnp.float32
        ).astype(jnp.bfloat16)
    )
    d_values = jnp.einsum("hqk,qhe->khe", probs_low, d_mixed, preferred_element_type=jnp.float32)
    d_probs = jnp.einsum("qhe,khe->hqk", d_mixed, values, preferred_element_type=jnp.float32)
    d_scores = (
        attn_probs * (d_probs - jnp.sum(d_probs * attn_probs, axis=-1, keepdims=True))
    ).astype(jnp.bfloat16)
    d_queries = jnp.einsum(
        "hqk,khe->qhe", d_scores, keys, preferred_element_type=jnp.float32
    ) * DH ** (-0.5)
    d_keys = jnp.einsum(
        "hqk,qhe->khe", d_scores, queries, preferred_element_type=jnp.float32
    ) * DH ** (-0.5)
    d_qkv = jnp.concatenate(
        [d_queries.reshape(length, proj), d_keys.reshape(length, proj), d_values.reshape(length, proj)],
        axis=1,
    ).astype(jnp.bfloat16)
    qkv_grad = lax.dot_general(
        normed_a, d_qkv, (((0,), (0,)), ((), ())), preferred_element_type=jnp.float32
    )

    packed = blank((width, 4 * proj + 3 * ffn), jnp.bfloat16)
    packed = lax.dynamic_update_slice(packed, gate_up_grad.astype(jnp.bfloat16), (0, 4 * proj))
    packed = lax.dynamic_update_slice(
        packed, down_grad_t.astype(jnp.bfloat16), (0, 4 * proj + 2 * ffn)
    )
    packed = lax.dynamic_update_slice(packed, out_weight_grad_t.astype(jnp.bfloat16), (0, 3 * proj))
    packed = lax.dynamic_update_slice(packed, qkv_grad.astype(jnp.bfloat16), (0, 0))
    reduced = lax.psum_scatter(packed, "dp", scatter_dimension=0, tiled=True).astype(jnp.float32)

    attn_in_part = lax.dot_general(
        d_qkv, qkv_w, (((1,), (1,)), ((), ())), preferred_element_type=jnp.float32
    ).astype(jnp.bfloat16)
    d_normed_a = attn_in_part.astype(jnp.float32) + swap_heads(attn_in_part).astype(jnp.float32)
    input_grad = own_rows(
        (d_middle + norm_back(norm_in, inv_in, d_normed_a * (1.0 + scale_a)))[None], head, rows
    )
    d_scale_a = jnp.sum(d_normed_a * norm_in, axis=0, keepdims=True)
    d_shift_a = jnp.sum(d_normed_a, axis=0, keepdims=True)
    d_modulation = jnp.concatenate(
        [d_scale_a, d_shift_a, d_gate_a, d_scale_t, d_shift_t, d_gate_t], axis=-1
    )

    d_bias_rows = trade_blocks(d_scores, head, rows, 1, 0)
    d_bias_flat = jnp.pad(d_bias_rows.reshape(heads_all, -1), ((0, HEAD_PAD - heads_all), (0, 0)))
    pair_grad, pair_wg, pair_gg = pair_backward(pair_flat, d_bias_flat, pair_gain_row, pair_wt)
    pair_grad = pair_grad.reshape(pair_input.shape)
    pair_weight_grad = pair_wg[:heads_all].T
    pair_gain_grad = pair_gg[0]

    pair_small = head_sum(
        jnp.concatenate([pair_weight_grad.reshape(-1), pair_gain_grad])[None]
    )
    small = jnp.concatenate([d_modulation, time_cond, d_out_bias], axis=-1)
    small_rows = dp_gather(small)
    mod_size = d_modulation.shape[-1]
    cond_size = time_cond.shape[-1]
    pw_size = pair_weight.size
    mod_chain = small_rows[:, :mod_size]
    cond_chain = small_rows[:, mod_size : mod_size + cond_size]
    out_bias_grad = jnp.sum(small_rows[:, mod_size + cond_size :], axis=0)
    pair_total = dp_sum(pair_small)[0]
    pair_weight_grad = pair_total[:pw_size].reshape(pair_weight.shape)
    pair_gain_grad = pair_total[pw_size:]
    cond_act = lax.optimization_barrier(jax.nn.silu(cond_chain).astype(jnp.bfloat16)).astype(
        jnp.float32
    )
    mod_weight_grad = jnp.dot(cond_act.T, mod_chain, precision=precise)
    mod_bias_grad = jnp.sum(mod_chain, axis=0)
    cond_grad = jnp.dot(
        d_modulation, mod_weight.astype(jnp.float32).T, precision=precise
    ) * silu_slope(time_cond)

    cuts = [0, 3 * proj, 4 * proj, 4 * proj + 2 * ffn, 4 * proj + 3 * ffn]
    pieces = [reduced[:, cuts[i] : cuts[i + 1]] for i in range(4)]
    qkv_grad = pieces[0].reshape(-1, 3, proj)
    out_weight_grad = pieces[1].T
    gate_up_grad = pieces[2].reshape(-1, 2, ffn)
    down_grad = pieces[3].T
    return (
        layer_output,
        input_grad,
        pair_grad,
        cond_grad,
        mod_weight_grad,
        mod_bias_grad,
        qkv_grad,
        pair_gain_grad,
        pair_weight_grad,
        out_weight_grad,
        out_bias_grad,
        gate_up_grad,
        down_grad,
    )


def solution(mesh):
    placed = (
        P("dp", "head", None),
        P("dp", "head", None, None),
        P("dp", None),
        P("dp"),
        P("dp", None),
        P(),
        P(),
        P(None, None, "head"),
        P(),
        P(),
        P("head", None),
        P(),
        P(None, None, "head"),
        P("head", None),
        P("dp", "head", None),
    )
    return jax.shard_map(
        shards,
        mesh=mesh,
        in_specs=placed,
        out_specs=(
            P("dp", "head", None),
            P("dp", "head", None),
            P("dp", "head", None, None),
            P("dp", None),
            P(),
            P(),
            P("dp", None, "head"),
            P(),
            P(),
            P("head", "dp"),
            P(),
            P("dp", None, "head"),
            P("head", "dp"),
        ),
        check_vma=False,
    )
```

```python
import jax
import jax.numpy as jnp
from jax import lax
from jax.experimental import pallas as pl
from jax.experimental.pallas import tpu as pltpu
from jax.sharding import PartitionSpec as P

DH = 64


epsilon = 1e-05
masked_score = -1000000000.0
precise = lax.Precision.HIGHEST
LANES = 128
PAIR_TILE = 4096
PAIR_BACK_TILE = 2048
HEAD_PAD = 16


def blank_kernel(out_ref):
    del out_ref


def blank(shape, dtype):
    return pl.pallas_call(
        blank_kernel,
        out_shape=jax.ShapeDtypeStruct(shape, dtype),
        out_specs=pl.BlockSpec(memory_space=pl.ANY),
    )()


def pair_stats(x):
    centred = x - jnp.mean(x, axis=-1, keepdims=True)
    inv_std = lax.rsqrt(jnp.mean(centred * centred, axis=-1, keepdims=True) + epsilon)
    return centred * inv_std, inv_std


def pair_forward_kernel(x_ref, gain_ref, wt_ref, bias_ref):
    normed, _ = pair_stats(x_ref[...].astype(jnp.float32))
    scaled = (normed * gain_ref[...]).astype(jnp.bfloat16)
    bias = lax.dot_general(
        wt_ref[...], scaled, (((1,), (1,)), ((), ())), preferred_element_type=jnp.float32
    )
    bias_ref[...] = bias[: bias_ref.shape[0]].astype(bias_ref.dtype)


def pair_forward(flat, gain, wt, heads):
    m, width = flat.shape
    tile = min(PAIR_TILE, m)
    return pl.pallas_call(
        pair_forward_kernel,
        grid=(m // tile,),
        in_specs=[
            pl.BlockSpec((tile, width), lambda i: (i, 0)),
            pl.BlockSpec((1, width), lambda i: (0, 0)),
            pl.BlockSpec(wt.shape, lambda i: (0, 0)),
        ],
        out_specs=pl.BlockSpec((heads, tile), lambda i: (0, i)),
        out_shape=jax.ShapeDtypeStruct((heads, m), jnp.bfloat16),
        cost_estimate=pl.CostEstimate(
            flops=m * width * (2 * HEAD_PAD + 10),
            transcendentals=m,
            bytes_accessed=m * width * 2 + heads * m * 2,
        ),
    )(flat, gain, wt)


def pair_backward_kernel(x_ref, ds_ref, gain_ref, wt_ref, grad_ref, wg_ref, gg_ref):
    step = pl.program_id(0)
    normed, inv_std = pair_stats(x_ref[...].astype(jnp.float32))
    gain = gain_ref[...]
    scaled = (normed * gain).astype(jnp.bfloat16)
    ds = ds_ref[...]
    d_scaled = lax.dot_general(
        ds, wt_ref[...], (((0,), (0,)), ((), ())), preferred_element_type=jnp.float32
    )
    wg = lax.dot_general(ds, scaled, (((1,), (0,)), ((), ())), preferred_element_type=jnp.float32)
    gg = jnp.sum(d_scaled * normed, axis=0, keepdims=True)
    d_normed = d_scaled * gain
    mean_grad = jnp.mean(d_normed, axis=-1, keepdims=True)
    mean_proj = jnp.mean(d_normed * normed, axis=-1, keepdims=True)
    grad_ref[...] = (inv_std * (d_normed - mean_grad - normed * mean_proj)).astype(grad_ref.dtype)

    @pl.when(step == 0)
    def _():
        wg_ref[...] = jnp.zeros_like(wg_ref)
        gg_ref[...] = jnp.zeros_like(gg_ref)

    wg_ref[...] += wg
    gg_ref[...] += gg


def pair_backward(flat, ds, gain, wt):
    m, width = flat.shape
    tile = min(PAIR_BACK_TILE, m)
    pad = ds.shape[0]
    return pl.pallas_call(
        pair_backward_kernel,
        grid=(m // tile,),
        in_specs=[
            pl.BlockSpec((tile, width), lambda i: (i, 0)),
            pl.BlockSpec((pad, tile), lambda i: (0, i)),
            pl.BlockSpec((1, width), lambda i: (0, 0)),
            pl.BlockSpec(wt.shape, lambda i: (0, 0)),
        ],
        out_specs=[
            pl.BlockSpec((tile, width), lambda i: (i, 0)),
            pl.BlockSpec((pad, width), lambda i: (0, 0)),
            pl.BlockSpec((1, width), lambda i: (0, 0)),
        ],
        out_shape=[
            jax.ShapeDtypeStruct((m, width), jnp.bfloat16),
            jax.ShapeDtypeStruct((pad, width), jnp.float32),
            jax.ShapeDtypeStruct((1, width), jnp.float32),
        ],
        compiler_params=pltpu.CompilerParams(dimension_semantics=("arbitrary",)),
        cost_estimate=pl.CostEstimate(
            flops=m * width * (4 * HEAD_PAD + 20),
            transcendentals=m,
            bytes_accessed=2 * m * width * 2 + pad * m * 2,
        ),
    )(flat, ds, gain, wt)


def layer_norm(values):
    centred = values - jnp.mean(values, axis=-1, keepdims=True)
    inv_std = lax.rsqrt(jnp.mean(centred * centred, axis=-1, keepdims=True) + epsilon)
    return (centred * inv_std, inv_std)


def norm_back(normed, inv_std, grad):
    mean_grad = jnp.mean(grad, axis=-1, keepdims=True)
    mean_proj = jnp.mean(grad * normed, axis=-1, keepdims=True)
    return inv_std * (grad - mean_grad - normed * mean_proj)


def silu_slope(values):
    sigma = jax.nn.sigmoid(values)
    return sigma * (1.0 + values * (1.0 - sigma))


def head_split(values):
    return values.reshape(values.shape[:-1] + (values.shape[-1] // DH, DH))


def swap_heads(values):
    return lax.ppermute(values, "head", [(0, 1), (1, 0)])


def whole_rows(own, first):
    other = swap_heads(own)
    return jnp.where(
        first,
        jnp.concatenate([own, other], axis=0),
        jnp.concatenate([other, own], axis=0),
    )


def dp_gather(values):
    count = lax.axis_size("dp")
    index = lax.axis_index("dp")
    block = values
    step = 1
    while step < count:
        other = lax.ppermute(block, "dp", [(i, i ^ step) for i in range(count)])
        block = jnp.where(
            (index & step) == 0,
            jnp.concatenate([block, other], axis=0),
            jnp.concatenate([other, block], axis=0),
        )
        step *= 2
    return block


def dp_sum(values):
    count = lax.axis_size("dp")
    index = lax.axis_index("dp")
    step = 1
    while step < count:
        other = lax.ppermute(values, "dp", [(i, i ^ step) for i in range(count)])
        values = jnp.where((index & step) == 0, values + other, other + values)
        step *= 2
    return values


def own_rows(values, head, rows):
    return lax.dynamic_slice_in_dim(values, head * rows, rows, 1)


def head_sum(part):
    return part + swap_heads(part)


def head_sum_low(part):
    low = part.astype(jnp.bfloat16)
    return low.astype(jnp.float32) + swap_heads(low).astype(jnp.float32)


def trade_blocks(values, head, size, axis, mine_axis):
    mine = lax.dynamic_slice_in_dim(values, head * size, size, axis)
    theirs = swap_heads(lax.dynamic_slice_in_dim(values, (1 - head) * size, size, axis))
    return jnp.where(
        head == 0,
        jnp.concatenate([mine, theirs], axis=mine_axis),
        jnp.concatenate([theirs, mine], axis=mine_axis),
    )


def attn_scores(queries, keys, biases, valid):
    scores = jnp.einsum("cqhe,ckhe->chqk", queries, keys, preferred_element_type=jnp.float32)
    scores = scores * DH ** (-0.5) + biases.astype(jnp.float32)
    return jnp.where(valid[:, None, None, :], scores, masked_score)


def to_chunks(values, parts):
    return values.reshape(parts, -1, LANES)


def shards(
    layer_input,
    pair_input,
    time_cond,
    chain_lengths,
    residue_mask,
    mod_weight,
    mod_bias,
    qkv_weight,
    pair_gain,
    pair_weight,
    out_weight,
    out_bias,
    gate_up_weight,
    down_weight,
    output_grad,
):
    assert layer_input.shape[0] == 1
    rows = layer_input.shape[1]
    width = layer_input.shape[2]
    length = residue_mask.shape[1]
    head = lax.axis_index("head")
    first = head == 0
    data_count = lax.axis_size("dp")
    proj = qkv_weight.shape[2]
    ffn = gate_up_weight.shape[2]
    qkv_w = qkv_weight.reshape(width, 3 * proj)
    gate_up_w = gate_up_weight.reshape(width, 2 * ffn)

    x_rows = whole_rows(layer_input[0], first)
    g_rows = whole_rows(output_grad[0], first)
    out_weight_all = whole_rows(out_weight, first)

    positions = jnp.arange(length, dtype=jnp.int32)
    valid = (positions < chain_lengths[0]) & ((residue_mask[0] == 1) | (positions == 0))
    silu_cond = jax.nn.silu(time_cond).astype(jnp.bfloat16)
    modulation = jnp.dot(silu_cond, mod_weight, preferred_element_type=jnp.float32) + mod_bias
    scale_a, shift_a, gate_a, scale_t, shift_t, gate_t = [
        modulation[:, section * width : (section + 1) * width] for section in range(6)
    ]

    heads_all = pair_weight.shape[1]
    pair_width = pair_input.shape[-1]
    pair_flat = pair_input.reshape(-1, pair_width)
    pair_wt = jnp.pad(pair_weight.T, ((0, HEAD_PAD - heads_all), (0, 0)))
    pair_gain_row = pair_gain.reshape(1, pair_width)
    bias_flat = pair_forward(pair_flat, pair_gain_row, pair_wt, heads_all)
    bias_rows = bias_flat.reshape(heads_all, rows, length)
    heads_own = proj // DH
    biases = trade_blocks(bias_rows, head, heads_own, 0, 1)

    residues = x_rows.astype(jnp.float32)
    norm_in, inv_in = layer_norm(residues)
    normed_a = (norm_in * (1.0 + scale_a) + shift_a).astype(jnp.bfloat16)
    projected = jnp.concatenate(
        [jnp.dot(normed_a, qkv_weight[:, t, :], preferred_element_type=jnp.float32) for t in range(3)],
        axis=1,
    ).astype(jnp.bfloat16)
    queries = head_split(projected[:, :proj])
    keys = head_split(projected[:, proj : 2 * proj])
    values = head_split(projected[:, 2 * proj :])
    scores = jnp.einsum("qhe,khe->hqk", queries, keys, preferred_element_type=jnp.float32)
    scores = scores * DH ** (-0.5) + biases.astype(jnp.float32)
    scores = jnp.where(valid[None, None, :], scores, masked_score)
    row_max = jnp.max(scores, axis=-1, keepdims=True)
    exp_scores = jnp.exp(scores - row_max)
    row_total = jnp.sum(exp_scores, axis=-1, keepdims=True)
    attn_probs = exp_scores / row_total
    probs_low = attn_probs.astype(jnp.bfloat16)
    mixed = jnp.einsum("hqk,khe->qhe", probs_low, values, preferred_element_type=jnp.float32)
    mixed = mixed.reshape(length, proj).astype(jnp.bfloat16)
    mixed_all = jnp.where(
        first,
        jnp.concatenate([mixed, swap_heads(mixed)], axis=1),
        jnp.concatenate([swap_heads(mixed), mixed], axis=1),
    )
    attn_branch = jnp.dot(mixed_all, out_weight_all, preferred_element_type=jnp.float32) + out_bias
    sig_a = jax.nn.sigmoid(gate_a)
    middle = residues + sig_a * attn_branch

    norm_mid, inv_mid = layer_norm(middle)
    normed_t = (norm_mid * (1.0 + scale_t) + shift_t).astype(jnp.bfloat16)
    gate_up = jnp.dot(normed_t, gate_up_w, preferred_element_type=jnp.float32)
    gate_pre = gate_up[:, :ffn]
    up_pre = gate_up[:, ffn:]
    hidden = (jax.nn.silu(gate_pre) * up_pre).astype(jnp.bfloat16)
    ffn_part = jnp.dot(hidden, down_weight, preferred_element_type=jnp.float32).astype(jnp.bfloat16)
    ffn_branch = ffn_part.astype(jnp.float32) + swap_heads(ffn_part).astype(jnp.float32)
    sig_t = jax.nn.sigmoid(gate_t)
    layer_output = own_rows((middle + sig_t * ffn_branch).astype(jnp.bfloat16)[None], head, rows)

    grad_out = g_rows.astype(jnp.float32)
    d_ffn = (grad_out * sig_t).astype(jnp.bfloat16)
    d_gate_t = jnp.sum(grad_out * ffn_branch * sig_t * (1.0 - sig_t), axis=0, keepdims=True)
    down_grad_t = lax.dot_general(
        d_ffn, hidden, (((0,), (0,)), ((), ())), preferred_element_type=jnp.float32
    )
    d_hidden = lax.dot_general(
        d_ffn, down_weight, (((1,), (1,)), ((), ())), preferred_element_type=jnp.float32
    )
    d_gate = d_hidden * up_pre * silu_slope(gate_pre)
    d_up = d_hidden * jax.nn.silu(gate_pre)
    d_gate_up = jnp.concatenate([d_gate, d_up], axis=1).astype(jnp.bfloat16)
    gate_up_grad = lax.dot_general(
        normed_t, d_gate_up, (((0,), (0,)), ((), ())), preferred_element_type=jnp.float32
    )
    ffn_in_part = lax.dot_general(
        d_gate_up, gate_up_w, (((1,), (1,)), ((), ())), preferred_element_type=jnp.float32
    )
    d_normed_t = head_sum_low(ffn_in_part)
    d_middle = grad_out + norm_back(norm_mid, inv_mid, d_normed_t * (1.0 + scale_t))
    d_scale_t = jnp.sum(d_normed_t * norm_mid, axis=0, keepdims=True)
    d_shift_t = jnp.sum(d_normed_t, axis=0, keepdims=True)
    d_attn = d_middle * sig_a
    d_gate_a = jnp.sum(d_middle * attn_branch * sig_a * (1.0 - sig_a), axis=0, keepdims=True)
    d_out_bias = jnp.sum(d_attn, axis=0, keepdims=True)
    d_attn_low = d_attn.astype(jnp.bfloat16)

    out_weight_grad_t = lax.dot_general(
        d_attn_low, mixed, (((0,), (0,)), ((), ())), preferred_element_type=jnp.float32
    )
    d_mixed = head_split(
        lax.dot_general(
            d_attn_low, out_weight, (((1,), (1,)), ((), ())), preferred_element_type=jnp.float32
        ).astype(jnp.bfloat16)
    )
    d_values = jnp.einsum("hqk,qhe->khe", probs_low, d_mixed, preferred_element_type=jnp.float32)
    d_probs = jnp.einsum("qhe,khe->hqk", d_mixed, values, preferred_element_type=jnp.float32)
    d_scores = (
        attn_probs * (d_probs - jnp.sum(d_probs * attn_probs, axis=-1, keepdims=True))
    ).astype(jnp.bfloat16)
    d_queries = jnp.einsum(
        "hqk,khe->qhe", d_scores, keys, preferred_element_type=jnp.float32
    ) * DH ** (-0.5)
    d_keys = jnp.einsum(
        "hqk,qhe->khe", d_scores, queries, preferred_element_type=jnp.float32
    ) * DH ** (-0.5)
    d_qkv = jnp.concatenate(
        [d_queries.reshape(length, proj), d_keys.reshape(length, proj), d_values.reshape(length, proj)],
        axis=1,
    ).astype(jnp.bfloat16)
    qkv_grad = lax.dot_general(
        normed_a, d_qkv, (((0,), (0,)), ((), ())), preferred_element_type=jnp.float32
    )

    packed = blank((width, 4 * proj + 3 * ffn), jnp.bfloat16)
    packed = lax.dynamic_update_slice(packed, gate_up_grad.astype(jnp.bfloat16), (0, 4 * proj))
    packed = lax.dynamic_update_slice(
        packed, down_grad_t.astype(jnp.bfloat16), (0, 4 * proj + 2 * ffn)
    )
    packed = lax.dynamic_update_slice(packed, out_weight_grad_t.astype(jnp.bfloat16), (0, 3 * proj))
    packed = lax.dynamic_update_slice(packed, qkv_grad.astype(jnp.bfloat16), (0, 0))
    reduced = lax.psum_scatter(packed, "dp", scatter_dimension=0, tiled=True).astype(jnp.float32)

    attn_in_part = sum(
        lax.dot_general(
            d_qkv[:, t * proj : (t + 1) * proj], qkv_weight[:, t, :], (((1,), (1,)), ((), ())),
            preferred_element_type=jnp.float32,
        )
        for t in range(3)
    ).astype(jnp.bfloat16)
    d_normed_a = attn_in_part.astype(jnp.float32) + swap_heads(attn_in_part).astype(jnp.float32)
    input_grad = own_rows(
        (d_middle + norm_back(norm_in, inv_in, d_normed_a * (1.0 + scale_a)))[None], head, rows
    )
    d_scale_a = jnp.sum(d_normed_a * norm_in, axis=0, keepdims=True)
    d_shift_a = jnp.sum(d_normed_a, axis=0, keepdims=True)
    d_modulation = jnp.concatenate(
        [d_scale_a, d_shift_a, d_gate_a, d_scale_t, d_shift_t, d_gate_t], axis=-1
    )

    d_bias_rows = trade_blocks(d_scores, head, rows, 1, 0)
    d_bias_flat = jnp.pad(d_bias_rows.reshape(heads_all, -1), ((0, HEAD_PAD - heads_all), (0, 0)))
    pair_grad, pair_wg, pair_gg = pair_backward(pair_flat, d_bias_flat, pair_gain_row, pair_wt)
    pair_grad = pair_grad.reshape(pair_input.shape)
    pair_weight_grad = pair_wg[:heads_all].T
    pair_gain_grad = pair_gg[0]

    pair_small = head_sum(
        jnp.concatenate([pair_weight_grad.reshape(-1), pair_gain_grad])[None]
    )
    small = jnp.concatenate([d_modulation, time_cond, d_out_bias], axis=-1)
    small_rows = dp_gather(small)
    mod_size = d_modulation.shape[-1]
    cond_size = time_cond.shape[-1]
    pw_size = pair_weight.size
    mod_chain = small_rows[:, :mod_size]
    cond_chain = small_rows[:, mod_size : mod_size + cond_size]
    out_bias_grad = jnp.sum(small_rows[:, mod_size + cond_size :], axis=0)
    pair_total = dp_sum(pair_small)[0]
    pair_weight_grad = pair_total[:pw_size].reshape(pair_weight.shape)
    pair_gain_grad = pair_total[pw_size:]
    cond_act = lax.optimization_barrier(jax.nn.silu(cond_chain).astype(jnp.bfloat16)).astype(
        jnp.float32
    )
    mod_weight_grad = jnp.dot(cond_act.T, mod_chain, precision=precise)
    mod_bias_grad = jnp.sum(mod_chain, axis=0)
    cond_grad = jnp.dot(
        d_modulation, mod_weight.astype(jnp.float32).T, precision=precise
    ) * silu_slope(time_cond)

    cuts = [0, 3 * proj, 4 * proj, 4 * proj + 2 * ffn, 4 * proj + 3 * ffn]
    pieces = [reduced[:, cuts[i] : cuts[i + 1]] for i in range(4)]
    qkv_grad = pieces[0].reshape(-1, 3, proj)
    out_weight_grad = pieces[1].T
    gate_up_grad = pieces[2].reshape(-1, 2, ffn)
    down_grad = pieces[3].T
    return (
        layer_output,
        input_grad,
        pair_grad,
        cond_grad,
        mod_weight_grad,
        mod_bias_grad,
        qkv_grad,
        pair_gain_grad,
        pair_weight_grad,
        out_weight_grad,
        out_bias_grad,
        gate_up_grad,
        down_grad,
    )


def solution(mesh):
    placed = (
        P("dp", "head", None),
        P("dp", "head", None, None),
        P("dp", None),
        P("dp"),
        P("dp", None),
        P(),
        P(),
        P(None, None, "head"),
        P(),
        P(),
        P("head", None),
        P(),
        P(None, None, "head"),
        P("head", None),
        P("dp", "head", None),
    )
    return jax.shard_map(
        shards,
        mesh=mesh,
        in_specs=placed,
        out_specs=(
            P("dp", "head", None),
            P("dp", "head", None),
            P("dp", "head", None, None),
            P("dp", None),
            P(),
            P(),
            P("dp", None, "head"),
            P(),
            P(),
            P("head", "dp"),
            P(),
            P("dp", None, "head"),
            P("head", "dp"),
        ),
        check_vma=False,
    )
```

```python
import jax
import jax.numpy as jnp
from jax import lax
from jax.experimental import pallas as pl
from jax.experimental.pallas import tpu as pltpu
from jax.sharding import PartitionSpec as P

DH = 64


epsilon = 1e-05
masked_score = -1000000000.0
precise = lax.Precision.HIGHEST
LANES = 128
PAIR_TILE = 4096
PAIR_BACK_TILE = 2048
HEAD_PAD = 16


def blank_kernel(out_ref):
    del out_ref


def blank(shape, dtype):
    return pl.pallas_call(
        blank_kernel,
        out_shape=jax.ShapeDtypeStruct(shape, dtype),
        out_specs=pl.BlockSpec(memory_space=pl.ANY),
    )()


def pair_stats(x):
    centred = x - jnp.mean(x, axis=-1, keepdims=True)
    inv_std = lax.rsqrt(jnp.mean(centred * centred, axis=-1, keepdims=True) + epsilon)
    return centred * inv_std, inv_std


def pair_forward_kernel(x_ref, gain_ref, wt_ref, bias_ref):
    normed, _ = pair_stats(x_ref[...].astype(jnp.float32))
    scaled = (normed * gain_ref[...]).astype(jnp.bfloat16)
    bias = lax.dot_general(
        wt_ref[...], scaled, (((0,), (1,)), ((), ())), preferred_element_type=jnp.float32
    )
    bias_ref[...] = bias.astype(bias_ref.dtype)


def pair_forward(flat, gain, wt, heads):
    m, width = flat.shape
    tile = min(PAIR_TILE, m)
    return pl.pallas_call(
        pair_forward_kernel,
        grid=(m // tile,),
        in_specs=[
            pl.BlockSpec((tile, width), lambda i: (i, 0)),
            pl.BlockSpec((1, width), lambda i: (0, 0)),
            pl.BlockSpec(wt.shape, lambda i: (0, 0)),
        ],
        out_specs=pl.BlockSpec((heads, tile), lambda i: (0, i)),
        out_shape=jax.ShapeDtypeStruct((heads, m), jnp.bfloat16),
        cost_estimate=pl.CostEstimate(
            flops=m * width * (2 * HEAD_PAD + 10),
            transcendentals=m,
            bytes_accessed=m * width * 2 + heads * m * 2,
        ),
    )(flat, gain, wt)


def pair_backward_kernel(x_ref, ds_ref, gain_ref, wt_ref, grad_ref, wg_ref, gg_ref):
    step = pl.program_id(0)
    normed, inv_std = pair_stats(x_ref[...].astype(jnp.float32))
    gain = gain_ref[...]
    scaled = (normed * gain).astype(jnp.bfloat16)
    ds = ds_ref[...]
    d_scaled = lax.dot_general(
        ds, wt_ref[...], (((0,), (0,)), ((), ())), preferred_element_type=jnp.float32
    )
    wg = lax.dot_general(ds, scaled, (((1,), (0,)), ((), ())), preferred_element_type=jnp.float32)
    gg = jnp.sum(d_scaled * normed, axis=0, keepdims=True)
    d_normed = d_scaled * gain
    mean_grad = jnp.mean(d_normed, axis=-1, keepdims=True)
    mean_proj = jnp.mean(d_normed * normed, axis=-1, keepdims=True)
    grad_ref[...] = (inv_std * (d_normed - mean_grad - normed * mean_proj)).astype(grad_ref.dtype)

    @pl.when(step == 0)
    def _():
        wg_ref[...] = jnp.zeros_like(wg_ref)
        gg_ref[...] = jnp.zeros_like(gg_ref)

    wg_ref[...] += wg
    gg_ref[...] += gg


def pair_backward(flat, ds, gain, wt):
    m, width = flat.shape
    tile = min(PAIR_BACK_TILE, m)
    pad = ds.shape[0]
    return pl.pallas_call(
        pair_backward_kernel,
        grid=(m // tile,),
        in_specs=[
            pl.BlockSpec((tile, width), lambda i: (i, 0)),
            pl.BlockSpec((pad, tile), lambda i: (0, i)),
            pl.BlockSpec((1, width), lambda i: (0, 0)),
            pl.BlockSpec(wt.shape, lambda i: (0, 0)),
        ],
        out_specs=[
            pl.BlockSpec((tile, width), lambda i: (i, 0)),
            pl.BlockSpec((pad, width), lambda i: (0, 0)),
            pl.BlockSpec((1, width), lambda i: (0, 0)),
        ],
        out_shape=[
            jax.ShapeDtypeStruct((m, width), jnp.bfloat16),
            jax.ShapeDtypeStruct((pad, width), jnp.float32),
            jax.ShapeDtypeStruct((1, width), jnp.float32),
        ],
        compiler_params=pltpu.CompilerParams(dimension_semantics=("arbitrary",)),
        cost_estimate=pl.CostEstimate(
            flops=m * width * (4 * HEAD_PAD + 20),
            transcendentals=m,
            bytes_accessed=2 * m * width * 2 + pad * m * 2,
        ),
    )(flat, ds, gain, wt)


def layer_norm(values):
    centred = values - jnp.mean(values, axis=-1, keepdims=True)
    inv_std = lax.rsqrt(jnp.mean(centred * centred, axis=-1, keepdims=True) + epsilon)
    return (centred * inv_std, inv_std)


def norm_back(normed, inv_std, grad):
    mean_grad = jnp.mean(grad, axis=-1, keepdims=True)
    mean_proj = jnp.mean(grad * normed, axis=-1, keepdims=True)
    return inv_std * (grad - mean_grad - normed * mean_proj)


def silu_slope(values):
    sigma = jax.nn.sigmoid(values)
    return sigma * (1.0 + values * (1.0 - sigma))


def head_split(values):
    return values.reshape(values.shape[:-1] + (values.shape[-1] // DH, DH))


def swap_heads(values):
    return lax.ppermute(values, "head", [(0, 1), (1, 0)])


def whole_rows(own, first):
    other = swap_heads(own)
    return jnp.where(
        first,
        jnp.concatenate([own, other], axis=0),
        jnp.concatenate([other, own], axis=0),
    )


def dp_gather(values):
    count = lax.axis_size("dp")
    index = lax.axis_index("dp")
    block = values
    step = 1
    while step < count:
        other = lax.ppermute(block, "dp", [(i, i ^ step) for i in range(count)])
        block = jnp.where(
            (index & step) == 0,
            jnp.concatenate([block, other], axis=0),
            jnp.concatenate([other, block], axis=0),
        )
        step *= 2
    return block


def dp_sum(values):
    count = lax.axis_size("dp")
    index = lax.axis_index("dp")
    step = 1
    while step < count:
        other = lax.ppermute(values, "dp", [(i, i ^ step) for i in range(count)])
        values = jnp.where((index & step) == 0, values + other, other + values)
        step *= 2
    return values


def own_rows(values, head, rows):
    return lax.dynamic_slice_in_dim(values, head * rows, rows, 1)


def head_sum(part):
    return part + swap_heads(part)


def head_sum_low(part):
    low = part.astype(jnp.bfloat16)
    return low.astype(jnp.float32) + swap_heads(low).astype(jnp.float32)


def trade_blocks(values, head, size, axis, mine_axis):
    mine = lax.dynamic_slice_in_dim(values, head * size, size, axis)
    theirs = swap_heads(lax.dynamic_slice_in_dim(values, (1 - head) * size, size, axis))
    return jnp.where(
        head == 0,
        jnp.concatenate([mine, theirs], axis=mine_axis),
        jnp.concatenate([theirs, mine], axis=mine_axis),
    )


def attn_scores(queries, keys, biases, valid):
    scores = jnp.einsum("cqhe,ckhe->chqk", queries, keys, preferred_element_type=jnp.float32)
    scores = scores * DH ** (-0.5) + biases.astype(jnp.float32)
    return jnp.where(valid[:, None, None, :], scores, masked_score)


def to_chunks(values, parts):
    return values.reshape(parts, -1, LANES)


def shards(
    layer_input,
    pair_input,
    time_cond,
    chain_lengths,
    residue_mask,
    mod_weight,
    mod_bias,
    qkv_weight,
    pair_gain,
    pair_weight,
    out_weight,
    out_bias,
    gate_up_weight,
    down_weight,
    output_grad,
):
    assert layer_input.shape[0] == 1
    rows = layer_input.shape[1]
    width = layer_input.shape[2]
    length = residue_mask.shape[1]
    head = lax.axis_index("head")
    first = head == 0
    data_count = lax.axis_size("dp")
    proj = qkv_weight.shape[2]
    ffn = gate_up_weight.shape[2]
    qkv_w = qkv_weight.reshape(width, 3 * proj)
    gate_up_w = gate_up_weight.reshape(width, 2 * ffn)

    x_rows = whole_rows(layer_input[0], first)
    g_rows = whole_rows(output_grad[0], first)
    out_weight_all = whole_rows(out_weight, first)

    positions = jnp.arange(length, dtype=jnp.int32)
    valid = (positions < chain_lengths[0]) & ((residue_mask[0] == 1) | (positions == 0))
    silu_cond = jax.nn.silu(time_cond).astype(jnp.bfloat16)
    modulation = jnp.dot(silu_cond, mod_weight, preferred_element_type=jnp.float32) + mod_bias
    scale_a, shift_a, gate_a, scale_t, shift_t, gate_t = [
        modulation[:, section * width : (section + 1) * width] for section in range(6)
    ]

    heads_all = pair_weight.shape[1]
    pair_width = pair_input.shape[-1]
    pair_flat = pair_input.reshape(-1, pair_width)
    pair_wt = jnp.pad(pair_weight.T, ((0, HEAD_PAD - heads_all), (0, 0)))
    pair_gain_row = pair_gain.reshape(1, pair_width)
    bias_flat = pair_forward(pair_flat, pair_gain_row, pair_weight, heads_all)
    bias_rows = bias_flat.reshape(heads_all, rows, length)
    heads_own = proj // DH
    biases = trade_blocks(bias_rows, head, heads_own, 0, 1)

    residues = x_rows.astype(jnp.float32)
    norm_in, inv_in = layer_norm(residues)
    normed_a = (norm_in * (1.0 + scale_a) + shift_a).astype(jnp.bfloat16)
    projected = jnp.dot(normed_a, qkv_w, preferred_element_type=jnp.float32).astype(jnp.bfloat16)
    queries = head_split(projected[:, :proj])
    keys = head_split(projected[:, proj : 2 * proj])
    values = head_split(projected[:, 2 * proj :])
    scores = jnp.einsum("qhe,khe->hqk", queries, keys, preferred_element_type=jnp.float32)
    scores = scores * DH ** (-0.5) + biases.astype(jnp.float32)
    scores = jnp.where(valid[None, None, :], scores, masked_score)
    row_max = jnp.max(scores, axis=-1, keepdims=True)
    exp_scores = jnp.exp(scores - row_max)
    row_total = jnp.sum(exp_scores, axis=-1, keepdims=True)
    attn_probs = exp_scores / row_total
    probs_low = attn_probs.astype(jnp.bfloat16)
    mixed = jnp.einsum("hqk,khe->qhe", probs_low, values, preferred_element_type=jnp.float32)
    mixed = mixed.reshape(length, proj).astype(jnp.bfloat16)
    mixed_all = jnp.where(
        first,
        jnp.concatenate([mixed, swap_heads(mixed)], axis=1),
        jnp.concatenate([swap_heads(mixed), mixed], axis=1),
    )
    attn_branch = jnp.dot(mixed_all, out_weight_all, preferred_element_type=jnp.float32) + out_bias
    sig_a = jax.nn.sigmoid(gate_a)
    middle = residues + sig_a * attn_branch

    norm_mid, inv_mid = layer_norm(middle)
    normed_t = (norm_mid * (1.0 + scale_t) + shift_t).astype(jnp.bfloat16)
    gate_up = jnp.dot(normed_t, gate_up_w, preferred_element_type=jnp.float32)
    gate_pre = gate_up[:, :ffn]
    up_pre = gate_up[:, ffn:]
    hidden = (jax.nn.silu(gate_pre) * up_pre).astype(jnp.bfloat16)
    ffn_part = jnp.dot(hidden, down_weight, preferred_element_type=jnp.float32).astype(jnp.bfloat16)
    ffn_branch = ffn_part.astype(jnp.float32) + swap_heads(ffn_part).astype(jnp.float32)
    sig_t = jax.nn.sigmoid(gate_t)
    layer_output = own_rows((middle + sig_t * ffn_branch).astype(jnp.bfloat16)[None], head, rows)

    grad_out = g_rows.astype(jnp.float32)
    d_ffn = (grad_out * sig_t).astype(jnp.bfloat16)
    d_gate_t = jnp.sum(grad_out * ffn_branch * sig_t * (1.0 - sig_t), axis=0, keepdims=True)
    down_grad_t = lax.dot_general(
        d_ffn, hidden, (((0,), (0,)), ((), ())), preferred_element_type=jnp.float32
    )
    d_hidden = lax.dot_general(
        d_ffn, down_weight, (((1,), (1,)), ((), ())), preferred_element_type=jnp.float32
    )
    d_gate = d_hidden * up_pre * silu_slope(gate_pre)
    d_up = d_hidden * jax.nn.silu(gate_pre)
    d_gate_up = jnp.concatenate([d_gate, d_up], axis=1).astype(jnp.bfloat16)
    gate_up_grad = lax.dot_general(
        normed_t, d_gate_up, (((0,), (0,)), ((), ())), preferred_element_type=jnp.float32
    )
    ffn_in_part = lax.dot_general(
        d_gate_up, gate_up_w, (((1,), (1,)), ((), ())), preferred_element_type=jnp.float32
    )
    d_normed_t = head_sum_low(ffn_in_part)
    d_middle = grad_out + norm_back(norm_mid, inv_mid, d_normed_t * (1.0 + scale_t))
    d_scale_t = jnp.sum(d_normed_t * norm_mid, axis=0, keepdims=True)
    d_shift_t = jnp.sum(d_normed_t, axis=0, keepdims=True)
    d_attn = d_middle * sig_a
    d_gate_a = jnp.sum(d_middle * attn_branch * sig_a * (1.0 - sig_a), axis=0, keepdims=True)
    d_out_bias = jnp.sum(d_attn, axis=0, keepdims=True)
    d_attn_low = d_attn.astype(jnp.bfloat16)

    out_weight_grad_t = lax.dot_general(
        d_attn_low, mixed, (((0,), (0,)), ((), ())), preferred_element_type=jnp.float32
    )
    d_mixed = head_split(
        lax.dot_general(
            d_attn_low, out_weight, (((1,), (1,)), ((), ())), preferred_element_type=jnp.float32
        ).astype(jnp.bfloat16)
    )
    d_values = jnp.einsum("hqk,qhe->khe", probs_low, d_mixed, preferred_element_type=jnp.float32)
    d_probs = jnp.einsum("qhe,khe->hqk", d_mixed, values, preferred_element_type=jnp.float32)
    d_scores = (
        attn_probs * (d_probs - jnp.sum(d_probs * attn_probs, axis=-1, keepdims=True))
    ).astype(jnp.bfloat16)
    d_queries = jnp.einsum(
        "hqk,khe->qhe", d_scores, keys, preferred_element_type=jnp.float32
    ) * DH ** (-0.5)
    d_keys = jnp.einsum(
        "hqk,qhe->khe", d_scores, queries, preferred_element_type=jnp.float32
    ) * DH ** (-0.5)
    d_qkv = jnp.concatenate(
        [d_queries.reshape(length, proj), d_keys.reshape(length, proj), d_values.reshape(length, proj)],
        axis=1,
    ).astype(jnp.bfloat16)
    qkv_grad = lax.dot_general(
        normed_a, d_qkv, (((0,), (0,)), ((), ())), preferred_element_type=jnp.float32
    )

    packed = blank((width, 4 * proj + 3 * ffn), jnp.bfloat16)
    packed = lax.dynamic_update_slice(packed, gate_up_grad.astype(jnp.bfloat16), (0, 4 * proj))
    packed = lax.dynamic_update_slice(
        packed, down_grad_t.astype(jnp.bfloat16), (0, 4 * proj + 2 * ffn)
    )
    packed = lax.dynamic_update_slice(packed, out_weight_grad_t.astype(jnp.bfloat16), (0, 3 * proj))
    packed = lax.dynamic_update_slice(packed, qkv_grad.astype(jnp.bfloat16), (0, 0))
    reduced = lax.psum_scatter(packed, "dp", scatter_dimension=0, tiled=True).astype(jnp.float32)

    attn_in_part = lax.dot_general(
        d_qkv, qkv_w, (((1,), (1,)), ((), ())), preferred_element_type=jnp.float32
    ).astype(jnp.bfloat16)
    d_normed_a = attn_in_part.astype(jnp.float32) + swap_heads(attn_in_part).astype(jnp.float32)
    input_grad = own_rows(
        (d_middle + norm_back(norm_in, inv_in, d_normed_a * (1.0 + scale_a)))[None], head, rows
    )
    d_scale_a = jnp.sum(d_normed_a * norm_in, axis=0, keepdims=True)
    d_shift_a = jnp.sum(d_normed_a, axis=0, keepdims=True)
    d_modulation = jnp.concatenate(
        [d_scale_a, d_shift_a, d_gate_a, d_scale_t, d_shift_t, d_gate_t], axis=-1
    )

    d_bias_rows = trade_blocks(d_scores, head, rows, 1, 0)
    d_bias_flat = jnp.pad(d_bias_rows.reshape(heads_all, -1), ((0, HEAD_PAD - heads_all), (0, 0)))
    pair_grad, pair_wg, pair_gg = pair_backward(pair_flat, d_bias_flat, pair_gain_row, pair_wt)
    pair_grad = pair_grad.reshape(pair_input.shape)
    pair_weight_grad = pair_wg[:heads_all].T
    pair_gain_grad = pair_gg[0]

    pair_small = head_sum(
        jnp.concatenate([pair_weight_grad.reshape(-1), pair_gain_grad])[None]
    )
    small = jnp.concatenate([d_modulation, time_cond, d_out_bias], axis=-1)
    small_rows = dp_gather(small)
    mod_size = d_modulation.shape[-1]
    cond_size = time_cond.shape[-1]
    pw_size = pair_weight.size
    mod_chain = small_rows[:, :mod_size]
    cond_chain = small_rows[:, mod_size : mod_size + cond_size]
    out_bias_grad = jnp.sum(small_rows[:, mod_size + cond_size :], axis=0)
    pair_total = dp_sum(pair_small)[0]
    pair_weight_grad = pair_total[:pw_size].reshape(pair_weight.shape)
    pair_gain_grad = pair_total[pw_size:]
    cond_act = lax.optimization_barrier(jax.nn.silu(cond_chain).astype(jnp.bfloat16)).astype(
        jnp.float32
    )
    mod_weight_grad = jnp.dot(cond_act.T, mod_chain, precision=precise)
    mod_bias_grad = jnp.sum(mod_chain, axis=0)
    cond_grad = jnp.dot(
        d_modulation, mod_weight.astype(jnp.float32).T, precision=precise
    ) * silu_slope(time_cond)

    cuts = [0, 3 * proj, 4 * proj, 4 * proj + 2 * ffn, 4 * proj + 3 * ffn]
    pieces = [reduced[:, cuts[i] : cuts[i + 1]] for i in range(4)]
    qkv_grad = pieces[0].reshape(-1, 3, proj)
    out_weight_grad = pieces[1].T
    gate_up_grad = pieces[2].reshape(-1, 2, ffn)
    down_grad = pieces[3].T
    return (
        layer_output,
        input_grad,
        pair_grad,
        cond_grad,
        mod_weight_grad,
        mod_bias_grad,
        qkv_grad,
        pair_gain_grad,
        pair_weight_grad,
        out_weight_grad,
        out_bias_grad,
        gate_up_grad,
        down_grad,
    )


def solution(mesh):
    placed = (
        P("dp", "head", None),
        P("dp", "head", None, None),
        P("dp", None),
        P("dp"),
        P("dp", None),
        P(),
        P(),
        P(None, None, "head"),
        P(),
        P(),
        P("head", None),
        P(),
        P(None, None, "head"),
        P("head", None),
        P("dp", "head", None),
    )
    return jax.shard_map(
        shards,
        mesh=mesh,
        in_specs=placed,
        out_specs=(
            P("dp", "head", None),
            P("dp", "head", None),
            P("dp", "head", None, None),
            P("dp", None),
            P(),
            P(),
            P("dp", None, "head"),
            P(),
            P(),
            P("head", "dp"),
            P(),
            P("dp", None, "head"),
            P("head", "dp"),
        ),
        check_vma=False,
    )
```

```python
import jax
import jax.numpy as jnp
from jax import lax
from jax.experimental import pallas as pl
from jax.experimental.pallas import tpu as pltpu
from jax.sharding import PartitionSpec as P

DH = 64


epsilon = 1e-05
masked_score = -1000000000.0
precise = lax.Precision.HIGHEST
LANES = 128
PAIR_TILE = 4096
PAIR_BACK_TILE = 2048
HEAD_PAD = 16


def blank_kernel(out_ref):
    del out_ref


def blank(shape, dtype):
    return pl.pallas_call(
        blank_kernel,
        out_shape=jax.ShapeDtypeStruct(shape, dtype),
        out_specs=pl.BlockSpec(memory_space=pl.ANY),
    )()


def pair_stats(x):
    centred = x - jnp.mean(x, axis=-1, keepdims=True)
    inv_std = lax.rsqrt(jnp.mean(centred * centred, axis=-1, keepdims=True) + epsilon)
    return centred * inv_std, inv_std


def pair_forward_kernel(x_ref, gain_ref, wt_ref, bias_ref):
    normed, _ = pair_stats(x_ref[...].astype(jnp.float32))
    scaled = (normed * gain_ref[...]).astype(jnp.bfloat16)
    bias = lax.dot_general(
        wt_ref[...], scaled, (((0,), (1,)), ((), ())), preferred_element_type=jnp.float32
    )
    bias_ref[...] = bias.astype(bias_ref.dtype)


def pair_forward(flat, gain, wt, heads):
    m, width = flat.shape
    tile = min(PAIR_TILE, m)
    return pl.pallas_call(
        pair_forward_kernel,
        grid=(m // tile,),
        in_specs=[
            pl.BlockSpec((tile, width), lambda i: (i, 0)),
            pl.BlockSpec((1, width), lambda i: (0, 0)),
            pl.BlockSpec(wt.shape, lambda i: (0, 0)),
        ],
        out_specs=pl.BlockSpec((heads, tile), lambda i: (0, i)),
        out_shape=jax.ShapeDtypeStruct((heads, m), jnp.bfloat16),
        cost_estimate=pl.CostEstimate(
            flops=m * width * (2 * HEAD_PAD + 10),
            transcendentals=m,
            bytes_accessed=m * width * 2 + heads * m * 2,
        ),
    )(flat, gain, wt)


def pair_backward_kernel(x_ref, ds_ref, gain_ref, wt_ref, grad_ref, wg_ref, gg_ref):
    step = pl.program_id(0)
    normed, inv_std = pair_stats(x_ref[...].astype(jnp.float32))
    gain = gain_ref[...]
    scaled = (normed * gain).astype(jnp.bfloat16)
    ds = ds_ref[...]
    d_scaled = lax.dot_general(
        ds, wt_ref[...], (((0,), (0,)), ((), ())), preferred_element_type=jnp.float32
    )
    wg = lax.dot_general(ds, scaled, (((1,), (0,)), ((), ())), preferred_element_type=jnp.float32)
    gg = jnp.sum(d_scaled * normed, axis=0, keepdims=True)
    d_normed = d_scaled * gain
    mean_grad = jnp.mean(d_normed, axis=-1, keepdims=True)
    mean_proj = jnp.mean(d_normed * normed, axis=-1, keepdims=True)
    grad_ref[...] = (inv_std * (d_normed - mean_grad - normed * mean_proj)).astype(grad_ref.dtype)

    @pl.when(step == 0)
    def _():
        wg_ref[...] = jnp.zeros_like(wg_ref)
        gg_ref[...] = jnp.zeros_like(gg_ref)

    wg_ref[...] += wg
    gg_ref[...] += gg


def pair_backward(flat, ds, gain, wt):
    m, width = flat.shape
    tile = min(PAIR_BACK_TILE, m)
    pad = ds.shape[0]
    return pl.pallas_call(
        pair_backward_kernel,
        grid=(m // tile,),
        in_specs=[
            pl.BlockSpec((tile, width), lambda i: (i, 0)),
            pl.BlockSpec((pad, tile), lambda i: (0, i)),
            pl.BlockSpec((1, width), lambda i: (0, 0)),
            pl.BlockSpec(wt.shape, lambda i: (0, 0)),
        ],
        out_specs=[
            pl.BlockSpec((tile, width), lambda i: (i, 0)),
            pl.BlockSpec((pad, width), lambda i: (0, 0)),
            pl.BlockSpec((1, width), lambda i: (0, 0)),
        ],
        out_shape=[
            jax.ShapeDtypeStruct((m, width), jnp.bfloat16),
            jax.ShapeDtypeStruct((pad, width), jnp.float32),
            jax.ShapeDtypeStruct((1, width), jnp.float32),
        ],
        compiler_params=pltpu.CompilerParams(dimension_semantics=("arbitrary",)),
        cost_estimate=pl.CostEstimate(
            flops=m * width * (4 * HEAD_PAD + 20),
            transcendentals=m,
            bytes_accessed=2 * m * width * 2 + pad * m * 2,
        ),
    )(flat, ds, gain, wt)


def layer_norm(values):
    centred = values - jnp.mean(values, axis=-1, keepdims=True)
    inv_std = lax.rsqrt(jnp.mean(centred * centred, axis=-1, keepdims=True) + epsilon)
    return (centred * inv_std, inv_std)


def norm_back(normed, inv_std, grad):
    mean_grad = jnp.mean(grad, axis=-1, keepdims=True)
    mean_proj = jnp.mean(grad * normed, axis=-1, keepdims=True)
    return inv_std * (grad - mean_grad - normed * mean_proj)


def silu_slope(values):
    sigma = jax.nn.sigmoid(values)
    return sigma * (1.0 + values * (1.0 - sigma))


def head_split(values):
    return values.reshape(values.shape[:-1] + (values.shape[-1] // DH, DH))


def swap_heads(values):
    return lax.ppermute(values, "head", [(0, 1), (1, 0)])


def whole_rows(own, first):
    other = swap_heads(own)
    return jnp.where(
        first,
        jnp.concatenate([own, other], axis=0),
        jnp.concatenate([other, own], axis=0),
    )


def dp_gather(values):
    count = lax.axis_size("dp")
    index = lax.axis_index("dp")
    block = values
    step = 1
    while step < count:
        other = lax.ppermute(block, "dp", [(i, i ^ step) for i in range(count)])
        block = jnp.where(
            (index & step) == 0,
            jnp.concatenate([block, other], axis=0),
            jnp.concatenate([other, block], axis=0),
        )
        step *= 2
    return block


def dp_sum(values):
    count = lax.axis_size("dp")
    index = lax.axis_index("dp")
    step = 1
    while step < count:
        other = lax.ppermute(values, "dp", [(i, i ^ step) for i in range(count)])
        values = jnp.where((index & step) == 0, values + other, other + values)
        step *= 2
    return values


def own_rows(values, head, rows):
    return lax.dynamic_slice_in_dim(values, head * rows, rows, 1)


def head_sum(part):
    return part + swap_heads(part)


def head_sum_low(part):
    low = part.astype(jnp.bfloat16)
    return low.astype(jnp.float32) + swap_heads(low).astype(jnp.float32)


def trade_blocks(values, head, size, axis, mine_axis):
    mine = lax.dynamic_slice_in_dim(values, head * size, size, axis)
    theirs = swap_heads(lax.dynamic_slice_in_dim(values, (1 - head) * size, size, axis))
    return jnp.where(
        head == 0,
        jnp.concatenate([mine, theirs], axis=mine_axis),
        jnp.concatenate([theirs, mine], axis=mine_axis),
    )


def attn_scores(queries, keys, biases, valid):
    scores = jnp.einsum("cqhe,ckhe->chqk", queries, keys, preferred_element_type=jnp.float32)
    scores = scores * DH ** (-0.5) + biases.astype(jnp.float32)
    return jnp.where(valid[:, None, None, :], scores, masked_score)


def to_chunks(values, parts):
    return values.reshape(parts, -1, LANES)


def shards(
    layer_input,
    pair_input,
    time_cond,
    chain_lengths,
    residue_mask,
    mod_weight,
    mod_bias,
    qkv_weight,
    pair_gain,
    pair_weight,
    out_weight,
    out_bias,
    gate_up_weight,
    down_weight,
    output_grad,
):
    assert layer_input.shape[0] == 1
    rows = layer_input.shape[1]
    width = layer_input.shape[2]
    length = residue_mask.shape[1]
    head = lax.axis_index("head")
    first = head == 0
    data_count = lax.axis_size("dp")
    proj = qkv_weight.shape[2]
    ffn = gate_up_weight.shape[2]
    qkv_w = qkv_weight.reshape(width, 3 * proj)
    gate_up_w = gate_up_weight.reshape(width, 2 * ffn)

    x_rows = whole_rows(layer_input[0], first)
    g_rows = whole_rows(output_grad[0], first)
    out_weight_all = whole_rows(out_weight, first)

    positions = jnp.arange(length, dtype=jnp.int32)
    valid = (positions < chain_lengths[0]) & ((residue_mask[0] == 1) | (positions == 0))
    silu_cond = jax.nn.silu(time_cond).astype(jnp.bfloat16)
    modulation = jnp.dot(silu_cond, mod_weight, preferred_element_type=jnp.float32) + mod_bias
    scale_a, shift_a, gate_a, scale_t, shift_t, gate_t = [
        modulation[:, section * width : (section + 1) * width] for section in range(6)
    ]

    heads_all = pair_weight.shape[1]
    pair_width = pair_input.shape[-1]
    pair_flat = pair_input.reshape(-1, pair_width)
    pair_wt = jnp.pad(pair_weight.T, ((0, HEAD_PAD - heads_all), (0, 0)))
    pair_gain_row = pair_gain.reshape(1, pair_width)
    bias_flat = pair_forward(pair_flat, pair_gain_row, pair_weight, heads_all)
    bias_rows = bias_flat.reshape(heads_all, rows, length)
    heads_own = proj // DH
    biases = trade_blocks(bias_rows, head, heads_own, 0, 1)

    residues = x_rows.astype(jnp.float32)
    norm_in, inv_in = layer_norm(residues)
    normed_a = (norm_in * (1.0 + scale_a) + shift_a).astype(jnp.bfloat16)
    projected = jnp.dot(normed_a, qkv_w, preferred_element_type=jnp.float32).astype(jnp.bfloat16)
    queries = head_split(projected[:, :proj])
    keys = head_split(projected[:, proj : 2 * proj])
    values = head_split(projected[:, 2 * proj :])
    scores = jnp.einsum("qhe,khe->hqk", queries, keys, preferred_element_type=jnp.float32)
    scores = scores * DH ** (-0.5) + biases.astype(jnp.float32)
    scores = jnp.where(valid[None, None, :], scores, masked_score)
    row_max = jnp.max(scores, axis=-1, keepdims=True)
    exp_scores = jnp.exp(scores - row_max)
    row_total = jnp.sum(exp_scores, axis=-1, keepdims=True)
    attn_probs = exp_scores / row_total
    probs_low = attn_probs.astype(jnp.bfloat16)
    mixed = jnp.einsum("hqk,khe->qhe", probs_low, values, preferred_element_type=jnp.float32)
    mixed = mixed.reshape(length, proj).astype(jnp.bfloat16)
    mixed_all = jnp.where(
        first,
        jnp.concatenate([mixed, swap_heads(mixed)], axis=1),
        jnp.concatenate([swap_heads(mixed), mixed], axis=1),
    )
    attn_branch = jnp.dot(mixed_all, out_weight_all, preferred_element_type=jnp.float32) + out_bias
    sig_a = jax.nn.sigmoid(gate_a)
    middle = residues + sig_a * attn_branch

    norm_mid, inv_mid = layer_norm(middle)
    normed_t = (norm_mid * (1.0 + scale_t) + shift_t).astype(jnp.bfloat16)
    gate_up = jnp.dot(normed_t, gate_up_w, preferred_element_type=jnp.float32)
    gate_pre = gate_up[:, :ffn]
    up_pre = gate_up[:, ffn:]
    hidden = (jax.nn.silu(gate_pre) * up_pre).astype(jnp.bfloat16)
    ffn_part = jnp.dot(hidden, down_weight, preferred_element_type=jnp.float32).astype(jnp.bfloat16)
    ffn_branch = ffn_part.astype(jnp.float32) + swap_heads(ffn_part).astype(jnp.float32)
    sig_t = jax.nn.sigmoid(gate_t)
    layer_output = own_rows((middle + sig_t * ffn_branch).astype(jnp.bfloat16)[None], head, rows)

    grad_out = g_rows.astype(jnp.float32)
    d_ffn = (grad_out * sig_t).astype(jnp.bfloat16)
    down_grad_t = lax.dot_general(
        d_ffn, hidden, (((0,), (0,)), ((), ())), preferred_element_type=jnp.float32
    )
    d_hidden = lax.dot_general(
        d_ffn, down_weight, (((1,), (1,)), ((), ())), preferred_element_type=jnp.float32
    )
    d_gate = d_hidden * up_pre * silu_slope(gate_pre)
    d_up = d_hidden * jax.nn.silu(gate_pre)
    d_gate_up = jnp.concatenate([d_gate, d_up], axis=1).astype(jnp.bfloat16)
    gate_up_grad = lax.dot_general(
        normed_t, d_gate_up, (((0,), (0,)), ((), ())), preferred_element_type=jnp.float32
    )
    ffn_in_part = lax.dot_general(
        d_gate_up, gate_up_w, (((1,), (1,)), ((), ())), preferred_element_type=jnp.float32
    )
    d_normed_t = head_sum_low(ffn_in_part)
    d_middle = grad_out + norm_back(norm_mid, inv_mid, d_normed_t * (1.0 + scale_t))
    d_attn = d_middle * sig_a
    d_attn_low = d_attn.astype(jnp.bfloat16)

    out_weight_grad_t = lax.dot_general(
        d_attn_low, mixed, (((0,), (0,)), ((), ())), preferred_element_type=jnp.float32
    )
    d_mixed = head_split(
        lax.dot_general(
            d_attn_low, out_weight, (((1,), (1,)), ((), ())), preferred_element_type=jnp.float32
        ).astype(jnp.bfloat16)
    )
    d_values = jnp.einsum("hqk,qhe->khe", probs_low, d_mixed, preferred_element_type=jnp.float32)
    d_probs = jnp.einsum("qhe,khe->hqk", d_mixed, values, preferred_element_type=jnp.float32)
    d_scores = (
        attn_probs * (d_probs - jnp.sum(d_probs * attn_probs, axis=-1, keepdims=True))
    ).astype(jnp.bfloat16)
    d_queries = jnp.einsum(
        "hqk,khe->qhe", d_scores, keys, preferred_element_type=jnp.float32
    ) * DH ** (-0.5)
    d_keys = jnp.einsum(
        "hqk,qhe->khe", d_scores, queries, preferred_element_type=jnp.float32
    ) * DH ** (-0.5)
    d_qkv = jnp.concatenate(
        [d_queries.reshape(length, proj), d_keys.reshape(length, proj), d_values.reshape(length, proj)],
        axis=1,
    ).astype(jnp.bfloat16)
    qkv_grad = lax.dot_general(
        normed_a, d_qkv, (((0,), (0,)), ((), ())), preferred_element_type=jnp.float32
    )

    late_dnt, late_nm, late_dm, late_ab, late_go, late_ffn, _ = lax.optimization_barrier(
        (d_normed_t, norm_mid, d_middle, attn_branch, grad_out, ffn_branch, qkv_grad)
    )
    d_gate_t = jnp.sum(late_go * late_ffn * sig_t * (1.0 - sig_t), axis=0, keepdims=True)
    d_scale_t = jnp.sum(late_dnt * late_nm, axis=0, keepdims=True)
    d_shift_t = jnp.sum(late_dnt, axis=0, keepdims=True)
    d_gate_a = jnp.sum(late_dm * late_ab * sig_a * (1.0 - sig_a), axis=0, keepdims=True)
    d_out_bias = jnp.sum(late_dm * sig_a, axis=0, keepdims=True)

    packed = blank((width, 4 * proj + 3 * ffn), jnp.bfloat16)
    packed = lax.dynamic_update_slice(packed, gate_up_grad.astype(jnp.bfloat16), (0, 4 * proj))
    packed = lax.dynamic_update_slice(
        packed, down_grad_t.astype(jnp.bfloat16), (0, 4 * proj + 2 * ffn)
    )
    packed = lax.dynamic_update_slice(packed, out_weight_grad_t.astype(jnp.bfloat16), (0, 3 * proj))
    packed = lax.dynamic_update_slice(packed, qkv_grad.astype(jnp.bfloat16), (0, 0))
    reduced = lax.psum_scatter(packed, "dp", scatter_dimension=0, tiled=True).astype(jnp.float32)

    attn_in_part = lax.dot_general(
        d_qkv, qkv_w, (((1,), (1,)), ((), ())), preferred_element_type=jnp.float32
    ).astype(jnp.bfloat16)
    d_normed_a = attn_in_part.astype(jnp.float32) + swap_heads(attn_in_part).astype(jnp.float32)
    input_grad = own_rows(
        (d_middle + norm_back(norm_in, inv_in, d_normed_a * (1.0 + scale_a)))[None], head, rows
    )
    d_scale_a = jnp.sum(d_normed_a * norm_in, axis=0, keepdims=True)
    d_shift_a = jnp.sum(d_normed_a, axis=0, keepdims=True)
    d_modulation = jnp.concatenate(
        [d_scale_a, d_shift_a, d_gate_a, d_scale_t, d_shift_t, d_gate_t], axis=-1
    )

    d_bias_rows = trade_blocks(d_scores, head, rows, 1, 0)
    d_bias_flat = jnp.pad(d_bias_rows.reshape(heads_all, -1), ((0, HEAD_PAD - heads_all), (0, 0)))
    pair_grad, pair_wg, pair_gg = pair_backward(pair_flat, d_bias_flat, pair_gain_row, pair_wt)
    pair_grad = pair_grad.reshape(pair_input.shape)
    pair_weight_grad = pair_wg[:heads_all].T
    pair_gain_grad = pair_gg[0]

    pair_small = head_sum(
        jnp.concatenate([pair_weight_grad.reshape(-1), pair_gain_grad])[None]
    )
    small = jnp.concatenate([d_modulation, time_cond, d_out_bias], axis=-1)
    small_rows = dp_gather(small)
    mod_size = d_modulation.shape[-1]
    cond_size = time_cond.shape[-1]
    pw_size = pair_weight.size
    mod_chain = small_rows[:, :mod_size]
    cond_chain = small_rows[:, mod_size : mod_size + cond_size]
    out_bias_grad = jnp.sum(small_rows[:, mod_size + cond_size :], axis=0)
    pair_total = dp_sum(pair_small)[0]
    pair_weight_grad = pair_total[:pw_size].reshape(pair_weight.shape)
    pair_gain_grad = pair_total[pw_size:]
    cond_act = lax.optimization_barrier(jax.nn.silu(cond_chain).astype(jnp.bfloat16)).astype(
        jnp.float32
    )
    mod_weight_grad = jnp.dot(cond_act.T, mod_chain, precision=precise)
    mod_bias_grad = jnp.sum(mod_chain, axis=0)
    cond_grad = jnp.dot(
        d_modulation, mod_weight.astype(jnp.float32).T, precision=precise
    ) * silu_slope(time_cond)

    cuts = [0, 3 * proj, 4 * proj, 4 * proj + 2 * ffn, 4 * proj + 3 * ffn]
    pieces = [reduced[:, cuts[i] : cuts[i + 1]] for i in range(4)]
    qkv_grad = pieces[0].reshape(-1, 3, proj)
    out_weight_grad = pieces[1].T
    gate_up_grad = pieces[2].reshape(-1, 2, ffn)
    down_grad = pieces[3].T
    return (
        layer_output,
        input_grad,
        pair_grad,
        cond_grad,
        mod_weight_grad,
        mod_bias_grad,
        qkv_grad,
        pair_gain_grad,
        pair_weight_grad,
        out_weight_grad,
        out_bias_grad,
        gate_up_grad,
        down_grad,
    )


def solution(mesh):
    placed = (
        P("dp", "head", None),
        P("dp", "head", None, None),
        P("dp", None),
        P("dp"),
        P("dp", None),
        P(),
        P(),
        P(None, None, "head"),
        P(),
        P(),
        P("head", None),
        P(),
        P(None, None, "head"),
        P("head", None),
        P("dp", "head", None),
    )
    return jax.shard_map(
        shards,
        mesh=mesh,
        in_specs=placed,
        out_specs=(
            P("dp", "head", None),
            P("dp", "head", None),
            P("dp", "head", None, None),
            P("dp", None),
            P(),
            P(),
            P("dp", None, "head"),
            P(),
            P(),
            P("head", "dp"),
            P(),
            P("dp", None, "head"),
            P("head", "dp"),
        ),
        check_vma=False,
    )
```

```python
import jax
import jax.numpy as jnp
from jax import lax
from jax.experimental import pallas as pl
from jax.experimental.pallas import tpu as pltpu
from jax.sharding import PartitionSpec as P

DH = 64


epsilon = 1e-05
masked_score = -1000000000.0
precise = lax.Precision.HIGHEST
LANES = 128
PAIR_TILE = 4096
PAIR_BACK_TILE = 2048
HEAD_PAD = 16


def blank_kernel(out_ref):
    del out_ref


def blank(shape, dtype):
    return pl.pallas_call(
        blank_kernel,
        out_shape=jax.ShapeDtypeStruct(shape, dtype),
        out_specs=pl.BlockSpec(memory_space=pl.ANY),
    )()


def pair_stats(x):
    centred = x - jnp.mean(x, axis=-1, keepdims=True)
    inv_std = lax.rsqrt(jnp.mean(centred * centred, axis=-1, keepdims=True) + epsilon)
    return centred * inv_std, inv_std


def pair_forward_kernel(x_ref, wt_ref, bias_ref):
    normed, _ = pair_stats(x_ref[...].astype(jnp.float32))
    scaled = normed.astype(jnp.bfloat16)
    bias = lax.dot_general(
        wt_ref[...], scaled, (((0,), (1,)), ((), ())), preferred_element_type=jnp.float32
    )
    bias_ref[...] = bias.astype(bias_ref.dtype)


def pair_forward(flat, gain, wt, heads):
    m, width = flat.shape
    tile = min(PAIR_TILE, m)
    wt = (wt.astype(jnp.float32) * gain.reshape(-1, 1)).astype(jnp.bfloat16)
    return pl.pallas_call(
        pair_forward_kernel,
        grid=(m // tile,),
        in_specs=[
            pl.BlockSpec((tile, width), lambda i: (i, 0)),
            pl.BlockSpec(wt.shape, lambda i: (0, 0)),
        ],
        out_specs=pl.BlockSpec((heads, tile), lambda i: (0, i)),
        out_shape=jax.ShapeDtypeStruct((heads, m), jnp.bfloat16),
        cost_estimate=pl.CostEstimate(
            flops=m * width * (2 * HEAD_PAD + 10),
            transcendentals=m,
            bytes_accessed=m * width * 2 + heads * m * 2,
        ),
    )(flat, wt)


def pair_backward_kernel(x_ref, ds_ref, gain_ref, wt_ref, grad_ref, wg_ref, gg_ref):
    step = pl.program_id(0)
    normed, inv_std = pair_stats(x_ref[...].astype(jnp.float32))
    gain = gain_ref[...]
    scaled = (normed * gain).astype(jnp.bfloat16)
    ds = ds_ref[...]
    d_scaled = lax.dot_general(
        ds, wt_ref[...], (((0,), (0,)), ((), ())), preferred_element_type=jnp.float32
    )
    wg = lax.dot_general(ds, scaled, (((1,), (0,)), ((), ())), preferred_element_type=jnp.float32)
    gg = jnp.sum(d_scaled * normed, axis=0, keepdims=True)
    d_normed = d_scaled * gain
    mean_grad = jnp.mean(d_normed, axis=-1, keepdims=True)
    mean_proj = jnp.mean(d_normed * normed, axis=-1, keepdims=True)
    grad_ref[...] = (inv_std * (d_normed - mean_grad - normed * mean_proj)).astype(grad_ref.dtype)

    @pl.when(step == 0)
    def _():
        wg_ref[...] = jnp.zeros_like(wg_ref)
        gg_ref[...] = jnp.zeros_like(gg_ref)

    wg_ref[...] += wg
    gg_ref[...] += gg


def pair_backward(flat, ds, gain, wt):
    m, width = flat.shape
    tile = min(PAIR_BACK_TILE, m)
    pad = ds.shape[0]
    return pl.pallas_call(
        pair_backward_kernel,
        grid=(m // tile,),
        in_specs=[
            pl.BlockSpec((tile, width), lambda i: (i, 0)),
            pl.BlockSpec((pad, tile), lambda i: (0, i)),
            pl.BlockSpec((1, width), lambda i: (0, 0)),
            pl.BlockSpec(wt.shape, lambda i: (0, 0)),
        ],
        out_specs=[
            pl.BlockSpec((tile, width), lambda i: (i, 0)),
            pl.BlockSpec((pad, width), lambda i: (0, 0)),
            pl.BlockSpec((1, width), lambda i: (0, 0)),
        ],
        out_shape=[
            jax.ShapeDtypeStruct((m, width), jnp.bfloat16),
            jax.ShapeDtypeStruct((pad, width), jnp.float32),
            jax.ShapeDtypeStruct((1, width), jnp.float32),
        ],
        compiler_params=pltpu.CompilerParams(dimension_semantics=("arbitrary",)),
        cost_estimate=pl.CostEstimate(
            flops=m * width * (4 * HEAD_PAD + 20),
            transcendentals=m,
            bytes_accessed=2 * m * width * 2 + pad * m * 2,
        ),
    )(flat, ds, gain, wt)


def layer_norm(values):
    centred = values - jnp.mean(values, axis=-1, keepdims=True)
    inv_std = lax.rsqrt(jnp.mean(centred * centred, axis=-1, keepdims=True) + epsilon)
    return (centred * inv_std, inv_std)


def norm_back(normed, inv_std, grad):
    mean_grad = jnp.mean(grad, axis=-1, keepdims=True)
    mean_proj = jnp.mean(grad * normed, axis=-1, keepdims=True)
    return inv_std * (grad - mean_grad - normed * mean_proj)


def silu_slope(values):
    sigma = jax.nn.sigmoid(values)
    return sigma * (1.0 + values * (1.0 - sigma))


def head_split(values):
    return values.reshape(values.shape[:-1] + (values.shape[-1] // DH, DH))


def swap_heads(values):
    return lax.ppermute(values, "head", [(0, 1), (1, 0)])


def whole_rows(own, first):
    other = swap_heads(own)
    return jnp.where(
        first,
        jnp.concatenate([own, other], axis=0),
        jnp.concatenate([other, own], axis=0),
    )


def dp_gather(values):
    count = lax.axis_size("dp")
    index = lax.axis_index("dp")
    block = values
    step = 1
    while step < count:
        other = lax.ppermute(block, "dp", [(i, i ^ step) for i in range(count)])
        block = jnp.where(
            (index & step) == 0,
            jnp.concatenate([block, other], axis=0),
            jnp.concatenate([other, block], axis=0),
        )
        step *= 2
    return block


def dp_sum(values):
    count = lax.axis_size("dp")
    index = lax.axis_index("dp")
    step = 1
    while step < count:
        other = lax.ppermute(values, "dp", [(i, i ^ step) for i in range(count)])
        values = jnp.where((index & step) == 0, values + other, other + values)
        step *= 2
    return values


def own_rows(values, head, rows):
    return lax.dynamic_slice_in_dim(values, head * rows, rows, 1)


def head_sum(part):
    return part + swap_heads(part)


def head_sum_low(part):
    low = part.astype(jnp.bfloat16)
    return low.astype(jnp.float32) + swap_heads(low).astype(jnp.float32)


def trade_blocks(values, head, size, axis, mine_axis):
    mine = lax.dynamic_slice_in_dim(values, head * size, size, axis)
    theirs = swap_heads(lax.dynamic_slice_in_dim(values, (1 - head) * size, size, axis))
    return jnp.where(
        head == 0,
        jnp.concatenate([mine, theirs], axis=mine_axis),
        jnp.concatenate([theirs, mine], axis=mine_axis),
    )


def attn_scores(queries, keys, biases, valid):
    scores = jnp.einsum("cqhe,ckhe->chqk", queries, keys, preferred_element_type=jnp.float32)
    scores = scores * DH ** (-0.5) + biases.astype(jnp.float32)
    return jnp.where(valid[:, None, None, :], scores, masked_score)


def to_chunks(values, parts):
    return values.reshape(parts, -1, LANES)


def shards(
    layer_input,
    pair_input,
    time_cond,
    chain_lengths,
    residue_mask,
    mod_weight,
    mod_bias,
    qkv_weight,
    pair_gain,
    pair_weight,
    out_weight,
    out_bias,
    gate_up_weight,
    down_weight,
    output_grad,
):
    assert layer_input.shape[0] == 1
    rows = layer_input.shape[1]
    width = layer_input.shape[2]
    length = residue_mask.shape[1]
    head = lax.axis_index("head")
    first = head == 0
    data_count = lax.axis_size("dp")
    proj = qkv_weight.shape[2]
    ffn = gate_up_weight.shape[2]
    qkv_w = qkv_weight.reshape(width, 3 * proj)
    gate_up_w = gate_up_weight.reshape(width, 2 * ffn)

    x_rows = whole_rows(layer_input[0], first)
    g_rows = whole_rows(output_grad[0], first)
    out_weight_all = whole_rows(out_weight, first)

    positions = jnp.arange(length, dtype=jnp.int32)
    valid = (positions < chain_lengths[0]) & ((residue_mask[0] == 1) | (positions == 0))
    silu_cond = jax.nn.silu(time_cond).astype(jnp.bfloat16)
    modulation = jnp.dot(silu_cond, mod_weight, preferred_element_type=jnp.float32) + mod_bias
    scale_a, shift_a, gate_a, scale_t, shift_t, gate_t = [
        modulation[:, section * width : (section + 1) * width] for section in range(6)
    ]

    heads_all = pair_weight.shape[1]
    pair_width = pair_input.shape[-1]
    pair_flat = pair_input.reshape(-1, pair_width)
    pair_wt = jnp.pad(pair_weight.T, ((0, HEAD_PAD - heads_all), (0, 0)))
    pair_gain_row = pair_gain.reshape(1, pair_width)
    bias_flat = pair_forward(pair_flat, pair_gain_row, pair_weight, heads_all)
    bias_rows = bias_flat.reshape(heads_all, rows, length)
    heads_own = proj // DH
    biases = trade_blocks(bias_rows, head, heads_own, 0, 1)

    residues = x_rows.astype(jnp.float32)
    norm_in, inv_in = layer_norm(residues)
    normed_a = (norm_in * (1.0 + scale_a) + shift_a).astype(jnp.bfloat16)
    projected = jnp.dot(normed_a, qkv_w, preferred_element_type=jnp.float32).astype(jnp.bfloat16)
    queries = head_split(projected[:, :proj])
    keys = head_split(projected[:, proj : 2 * proj])
    values = head_split(projected[:, 2 * proj :])
    scores = jnp.einsum("qhe,khe->hqk", queries, keys, preferred_element_type=jnp.float32)
    scores = scores * DH ** (-0.5) + biases.astype(jnp.float32)
    scores = jnp.where(valid[None, None, :], scores, masked_score)
    row_max = jnp.max(scores, axis=-1, keepdims=True)
    exp_scores = jnp.exp(scores - row_max)
    row_total = jnp.sum(exp_scores, axis=-1, keepdims=True)
    attn_probs = exp_scores / row_total
    probs_low = attn_probs.astype(jnp.bfloat16)
    mixed = jnp.einsum("hqk,khe->qhe", probs_low, values, preferred_element_type=jnp.float32)
    mixed = mixed.reshape(length, proj).astype(jnp.bfloat16)
    mixed_all = jnp.where(
        first,
        jnp.concatenate([mixed, swap_heads(mixed)], axis=1),
        jnp.concatenate([swap_heads(mixed), mixed], axis=1),
    )
    attn_branch = jnp.dot(mixed_all, out_weight_all, preferred_element_type=jnp.float32) + out_bias
    sig_a = jax.nn.sigmoid(gate_a)
    middle = residues + sig_a * attn_branch

    norm_mid, inv_mid = layer_norm(middle)
    normed_t = (norm_mid * (1.0 + scale_t) + shift_t).astype(jnp.bfloat16)
    gate_up = jnp.dot(normed_t, gate_up_w, preferred_element_type=jnp.float32)
    gate_pre = gate_up[:, :ffn]
    up_pre = gate_up[:, ffn:]
    hidden = (jax.nn.silu(gate_pre) * up_pre).astype(jnp.bfloat16)
    ffn_part = jnp.dot(hidden, down_weight, preferred_element_type=jnp.float32).astype(jnp.bfloat16)
    ffn_branch = ffn_part.astype(jnp.float32) + swap_heads(ffn_part).astype(jnp.float32)
    sig_t = jax.nn.sigmoid(gate_t)
    layer_output = own_rows((middle + sig_t * ffn_branch).astype(jnp.bfloat16)[None], head, rows)

    grad_out = g_rows.astype(jnp.float32)
    d_ffn = (grad_out * sig_t).astype(jnp.bfloat16)
    d_gate_t = jnp.sum(grad_out * ffn_branch * sig_t * (1.0 - sig_t), axis=0, keepdims=True)
    down_grad_t = lax.dot_general(
        d_ffn, hidden, (((0,), (0,)), ((), ())), preferred_element_type=jnp.float32
    )
    d_hidden = lax.dot_general(
        d_ffn, down_weight, (((1,), (1,)), ((), ())), preferred_element_type=jnp.float32
    )
    d_gate = d_hidden * up_pre * silu_slope(gate_pre)
    d_up = d_hidden * jax.nn.silu(gate_pre)
    d_gate_up = jnp.concatenate([d_gate, d_up], axis=1).astype(jnp.bfloat16)
    gate_up_grad = lax.dot_general(
        normed_t, d_gate_up, (((0,), (0,)), ((), ())), preferred_element_type=jnp.float32
    )
    ffn_in_part = lax.dot_general(
        d_gate_up, gate_up_w, (((1,), (1,)), ((), ())), preferred_element_type=jnp.float32
    )
    d_normed_t = head_sum_low(ffn_in_part)
    d_middle = grad_out + norm_back(norm_mid, inv_mid, d_normed_t * (1.0 + scale_t))
    d_scale_t = jnp.sum(d_normed_t * norm_mid, axis=0, keepdims=True)
    d_shift_t = jnp.sum(d_normed_t, axis=0, keepdims=True)
    d_attn = d_middle * sig_a
    d_gate_a = jnp.sum(d_middle * attn_branch * sig_a * (1.0 - sig_a), axis=0, keepdims=True)
    d_out_bias = jnp.sum(d_attn, axis=0, keepdims=True)
    d_attn_low = d_attn.astype(jnp.bfloat16)

    out_weight_grad_t = lax.dot_general(
        d_attn_low, mixed, (((0,), (0,)), ((), ())), preferred_element_type=jnp.float32
    )
    d_mixed = head_split(
        lax.dot_general(
            d_attn_low, out_weight, (((1,), (1,)), ((), ())), preferred_element_type=jnp.float32
        ).astype(jnp.bfloat16)
    )
    d_values = jnp.einsum("hqk,qhe->khe", probs_low, d_mixed, preferred_element_type=jnp.float32)
    d_probs = jnp.einsum("qhe,khe->hqk", d_mixed, values, preferred_element_type=jnp.float32)
    d_scores = (
        attn_probs * (d_probs - jnp.sum(d_probs * attn_probs, axis=-1, keepdims=True))
    ).astype(jnp.bfloat16)
    d_queries = jnp.einsum(
        "hqk,khe->qhe", d_scores, keys, preferred_element_type=jnp.float32
    ) * DH ** (-0.5)
    d_keys = jnp.einsum(
        "hqk,qhe->khe", d_scores, queries, preferred_element_type=jnp.float32
    ) * DH ** (-0.5)
    d_qkv = jnp.concatenate(
        [d_queries.reshape(length, proj), d_keys.reshape(length, proj), d_values.reshape(length, proj)],
        axis=1,
    ).astype(jnp.bfloat16)
    qkv_grad = lax.dot_general(
        normed_a, d_qkv, (((0,), (0,)), ((), ())), preferred_element_type=jnp.float32
    )

    packed = blank((width, 4 * proj + 3 * ffn), jnp.bfloat16)
    packed = lax.dynamic_update_slice(packed, gate_up_grad.astype(jnp.bfloat16), (0, 4 * proj))
    packed = lax.dynamic_update_slice(
        packed, down_grad_t.astype(jnp.bfloat16), (0, 4 * proj + 2 * ffn)
    )
    packed = lax.dynamic_update_slice(packed, out_weight_grad_t.astype(jnp.bfloat16), (0, 3 * proj))
    packed = lax.dynamic_update_slice(packed, qkv_grad.astype(jnp.bfloat16), (0, 0))
    reduced = lax.psum_scatter(packed, "dp", scatter_dimension=0, tiled=True).astype(jnp.float32)

    attn_in_part = lax.dot_general(
        d_qkv, qkv_w, (((1,), (1,)), ((), ())), preferred_element_type=jnp.float32
    ).astype(jnp.bfloat16)
    d_normed_a = attn_in_part.astype(jnp.float32) + swap_heads(attn_in_part).astype(jnp.float32)
    input_grad = own_rows(
        (d_middle + norm_back(norm_in, inv_in, d_normed_a * (1.0 + scale_a)))[None], head, rows
    )
    d_scale_a = jnp.sum(d_normed_a * norm_in, axis=0, keepdims=True)
    d_shift_a = jnp.sum(d_normed_a, axis=0, keepdims=True)
    d_modulation = jnp.concatenate(
        [d_scale_a, d_shift_a, d_gate_a, d_scale_t, d_shift_t, d_gate_t], axis=-1
    )

    d_bias_rows = trade_blocks(d_scores, head, rows, 1, 0)
    d_bias_flat = jnp.pad(d_bias_rows.reshape(heads_all, -1), ((0, HEAD_PAD - heads_all), (0, 0)))
    pair_grad, pair_wg, pair_gg = pair_backward(pair_flat, d_bias_flat, pair_gain_row, pair_wt)
    pair_grad = pair_grad.reshape(pair_input.shape)
    pair_weight_grad = pair_wg[:heads_all].T
    pair_gain_grad = pair_gg[0]

    pair_small = head_sum(
        jnp.concatenate([pair_weight_grad.reshape(-1), pair_gain_grad])[None]
    )
    small = jnp.concatenate([d_modulation, time_cond, d_out_bias], axis=-1)
    small_rows = dp_gather(small)
    mod_size = d_modulation.shape[-1]
    cond_size = time_cond.shape[-1]
    pw_size = pair_weight.size
    mod_chain = small_rows[:, :mod_size]
    cond_chain = small_rows[:, mod_size : mod_size + cond_size]
    out_bias_grad = jnp.sum(small_rows[:, mod_size + cond_size :], axis=0)
    pair_total = dp_sum(pair_small)[0]
    pair_weight_grad = pair_total[:pw_size].reshape(pair_weight.shape)
    pair_gain_grad = pair_total[pw_size:]
    cond_act = lax.optimization_barrier(jax.nn.silu(cond_chain).astype(jnp.bfloat16)).astype(
        jnp.float32
    )
    mod_weight_grad = jnp.dot(cond_act.T, mod_chain, precision=precise)
    mod_bias_grad = jnp.sum(mod_chain, axis=0)
    cond_grad = jnp.dot(
        d_modulation, mod_weight.astype(jnp.float32).T, precision=precise
    ) * silu_slope(time_cond)

    cuts = [0, 3 * proj, 4 * proj, 4 * proj + 2 * ffn, 4 * proj + 3 * ffn]
    pieces = [reduced[:, cuts[i] : cuts[i + 1]] for i in range(4)]
    qkv_grad = pieces[0].reshape(-1, 3, proj)
    out_weight_grad = pieces[1].T
    gate_up_grad = pieces[2].reshape(-1, 2, ffn)
    down_grad = pieces[3].T
    return (
        layer_output,
        input_grad,
        pair_grad,
        cond_grad,
        mod_weight_grad,
        mod_bias_grad,
        qkv_grad,
        pair_gain_grad,
        pair_weight_grad,
        out_weight_grad,
        out_bias_grad,
        gate_up_grad,
        down_grad,
    )


def solution(mesh):
    placed = (
        P("dp", "head", None),
        P("dp", "head", None, None),
        P("dp", None),
        P("dp"),
        P("dp", None),
        P(),
        P(),
        P(None, None, "head"),
        P(),
        P(),
        P("head", None),
        P(),
        P(None, None, "head"),
        P("head", None),
        P("dp", "head", None),
    )
    return jax.shard_map(
        shards,
        mesh=mesh,
        in_specs=placed,
        out_specs=(
            P("dp", "head", None),
            P("dp", "head", None),
            P("dp", "head", None, None),
            P("dp", None),
            P(),
            P(),
            P("dp", None, "head"),
            P(),
            P(),
            P("head", "dp"),
            P(),
            P("dp", None, "head"),
            P("head", "dp"),
        ),
        check_vma=False,
    )
```

```python
import jax
import jax.numpy as jnp
from jax import lax
from jax.experimental import pallas as pl
from jax.experimental.pallas import tpu as pltpu
from jax.sharding import PartitionSpec as P

DH = 64


epsilon = 1e-05
masked_score = -1000000000.0
precise = lax.Precision.HIGHEST
LANES = 128
PAIR_TILE = 4096
PAIR_BACK_TILE = 2048
HEAD_PAD = 16


def blank_kernel(out_ref):
    del out_ref


def blank(shape, dtype):
    return pl.pallas_call(
        blank_kernel,
        out_shape=jax.ShapeDtypeStruct(shape, dtype),
        out_specs=pl.BlockSpec(memory_space=pl.ANY),
    )()


def pair_stats(x):
    centred = x - jnp.mean(x, axis=-1, keepdims=True)
    inv_std = lax.rsqrt(jnp.mean(centred * centred, axis=-1, keepdims=True) + epsilon)
    return centred * inv_std, inv_std


def pair_forward_kernel(x_ref, gain_ref, wt_ref, bias_ref):
    normed, _ = pair_stats(x_ref[...].astype(jnp.float32))
    scaled = (normed * gain_ref[...]).astype(jnp.bfloat16)
    bias = lax.dot_general(
        wt_ref[...], scaled, (((0,), (1,)), ((), ())), preferred_element_type=jnp.float32
    )
    bias_ref[...] = bias.astype(bias_ref.dtype)


def pair_forward(flat, gain, wt, heads):
    m, width = flat.shape
    tile = min(PAIR_TILE, m)
    return pl.pallas_call(
        pair_forward_kernel,
        grid=(m // tile,),
        in_specs=[
            pl.BlockSpec((tile, width), lambda i: (i, 0)),
            pl.BlockSpec((1, width), lambda i: (0, 0)),
            pl.BlockSpec(wt.shape, lambda i: (0, 0)),
        ],
        out_specs=pl.BlockSpec((heads, tile), lambda i: (0, i)),
        out_shape=jax.ShapeDtypeStruct((heads, m), jnp.bfloat16),
        cost_estimate=pl.CostEstimate(
            flops=m * width * (2 * HEAD_PAD + 10),
            transcendentals=m,
            bytes_accessed=m * width * 2 + heads * m * 2,
        ),
    )(flat, gain, wt)


def pair_backward_kernel(x_ref, ds_ref, gain_ref, wt_ref, grad_ref, wg_ref, gg_ref):
    step = pl.program_id(0)
    normed, inv_std = pair_stats(x_ref[...].astype(jnp.float32))
    gain = gain_ref[...]
    scaled = (normed * gain).astype(jnp.bfloat16)
    ds = ds_ref[...]
    d_scaled = lax.dot_general(
        ds, wt_ref[...], (((0,), (0,)), ((), ())), preferred_element_type=jnp.float32
    )
    wg = lax.dot_general(ds, scaled, (((1,), (0,)), ((), ())), preferred_element_type=jnp.float32)
    gg = jnp.sum(d_scaled * normed, axis=0, keepdims=True)
    d_normed = d_scaled * gain
    mean_grad = jnp.mean(d_normed, axis=-1, keepdims=True)
    mean_proj = jnp.mean(d_normed * normed, axis=-1, keepdims=True)
    grad_ref[...] = (inv_std * (d_normed - mean_grad - normed * mean_proj)).astype(grad_ref.dtype)

    @pl.when(step == 0)
    def _():
        wg_ref[...] = jnp.zeros_like(wg_ref)
        gg_ref[...] = jnp.zeros_like(gg_ref)

    wg_ref[...] += wg
    gg_ref[...] += gg


def pair_backward(flat, ds, gain, wt):
    m, width = flat.shape
    tile = min(PAIR_BACK_TILE, m)
    pad = ds.shape[0]
    return pl.pallas_call(
        pair_backward_kernel,
        grid=(m // tile,),
        in_specs=[
            pl.BlockSpec((tile, width), lambda i: (i, 0)),
            pl.BlockSpec((pad, tile), lambda i: (0, i)),
            pl.BlockSpec((1, width), lambda i: (0, 0)),
            pl.BlockSpec(wt.shape, lambda i: (0, 0)),
        ],
        out_specs=[
            pl.BlockSpec((tile, width), lambda i: (i, 0)),
            pl.BlockSpec((pad, width), lambda i: (0, 0)),
            pl.BlockSpec((1, width), lambda i: (0, 0)),
        ],
        out_shape=[
            jax.ShapeDtypeStruct((m, width), jnp.bfloat16),
            jax.ShapeDtypeStruct((pad, width), jnp.float32),
            jax.ShapeDtypeStruct((1, width), jnp.float32),
        ],
        compiler_params=pltpu.CompilerParams(dimension_semantics=("arbitrary",)),
        cost_estimate=pl.CostEstimate(
            flops=m * width * (4 * HEAD_PAD + 20),
            transcendentals=m,
            bytes_accessed=2 * m * width * 2 + pad * m * 2,
        ),
    )(flat, ds, gain, wt)


def layer_norm(values):
    centred = values - jnp.mean(values, axis=-1, keepdims=True)
    inv_std = lax.rsqrt(jnp.mean(centred * centred, axis=-1, keepdims=True) + epsilon)
    return (centred * inv_std, inv_std)


def norm_back(normed, inv_std, grad):
    mean_grad = jnp.mean(grad, axis=-1, keepdims=True)
    mean_proj = jnp.mean(grad * normed, axis=-1, keepdims=True)
    return inv_std * (grad - mean_grad - normed * mean_proj)


def silu_slope(values):
    sigma = jax.nn.sigmoid(values)
    return sigma * (1.0 + values * (1.0 - sigma))


def head_split(values):
    return values.reshape(values.shape[:-1] + (values.shape[-1] // DH, DH))


def swap_heads(values):
    return lax.ppermute(values, "head", [(0, 1), (1, 0)])


def whole_rows(own, first):
    other = swap_heads(own)
    return jnp.where(
        first,
        jnp.concatenate([own, other], axis=0),
        jnp.concatenate([other, own], axis=0),
    )


def bit_reverse(value, bits):
    out = 0
    for bit in range(bits):
        out |= ((value >> bit) & 1) << (bits - 1 - bit)
    return out


def dp_gather(values):
    count = lax.axis_size("dp")
    index = lax.axis_index("dp")
    bits = count.bit_length() - 1
    block = values
    step = count // 2
    while step >= 1:
        other = lax.ppermute(block, "dp", [(i, i ^ step) for i in range(count)])
        block = jnp.where(
            (index & step) == 0,
            jnp.concatenate([block, other], axis=0),
            jnp.concatenate([other, block], axis=0),
        )
        step //= 2
    return block[jnp.array([bit_reverse(i, bits) for i in range(count)])]


def dp_sum(values):
    count = lax.axis_size("dp")
    index = lax.axis_index("dp")
    step = 1
    while step < count:
        other = lax.ppermute(values, "dp", [(i, i ^ step) for i in range(count)])
        values = jnp.where((index & step) == 0, values + other, other + values)
        step *= 2
    return values


def own_rows(values, head, rows):
    return lax.dynamic_slice_in_dim(values, head * rows, rows, 1)


def head_sum(part):
    return part + swap_heads(part)


def head_sum_low(part):
    low = part.astype(jnp.bfloat16)
    return low.astype(jnp.float32) + swap_heads(low).astype(jnp.float32)


def trade_blocks(values, head, size, axis, mine_axis):
    mine = lax.dynamic_slice_in_dim(values, head * size, size, axis)
    theirs = swap_heads(lax.dynamic_slice_in_dim(values, (1 - head) * size, size, axis))
    return jnp.where(
        head == 0,
        jnp.concatenate([mine, theirs], axis=mine_axis),
        jnp.concatenate([theirs, mine], axis=mine_axis),
    )


def attn_scores(queries, keys, biases, valid):
    scores = jnp.einsum("cqhe,ckhe->chqk", queries, keys, preferred_element_type=jnp.float32)
    scores = scores * DH ** (-0.5) + biases.astype(jnp.float32)
    return jnp.where(valid[:, None, None, :], scores, masked_score)


def to_chunks(values, parts):
    return values.reshape(parts, -1, LANES)


def shards(
    layer_input,
    pair_input,
    time_cond,
    chain_lengths,
    residue_mask,
    mod_weight,
    mod_bias,
    qkv_weight,
    pair_gain,
    pair_weight,
    out_weight,
    out_bias,
    gate_up_weight,
    down_weight,
    output_grad,
):
    assert layer_input.shape[0] == 1
    rows = layer_input.shape[1]
    width = layer_input.shape[2]
    length = residue_mask.shape[1]
    head = lax.axis_index("head")
    first = head == 0
    data_count = lax.axis_size("dp")
    proj = qkv_weight.shape[2]
    ffn = gate_up_weight.shape[2]
    qkv_w = qkv_weight.reshape(width, 3 * proj)
    gate_up_w = gate_up_weight.reshape(width, 2 * ffn)

    x_rows = whole_rows(layer_input[0], first)
    g_rows = whole_rows(output_grad[0], first)
    out_weight_all = whole_rows(out_weight, first)

    positions = jnp.arange(length, dtype=jnp.int32)
    valid = (positions < chain_lengths[0]) & ((residue_mask[0] == 1) | (positions == 0))
    silu_cond = jax.nn.silu(time_cond).astype(jnp.bfloat16)
    modulation = jnp.dot(silu_cond, mod_weight, preferred_element_type=jnp.float32) + mod_bias
    scale_a, shift_a, gate_a, scale_t, shift_t, gate_t = [
        modulation[:, section * width : (section + 1) * width] for section in range(6)
    ]

    heads_all = pair_weight.shape[1]
    pair_width = pair_input.shape[-1]
    pair_flat = pair_input.reshape(-1, pair_width)
    pair_wt = jnp.pad(pair_weight.T, ((0, HEAD_PAD - heads_all), (0, 0)))
    pair_gain_row = pair_gain.reshape(1, pair_width)
    bias_flat = pair_forward(pair_flat, pair_gain_row, pair_weight, heads_all)
    bias_rows = bias_flat.reshape(heads_all, rows, length)
    heads_own = proj // DH
    biases = trade_blocks(bias_rows, head, heads_own, 0, 1)

    residues = x_rows.astype(jnp.float32)
    norm_in, inv_in = layer_norm(residues)
    normed_a = (norm_in * (1.0 + scale_a) + shift_a).astype(jnp.bfloat16)
    projected = jnp.dot(normed_a, qkv_w, preferred_element_type=jnp.float32).astype(jnp.bfloat16)
    queries = head_split(projected[:, :proj])
    keys = head_split(projected[:, proj : 2 * proj])
    values = head_split(projected[:, 2 * proj :])
    scores = jnp.einsum("qhe,khe->hqk", queries, keys, preferred_element_type=jnp.float32)
    scores = scores * DH ** (-0.5) + biases.astype(jnp.float32)
    scores = jnp.where(valid[None, None, :], scores, masked_score)
    row_max = jnp.max(scores, axis=-1, keepdims=True)
    exp_scores = jnp.exp(scores - row_max)
    row_total = jnp.sum(exp_scores, axis=-1, keepdims=True)
    attn_probs = exp_scores / row_total
    probs_low = attn_probs.astype(jnp.bfloat16)
    mixed = jnp.einsum("hqk,khe->qhe", probs_low, values, preferred_element_type=jnp.float32)
    mixed = mixed.reshape(length, proj).astype(jnp.bfloat16)
    mixed_all = jnp.where(
        first,
        jnp.concatenate([mixed, swap_heads(mixed)], axis=1),
        jnp.concatenate([swap_heads(mixed), mixed], axis=1),
    )
    attn_branch = jnp.dot(mixed_all, out_weight_all, preferred_element_type=jnp.float32) + out_bias
    sig_a = jax.nn.sigmoid(gate_a)
    middle = residues + sig_a * attn_branch

    norm_mid, inv_mid = layer_norm(middle)
    normed_t = (norm_mid * (1.0 + scale_t) + shift_t).astype(jnp.bfloat16)
    gate_up = jnp.dot(normed_t, gate_up_w, preferred_element_type=jnp.float32)
    gate_pre = gate_up[:, :ffn]
    up_pre = gate_up[:, ffn:]
    hidden = (jax.nn.silu(gate_pre) * up_pre).astype(jnp.bfloat16)
    ffn_part = jnp.dot(hidden, down_weight, preferred_element_type=jnp.float32).astype(jnp.bfloat16)
    ffn_branch = ffn_part.astype(jnp.float32) + swap_heads(ffn_part).astype(jnp.float32)
    sig_t = jax.nn.sigmoid(gate_t)
    layer_output = own_rows((middle + sig_t * ffn_branch).astype(jnp.bfloat16)[None], head, rows)

    grad_out = g_rows.astype(jnp.float32)
    d_ffn = (grad_out * sig_t).astype(jnp.bfloat16)
    d_gate_t = jnp.sum(grad_out * ffn_branch * sig_t * (1.0 - sig_t), axis=0, keepdims=True)
    down_grad_t = lax.dot_general(
        d_ffn, hidden, (((0,), (0,)), ((), ())), preferred_element_type=jnp.float32
    )
    d_hidden = lax.dot_general(
        d_ffn, down_weight, (((1,), (1,)), ((), ())), preferred_element_type=jnp.float32
    )
    d_gate = d_hidden * up_pre * silu_slope(gate_pre)
    d_up = d_hidden * jax.nn.silu(gate_pre)
    d_gate_up = jnp.concatenate([d_gate, d_up], axis=1).astype(jnp.bfloat16)
    gate_up_grad = lax.dot_general(
        normed_t, d_gate_up, (((0,), (0,)), ((), ())), preferred_element_type=jnp.float32
    )
    ffn_in_part = lax.dot_general(
        d_gate_up, gate_up_w, (((1,), (1,)), ((), ())), preferred_element_type=jnp.float32
    )
    d_normed_t = head_sum_low(ffn_in_part)
    d_middle = grad_out + norm_back(norm_mid, inv_mid, d_normed_t * (1.0 + scale_t))
    d_scale_t = jnp.sum(d_normed_t * norm_mid, axis=0, keepdims=True)
    d_shift_t = jnp.sum(d_normed_t, axis=0, keepdims=True)
    d_attn = d_middle * sig_a
    d_gate_a = jnp.sum(d_middle * attn_branch * sig_a * (1.0 - sig_a), axis=0, keepdims=True)
    d_out_bias = jnp.sum(d_attn, axis=0, keepdims=True)
    d_attn_low = d_attn.astype(jnp.bfloat16)

    out_weight_grad_t = lax.dot_general(
        d_attn_low, mixed, (((0,), (0,)), ((), ())), preferred_element_type=jnp.float32
    )
    d_mixed = head_split(
        lax.dot_general(
            d_attn_low, out_weight, (((1,), (1,)), ((), ())), preferred_element_type=jnp.float32
        ).astype(jnp.bfloat16)
    )
    d_values = jnp.einsum("hqk,qhe->khe", probs_low, d_mixed, preferred_element_type=jnp.float32)
    d_probs = jnp.einsum("qhe,khe->hqk", d_mixed, values, preferred_element_type=jnp.float32)
    d_scores = (
        attn_probs * (d_probs - jnp.sum(d_probs * attn_probs, axis=-1, keepdims=True))
    ).astype(jnp.bfloat16)
    d_queries = jnp.einsum(
        "hqk,khe->qhe", d_scores, keys, preferred_element_type=jnp.float32
    ) * DH ** (-0.5)
    d_keys = jnp.einsum(
        "hqk,qhe->khe", d_scores, queries, preferred_element_type=jnp.float32
    ) * DH ** (-0.5)
    d_qkv = jnp.concatenate(
        [d_queries.reshape(length, proj), d_keys.reshape(length, proj), d_values.reshape(length, proj)],
        axis=1,
    ).astype(jnp.bfloat16)
    qkv_grad = lax.dot_general(
        normed_a, d_qkv, (((0,), (0,)), ((), ())), preferred_element_type=jnp.float32
    )

    packed = blank((width, 4 * proj + 3 * ffn), jnp.bfloat16)
    packed = lax.dynamic_update_slice(packed, gate_up_grad.astype(jnp.bfloat16), (0, 4 * proj))
    packed = lax.dynamic_update_slice(
        packed, down_grad_t.astype(jnp.bfloat16), (0, 4 * proj + 2 * ffn)
    )
    packed = lax.dynamic_update_slice(packed, out_weight_grad_t.astype(jnp.bfloat16), (0, 3 * proj))
    packed = lax.dynamic_update_slice(packed, qkv_grad.astype(jnp.bfloat16), (0, 0))
    reduced = lax.psum_scatter(packed, "dp", scatter_dimension=0, tiled=True).astype(jnp.float32)

    attn_in_part = lax.dot_general(
        d_qkv, qkv_w, (((1,), (1,)), ((), ())), preferred_element_type=jnp.float32
    ).astype(jnp.bfloat16)
    d_normed_a = attn_in_part.astype(jnp.float32) + swap_heads(attn_in_part).astype(jnp.float32)
    input_grad = own_rows(
        (d_middle + norm_back(norm_in, inv_in, d_normed_a * (1.0 + scale_a)))[None], head, rows
    )
    d_scale_a = jnp.sum(d_normed_a * norm_in, axis=0, keepdims=True)
    d_shift_a = jnp.sum(d_normed_a, axis=0, keepdims=True)
    d_modulation = jnp.concatenate(
        [d_scale_a, d_shift_a, d_gate_a, d_scale_t, d_shift_t, d_gate_t], axis=-1
    )

    d_bias_rows = trade_blocks(d_scores, head, rows, 1, 0)
    d_bias_flat = jnp.pad(d_bias_rows.reshape(heads_all, -1), ((0, HEAD_PAD - heads_all), (0, 0)))
    pair_grad, pair_wg, pair_gg = pair_backward(pair_flat, d_bias_flat, pair_gain_row, pair_wt)
    pair_grad = pair_grad.reshape(pair_input.shape)
    pair_weight_grad = pair_wg[:heads_all].T
    pair_gain_grad = pair_gg[0]

    pair_small = head_sum(
        jnp.concatenate([pair_weight_grad.reshape(-1), pair_gain_grad])[None]
    )
    small = jnp.concatenate([d_modulation, time_cond, d_out_bias], axis=-1)
    small_rows = dp_gather(small)
    mod_size = d_modulation.shape[-1]
    cond_size = time_cond.shape[-1]
    pw_size = pair_weight.size
    mod_chain = small_rows[:, :mod_size]
    cond_chain = small_rows[:, mod_size : mod_size + cond_size]
    out_bias_grad = jnp.sum(small_rows[:, mod_size + cond_size :], axis=0)
    pair_total = dp_sum(pair_small)[0]
    pair_weight_grad = pair_total[:pw_size].reshape(pair_weight.shape)
    pair_gain_grad = pair_total[pw_size:]
    cond_act = lax.optimization_barrier(jax.nn.silu(cond_chain).astype(jnp.bfloat16)).astype(
        jnp.float32
    )
    mod_weight_grad = jnp.dot(cond_act.T, mod_chain, precision=precise)
    mod_bias_grad = jnp.sum(mod_chain, axis=0)
    cond_grad = jnp.dot(
        d_modulation, mod_weight.astype(jnp.float32).T, precision=precise
    ) * silu_slope(time_cond)

    cuts = [0, 3 * proj, 4 * proj, 4 * proj + 2 * ffn, 4 * proj + 3 * ffn]
    pieces = [reduced[:, cuts[i] : cuts[i + 1]] for i in range(4)]
    qkv_grad = pieces[0].reshape(-1, 3, proj)
    out_weight_grad = pieces[1].T
    gate_up_grad = pieces[2].reshape(-1, 2, ffn)
    down_grad = pieces[3].T
    return (
        layer_output,
        input_grad,
        pair_grad,
        cond_grad,
        mod_weight_grad,
        mod_bias_grad,
        qkv_grad,
        pair_gain_grad,
        pair_weight_grad,
        out_weight_grad,
        out_bias_grad,
        gate_up_grad,
        down_grad,
    )


def solution(mesh):
    placed = (
        P("dp", "head", None),
        P("dp", "head", None, None),
        P("dp", None),
        P("dp"),
        P("dp", None),
        P(),
        P(),
        P(None, None, "head"),
        P(),
        P(),
        P("head", None),
        P(),
        P(None, None, "head"),
        P("head", None),
        P("dp", "head", None),
    )
    return jax.shard_map(
        shards,
        mesh=mesh,
        in_specs=placed,
        out_specs=(
            P("dp", "head", None),
            P("dp", "head", None),
            P("dp", "head", None, None),
            P("dp", None),
            P(),
            P(),
            P("dp", None, "head"),
            P(),
            P(),
            P("head", "dp"),
            P(),
            P("dp", None, "head"),
            P("head", "dp"),
        ),
        check_vma=False,
    )
```
